256 devices in a mesh: grp: 8 (over x, core), dev: 32 (over z, y).
Axes of the slice: x: 4, y: 4, z: 8, core: 2. Of those that a mesh axis runs over, the one named last changes fastest.
Arguments:
- references: bfloat16 [192, 2048], P('dev'), may hold values from -4 to 4
- particles: bfloat16 [2048, 65536], P(None, ('grp', 'dev')), may hold values from -1300 to 1300
- defocus_bin: int32 [65536], P(('grp', 'dev')), may hold values from 0 to 63
- contrast_table: float32 [64, 32], replicated, may hold values from 0.1 to 1
- noise_power: float32 [32], replicated, may hold values from 300 to 3000
- class_prior: float32 [192], replicated, may hold values from -3 to 3
Outputs:
- new_references: float32 [192, 2048], P('dev')
- occupancy: float32 [192], P('dev')
The draws below stay inside these ranges and needn't reach their ends.
All inputs are finite; a program needn't handle non-finite values.
Results may differ from the reference program's by a relative error of at most 0.0015.
Values may be sent and summed in bfloat16 or wider, within the bound.
No kernel may reach another device: no remote copies, remote signals or barrier semaphores. Data moves between devices by JAX's collectives and lax.ppermute only.
A program may use at most 64 MiB of HBM per device.

```python
import math
import jax
import jax.numpy as jnp
from jax import lax

Q = 32
M = 32
R = 128
NBIN = 64
K = 192
NPART = 65536


def reference_values(key):
    return jax.random.truncated_normal(jax.random.fold_in(key, 101), -4.0, 4.0, (K, 2 * M * Q), jnp.float32)


def draw_references(key, part):
    return reference_values(key).astype(jnp.bfloat16)


def draw_particles(key, part):
    array_shape = (2 * M * Q, NPART)
    values = 30.0 * jax.random.truncated_normal(jax.random.fold_in(key, 105), -6.0, 6.0, array_shape, jnp.float32)
    return values.astype(jnp.bfloat16)


def touch_ends(entries, stream_key, smallest, high):
    longest = entries.shape.index(max(entries.shape))
    spots = []
    for shift in (0, 1):
        where = [jax.random.randint(jax.random.fold_in(stream_key, axis), (), 0, length) for axis, length in enumerate(entries.shape)]
        where[longest] = (where[longest] + shift) % entries.shape[longest]
        spots.append(tuple(where))
    return entries.at[spots[0]].set(smallest).at[spots[1]].set(high)


def centred(own_key, shape, scale, most, held_as=jnp.bfloat16):
    return jnp.clip(scale * jax.random.normal(own_key, shape, jnp.float32), -most, most).astype(held_as)


def setup_inputs(seed: int = 0) -> dict:
    streams_of = jax.random.split(jax.random.key(seed), 7)
    return {
        "references": draw_references(jax.random.fold_in(streams_of[6], 71), 0),
        "particles": draw_particles(jax.random.fold_in(streams_of[6], 71), 0),
        "defocus_bin": touch_ends(jax.random.randint(streams_of[2], (NPART,), 0, NBIN), jax.random.fold_in(streams_of[2], 1), 0, NBIN - 1).astype(jnp.int32),
        "contrast_table": jnp.clip(jax.random.uniform(streams_of[3], (NBIN, Q), jnp.float32, 0.1, 1.0), 0.1, 1.0),
        "noise_power": jnp.clip(jnp.exp(jax.random.uniform(streams_of[4], (Q,), jnp.float32, math.log(300.0), math.log(3000.0))), 300.0, 3000.0),
        "class_prior": centred(streams_of[5], (K,), 1.0, 3.0, jnp.float32),
    }


def angle_tables(cycle_freqs, count_turns):
    freq_index = jnp.arange(cycle_freqs, dtype=jnp.int32)
    turn_index = jnp.arange(count_turns, dtype=jnp.int32)
    wrapped = (freq_index[:, None] * turn_index[None, :]) % count_turns
    phases = (2.0 * math.pi / count_turns) * wrapped.astype(jnp.float32)
    factor = jnp.where(freq_index == 0, 1.0, 2.0).astype(jnp.float32)[:, None]
    cosine = jnp.cos(phases)
    sine_part = jnp.sin(phases)
    score_table = jnp.stack([factor * cosine, factor * sine_part], 0).astype(jnp.bfloat16)
    turn_table = jnp.stack([cosine, sine_part], 0).astype(jnp.bfloat16)
    return score_table, turn_table


def particle_terms(particles, defocus_bin, contrast_table, noise_power):
    columns = particles.shape[1]
    cycle_count = contrast_table.shape[1]
    freq_count = particles.shape[0] // (2 * cycle_count)
    onehot = (defocus_bin[None, :] == jnp.arange(contrast_table.shape[0], dtype=jnp.int32)[:, None]).astype(jnp.float32)
    contrast = jnp.dot(contrast_table.T, onehot, precision=lax.Precision.HIGHEST)
    scaled = contrast / noise_power[:, None]
    power_term = contrast * scaled
    weighted = (particles.astype(jnp.float32).reshape(freq_count, 2, cycle_count, columns) * scaled[None, None]).astype(jnp.bfloat16)
    return weighted.reshape(freq_count, 2 * cycle_count, columns), power_term


def class_rows(class_block):
    classes = class_block.shape[0]
    class_grid = class_block.reshape(classes, M, 2, Q)
    real_part = class_grid[:, :, 0, :]
    imag_part = class_grid[:, :, 1, :]
    rows_real = jnp.concatenate([real_part, imag_part], -1)
    rows_imag = jnp.concatenate([-imag_part, real_part], -1)
    stacked = jnp.stack([rows_real, rows_imag], 0)
    factor = jnp.where(jnp.arange(M) == 0, 1.0, 2.0).astype(jnp.float32)
    squares = class_grid.astype(jnp.float32) ** 2
    cycle_power = jnp.sum(jnp.sum(squares, axis=2) * factor[None, :, None], axis=1)
    return stacked, cycle_power


def reference(references, particles, defocus_bin, contrast_table, noise_power, class_prior):
    score_table, turn_table = angle_tables(M, R)
    stacked, cycle_power = class_rows(references)
    width = math.gcd(NPART, 1024)

    def one_block(running, offset):
        part_cols = lax.dynamic_slice_in_dim(particles, offset * width, width, 1)
        part_bins = lax.dynamic_slice_in_dim(defocus_bin, offset * width, width, 0)
        weighted, power_term = particle_terms(part_cols, part_bins, contrast_table, noise_power)
        crossed = jnp.einsum('pkmc,mcb->pmkb', stacked.astype(jnp.float32), weighted.astype(jnp.float32)).astype(jnp.bfloat16)
        scores = jnp.einsum('pmkb,pmr->krb', crossed.astype(jnp.float32), score_table.astype(jnp.float32))
        penalty = jnp.dot(cycle_power, power_term, precision=lax.Precision.HIGHEST)
        scores = scores - 0.5 * penalty[:, None, :] + class_prior[:, None, None]
        block_max = jnp.max(scores, axis=(0, 1))
        log_norm = block_max + jnp.log(jnp.sum(jnp.exp(scores - block_max[None, None, :]), axis=(0, 1)))
        responsibility = jnp.exp(scores - log_norm[None, None, :]).astype(jnp.bfloat16)
        spectra = jnp.einsum('krb,pmr->pmkb', responsibility.astype(jnp.float32), turn_table.astype(jnp.float32)).astype(jnp.bfloat16)
        products = jnp.einsum('pmkb,mcb->kpmc', spectra.astype(jnp.float32), weighted.astype(jnp.float32))
        real_sum = products[:, 0, :, :Q] + products[:, 1, :, Q:]
        imag_sum = products[:, 0, :, Q:] - products[:, 1, :, :Q]
        numerator = jnp.stack([real_sum, imag_sum], 2).reshape(K, 2 * M * Q)
        class_weight = jnp.sum(responsibility.astype(jnp.float32), axis=1)
        cycle_sum = jnp.dot(class_weight, power_term.T, precision=lax.Precision.HIGHEST)
        class_mass = jnp.sum(class_weight, axis=1)
        return (running[0] + numerator, running[1] + cycle_sum, running[2] + class_mass), None

    initial = (jnp.zeros((K, 2 * M * Q), jnp.float32), jnp.zeros((K, Q), jnp.float32), jnp.zeros((K,), jnp.float32))
    totals, unused = lax.scan(one_block, initial, jnp.arange(NPART // width, dtype=jnp.int32))
    numerator, cycle_sum, class_mass = totals
    new_references = (numerator.reshape(K, M, 2, Q) / cycle_sum[:, None, None, :]).reshape(K, 2 * M * Q)
    occupancy = class_mass * (K / NPART)
    return new_references, occupancy
```

```python
import math

import jax
import jax.numpy as jnp
from jax import lax
from jax.sharding import PartitionSpec as P

Q = 32
M = 32
R = 128
CLS_DEV = 6


def angle_tables(cycle_freqs, count_turns):
    freq_index = jnp.arange(cycle_freqs, dtype=jnp.int32)
    turn_index = jnp.arange(count_turns, dtype=jnp.int32)
    wrapped = freq_index[:, None] * turn_index[None, :] % count_turns
    phases = 2.0 * math.pi / count_turns * wrapped.astype(jnp.float32)
    factor = jnp.where(freq_index == 0, 1.0, 2.0).astype(jnp.float32)[:, None]
    cosine = jnp.cos(phases)
    sine_part = jnp.sin(phases)
    score_table = jnp.stack([factor * cosine, factor * sine_part], 0).astype(jnp.bfloat16)
    turn_table = jnp.stack([cosine, sine_part], 0).astype(jnp.bfloat16)
    return (score_table, turn_table)


def particle_terms(particles, defocus_bin, contrast_table, noise_power):
    columns = particles.shape[1]
    cycle_count = contrast_table.shape[1]
    freq_count = particles.shape[0] // (2 * cycle_count)
    onehot = (
        defocus_bin[None, :] == jnp.arange(contrast_table.shape[0], dtype=jnp.int32)[:, None]
    ).astype(jnp.float32)
    contrast = jnp.dot(contrast_table.T, onehot, precision=lax.Precision.HIGHEST)
    scaled = contrast / noise_power[:, None]
    power_term = contrast * scaled
    weighted = (
        particles.astype(jnp.float32).reshape(freq_count, 2, cycle_count, columns)
        * scaled[None, None]
    ).astype(jnp.bfloat16)
    return (weighted.reshape(freq_count, 2 * cycle_count, columns), power_term)


def class_rows(class_block):
    classes = class_block.shape[0]
    class_grid = class_block.reshape(classes, M, 2, Q)
    real_part = class_grid[:, :, 0, :]
    imag_part = class_grid[:, :, 1, :]
    rows_real = jnp.concatenate([real_part, imag_part], -1)
    rows_imag = jnp.concatenate([-imag_part, real_part], -1)
    stacked = jnp.stack([rows_real, rows_imag], 0)
    factor = jnp.where(jnp.arange(M) == 0, 1.0, 2.0).astype(jnp.float32)
    squares = class_grid.astype(jnp.float32) ** 2
    cycle_power = jnp.sum(jnp.sum(squares, axis=2) * factor[None, :, None], axis=1)
    return (stacked, cycle_power)


def block_rows(total_rows):
    return CLS_DEV * math.gcd(total_rows // CLS_DEV, 4)


def local(references, particles, defocus_bin, contrast_table, noise_power, class_prior):
    weighted, power_term = particle_terms(particles, defocus_bin, contrast_table, noise_power)
    score_table, turn_table = angle_tables(M, R)
    columns = particles.shape[1]
    classes_total = CLS_DEV * lax.axis_size("dev")

    def block_scores(class_block, first_row):
        stacked, cycle_power = class_rows(class_block)
        prior_part = lax.dynamic_slice_in_dim(class_prior, first_row, class_block.shape[0], 0)
        crossed = jnp.einsum(
            "pkmc,mcb->pmkb", stacked, weighted, preferred_element_type=jnp.float32
        ).astype(jnp.bfloat16)
        scores = jnp.einsum(
            "pmkb,pmr->krb", crossed, score_table, preferred_element_type=jnp.float32
        )
        penalty = jnp.dot(cycle_power, power_term, precision=lax.Precision.HIGHEST)
        return scores - 0.5 * penalty[:, None, :] + prior_part[:, None, None]

    initial = (jnp.full((columns,), -1e30, jnp.float32), jnp.zeros((columns,), jnp.float32))
    empty_sums = (
        jnp.zeros((classes_total, 2 * M * Q), jnp.float32),
        jnp.zeros((classes_total, Q), jnp.float32),
        jnp.zeros((classes_total,), jnp.float32),
    )
    gathered = lax.all_gather(references, "dev", axis=0, tiled=True)
    height = block_rows(gathered.shape[0])
    block_count = gathered.shape[0] // height
    blocks = gathered.reshape(block_count, height, gathered.shape[1])

    def one_block(current, block_item):
        class_block, offset = block_item
        scores = block_scores(class_block, offset * height)
        block_max = jnp.max(scores, axis=(0, 1))
        new_max = jnp.maximum(current[0], block_max)
        block_total = jnp.sum(jnp.exp(scores - new_max[None, None, :]), axis=(0, 1))
        return ((new_max, current[1] * jnp.exp(current[0] - new_max) + block_total), None)

    result, unused = lax.scan(
        one_block, initial, (blocks, jnp.arange(block_count, dtype=jnp.int32))
    )
    log_norm = result[0] + jnp.log(result[1])
    add_height = block_rows(gathered.shape[0])
    block_count = gathered.shape[0] // add_height
    blocks = gathered.reshape(block_count, add_height, gathered.shape[1])

    def one_block(current, block_item):
        class_block, offset = block_item
        row_start = offset * add_height
        scores = block_scores(class_block, row_start)
        responsibility = jnp.exp(scores - log_norm[None, None, :]).astype(jnp.bfloat16)
        spectra = jnp.einsum(
            "krb,pmr->pmkb", responsibility, turn_table, preferred_element_type=jnp.float32
        ).astype(jnp.bfloat16)
        products = jnp.einsum(
            "pmkb,mcb->kpmc", spectra, weighted, preferred_element_type=jnp.float32
        )
        real_sum = products[:, 0, :, :Q] + products[:, 1, :, Q:]
        imag_sum = products[:, 0, :, Q:] - products[:, 1, :, :Q]
        numerator = jnp.stack([real_sum, imag_sum], 2).reshape(add_height, 2 * M * Q)
        class_weight = jnp.sum(responsibility.astype(jnp.float32), axis=1)
        cycle_sum = jnp.dot(class_weight, power_term.T, precision=lax.Precision.HIGHEST)
        class_mass = jnp.sum(class_weight, axis=1)
        updated = (
            lax.dynamic_update_slice_in_dim(current[0], numerator, row_start, 0),
            lax.dynamic_update_slice_in_dim(current[1], cycle_sum, row_start, 0),
            lax.dynamic_update_slice_in_dim(current[2], class_mass, row_start, 0),
        )
        return (updated, None)

    result, unused = lax.scan(
        one_block, empty_sums, (blocks, jnp.arange(block_count, dtype=jnp.int32))
    )
    numer_all, cycles_all, mass_all = result
    width = numer_all.shape[1]
    packed = jnp.concatenate(
        [numer_all, cycles_all, mass_all[:, None], jnp.zeros((classes_total, 95), jnp.float32)], 1
    )
    packed = packed.reshape(lax.axis_size("dev"), CLS_DEV, packed.shape[1])
    own = lax.psum_scatter(packed, "dev", scatter_dimension=0, tiled=False)
    own = lax.psum(own, "grp")
    numerator = own[:, :width]
    cycle_sum = own[:, width : width + Q]
    class_mass = own[:, width + Q]
    new_references = (numerator.reshape(CLS_DEV, M, 2, Q) / cycle_sum[:, None, None, :]).reshape(
        CLS_DEV, 2 * M * Q
    )
    particle_total = columns * lax.axis_size("grp") * lax.axis_size("dev")
    occupancy = class_mass * (classes_total / particle_total)
    return (new_references, occupancy)


def solution(mesh):
    return jax.shard_map(
        local,
        mesh=mesh,
        in_specs=(P("dev", None), P(None, ("grp", "dev")), P(("grp", "dev")), P(), P(), P()),
        out_specs=(P("dev", None), P("dev")),
        check_vma=False,
    )
```

```python
import math

import jax
import jax.numpy as jnp
from jax import lax
from jax.sharding import PartitionSpec as P

Q = 32
M = 32
R = 128
CLS_DEV = 6


def angle_tables(cycle_freqs, count_turns):
    freq_index = jnp.arange(cycle_freqs, dtype=jnp.int32)
    turn_index = jnp.arange(count_turns, dtype=jnp.int32)
    wrapped = freq_index[:, None] * turn_index[None, :] % count_turns
    phases = 2.0 * math.pi / count_turns * wrapped.astype(jnp.float32)
    factor = jnp.where(freq_index == 0, 1.0, 2.0).astype(jnp.float32)[:, None]
    cosine = jnp.cos(phases)
    sine_part = jnp.sin(phases)
    score_table = jnp.stack([factor * cosine, factor * sine_part], 0).astype(jnp.bfloat16)
    turn_table = jnp.stack([cosine, sine_part], 0).astype(jnp.bfloat16)
    return (score_table, turn_table)


def particle_terms(particles, defocus_bin, contrast_table, noise_power):
    columns = particles.shape[1]
    cycle_count = contrast_table.shape[1]
    freq_count = particles.shape[0] // (2 * cycle_count)
    onehot = (
        defocus_bin[None, :] == jnp.arange(contrast_table.shape[0], dtype=jnp.int32)[:, None]
    ).astype(jnp.float32)
    contrast = jnp.dot(contrast_table.T, onehot, precision=lax.Precision.HIGHEST)
    scaled = contrast / noise_power[:, None]
    power_term = contrast * scaled
    weighted = (
        particles.astype(jnp.float32).reshape(freq_count, 2, cycle_count, columns)
        * scaled[None, None]
    ).astype(jnp.bfloat16)
    return (weighted.reshape(freq_count, 2 * cycle_count, columns), power_term)


def class_rows(class_block):
    classes = class_block.shape[0]
    class_grid = class_block.reshape(classes, M, 2, Q)
    real_part = class_grid[:, :, 0, :]
    imag_part = class_grid[:, :, 1, :]
    rows_real = jnp.concatenate([real_part, imag_part], -1)
    rows_imag = jnp.concatenate([-imag_part, real_part], -1)
    stacked = jnp.stack([rows_real, rows_imag], 0)
    factor = jnp.where(jnp.arange(M) == 0, 1.0, 2.0).astype(jnp.float32)
    squares = class_grid.astype(jnp.float32) ** 2
    cycle_power = jnp.sum(jnp.sum(squares, axis=2) * factor[None, :, None], axis=1)
    return (stacked, cycle_power)


def block_rows(total_rows):
    return CLS_DEV * math.gcd(total_rows // CLS_DEV, 4)


def local(references, particles, defocus_bin, contrast_table, noise_power, class_prior):
    weighted, power_term = particle_terms(particles, defocus_bin, contrast_table, noise_power)
    score_table, turn_table = angle_tables(M, R)
    columns = particles.shape[1]
    classes_total = CLS_DEV * lax.axis_size("dev")

    def block_scores(class_block, first_row):
        stacked, cycle_power = class_rows(class_block)
        prior_part = lax.dynamic_slice_in_dim(class_prior, first_row, class_block.shape[0], 0)
        crossed = jnp.einsum(
            "pkmc,mcb->pmkb", stacked, weighted, preferred_element_type=jnp.float32
        ).astype(jnp.bfloat16)
        scores = jnp.einsum(
            "pmkb,pmr->krb", crossed, score_table, preferred_element_type=jnp.float32
        )
        penalty = jnp.dot(cycle_power, power_term, precision=lax.Precision.HIGHEST)
        return scores - 0.5 * penalty[:, None, :] + prior_part[:, None, None]

    initial = (jnp.full((columns,), -1e30, jnp.float32), jnp.zeros((columns,), jnp.float32))
    empty_sums = (
        jnp.zeros((classes_total, 2 * M * Q), jnp.float32),
        jnp.zeros((classes_total, Q), jnp.float32),
        jnp.zeros((classes_total,), jnp.float32),
    )
    dev_count = lax.axis_size("dev")
    copies = jnp.broadcast_to(references[None], (dev_count,) + references.shape)
    gathered = lax.all_to_all(copies, "dev", 0, 0, tiled=True).reshape(
        dev_count * references.shape[0], references.shape[1]
    )
    height = block_rows(gathered.shape[0])
    block_count = gathered.shape[0] // height
    blocks = gathered.reshape(block_count, height, gathered.shape[1])

    def one_block(current, block_item):
        class_block, offset = block_item
        scores = block_scores(class_block, offset * height)
        block_max = jnp.max(scores, axis=(0, 1))
        new_max = jnp.maximum(current[0], block_max)
        block_total = jnp.sum(jnp.exp(scores - new_max[None, None, :]), axis=(0, 1))
        return ((new_max, current[1] * jnp.exp(current[0] - new_max) + block_total), None)

    result, unused = lax.scan(
        one_block, initial, (blocks, jnp.arange(block_count, dtype=jnp.int32))
    )
    log_norm = result[0] + jnp.log(result[1])
    add_height = block_rows(gathered.shape[0])
    block_count = gathered.shape[0] // add_height
    blocks = gathered.reshape(block_count, add_height, gathered.shape[1])

    def one_block(current, block_item):
        class_block, offset = block_item
        row_start = offset * add_height
        scores = block_scores(class_block, row_start)
        responsibility = jnp.exp(scores - log_norm[None, None, :]).astype(jnp.bfloat16)
        spectra = jnp.einsum(
            "krb,pmr->pmkb", responsibility, turn_table, preferred_element_type=jnp.float32
        ).astype(jnp.bfloat16)
        products = jnp.einsum(
            "pmkb,mcb->kpmc", spectra, weighted, preferred_element_type=jnp.float32
        )
        real_sum = products[:, 0, :, :Q] + products[:, 1, :, Q:]
        imag_sum = products[:, 0, :, Q:] - products[:, 1, :, :Q]
        numerator = jnp.stack([real_sum, imag_sum], 2).reshape(add_height, 2 * M * Q)
        class_weight = jnp.sum(responsibility.astype(jnp.float32), axis=1)
        cycle_sum = jnp.dot(class_weight, power_term.T, precision=lax.Precision.HIGHEST)
        class_mass = jnp.sum(class_weight, axis=1)
        updated = (
            lax.dynamic_update_slice_in_dim(current[0], numerator, row_start, 0),
            lax.dynamic_update_slice_in_dim(current[1], cycle_sum, row_start, 0),
            lax.dynamic_update_slice_in_dim(current[2], class_mass, row_start, 0),
        )
        return (updated, None)

    result, unused = lax.scan(
        one_block, empty_sums, (blocks, jnp.arange(block_count, dtype=jnp.int32))
    )
    numer_all, cycles_all, mass_all = result
    width = numer_all.shape[1]
    packed = jnp.concatenate(
        [numer_all, cycles_all, mass_all[:, None], jnp.zeros((classes_total, 95), jnp.float32)], 1
    )
    packed = packed.reshape(dev_count, CLS_DEV, packed.shape[1])
    own = jnp.sum(lax.all_to_all(packed, "dev", 0, 0, tiled=True), 0)
    own = jnp.sum(lax.all_gather(own, "grp", axis=0, tiled=False), 0)
    numerator = own[:, :width]
    cycle_sum = own[:, width : width + Q]
    class_mass = own[:, width + Q]
    new_references = (numerator.reshape(CLS_DEV, M, 2, Q) / cycle_sum[:, None, None, :]).reshape(
        CLS_DEV, 2 * M * Q
    )
    particle_total = columns * lax.axis_size("grp") * lax.axis_size("dev")
    occupancy = class_mass * (classes_total / particle_total)
    return (new_references, occupancy)


def solution(mesh):
    return jax.shard_map(
        local,
        mesh=mesh,
        in_specs=(P("dev", None), P(None, ("grp", "dev")), P(("grp", "dev")), P(), P(), P()),
        out_specs=(P("dev", None), P("dev")),
        check_vma=False,
    )
```

```python
import functools
import math

import jax
import jax.numpy as jnp
from jax import lax
from jax.experimental import pallas as pl
from jax.experimental.pallas import tpu as pltpu
from jax.sharding import PartitionSpec as P

Q = 32
M = 32
R = 128
CLS_DEV = 6
CLS_STEP = 8


def angle_tables(cycle_freqs, count_turns):
    freq_index = jnp.arange(cycle_freqs, dtype=jnp.int32)
    turn_index = jnp.arange(count_turns, dtype=jnp.int32)
    wrapped = freq_index[:, None] * turn_index[None, :] % count_turns
    phases = 2.0 * math.pi / count_turns * wrapped.astype(jnp.float32)
    factor = jnp.where(freq_index == 0, 1.0, 2.0).astype(jnp.float32)[:, None]
    cosine = jnp.cos(phases)
    sine_part = jnp.sin(phases)
    score_table = jnp.stack([factor * cosine, factor * sine_part], 0).astype(jnp.bfloat16)
    turn_table = jnp.stack([cosine, sine_part], 0).astype(jnp.bfloat16)
    return (score_table, turn_table)


def particle_terms(particles, defocus_bin, contrast_table, noise_power):
    columns = particles.shape[1]
    cycle_count = contrast_table.shape[1]
    freq_count = particles.shape[0] // (2 * cycle_count)
    onehot = (
        defocus_bin[None, :] == jnp.arange(contrast_table.shape[0], dtype=jnp.int32)[:, None]
    ).astype(jnp.float32)
    contrast = jnp.dot(contrast_table.T, onehot, precision=lax.Precision.HIGHEST)
    scaled = contrast / noise_power[:, None]
    power_term = contrast * scaled
    weighted = (
        particles.astype(jnp.float32).reshape(freq_count, 2, cycle_count, columns)
        * scaled[None, None]
    ).astype(jnp.bfloat16)
    return (weighted.reshape(freq_count, 2 * cycle_count, columns), power_term)


def class_rows(class_block):
    classes = class_block.shape[0]
    class_grid = class_block.reshape(classes, M, 2, Q)
    real_part = class_grid[:, :, 0, :]
    imag_part = class_grid[:, :, 1, :]
    rows_real = jnp.concatenate([real_part, imag_part], -1)
    rows_imag = jnp.concatenate([-imag_part, real_part], -1)
    stacked = jnp.stack([rows_real, rows_imag], 0)
    factor = jnp.where(jnp.arange(M) == 0, 1.0, 2.0).astype(jnp.float32)
    squares = class_grid.astype(jnp.float32) ** 2
    cycle_power = jnp.sum(jnp.sum(squares, axis=2) * factor[None, :, None], axis=1)
    return (stacked, cycle_power)


def block_scores(table_ref, crossed_ref, half_ref, prior_ref):
    raw = jnp.dot(table_ref[...], crossed_ref[...], preferred_element_type=jnp.float32)
    return raw - half_ref[...] + prior_ref[...]


def norm_kernel(cols, table_ref, crossed_ref, half_ref, prior_ref, out_ref, top_ref, total_ref):
    step = pl.program_id(0)

    @pl.when(step == 0)
    def _():
        top_ref[...] = jnp.full(top_ref.shape, -1e30, jnp.float32)
        total_ref[...] = jnp.zeros(total_ref.shape, jnp.float32)

    scores = block_scores(table_ref, crossed_ref, half_ref, prior_ref)
    parts = [scores[:, j * cols : (j + 1) * cols] for j in range(scores.shape[1] // cols)]
    block_top = functools.reduce(jnp.maximum, [jnp.max(s, axis=0, keepdims=True) for s in parts])
    old_top = top_ref[...]
    new_top = jnp.maximum(old_top, block_top)
    block_total = functools.reduce(
        jnp.add, [jnp.sum(jnp.exp(s - new_top), axis=0, keepdims=True) for s in parts]
    )
    total_ref[...] = total_ref[...] * jnp.exp(old_top - new_top) + block_total
    top_ref[...] = new_top

    @pl.when(step == pl.num_programs(0) - 1)
    def _():
        out_ref[...] = top_ref[...] + jnp.log(total_ref[...])


def spectra_kernel(
    table_ref, crossed_ref, half_ref, prior_ref, norm_ref, turn_ref, spectra_ref, weight_ref
):
    scores = block_scores(table_ref, crossed_ref, half_ref, prior_ref)
    responsibility = jnp.exp(scores - norm_ref[...]).astype(jnp.bfloat16)
    spectra_ref[...] = jnp.dot(
        turn_ref[...], responsibility, preferred_element_type=jnp.float32
    ).astype(jnp.bfloat16)
    weight_ref[...] = jnp.sum(responsibility.astype(jnp.float32), axis=0, keepdims=True)


def local(references, particles, defocus_bin, contrast_table, noise_power, class_prior):
    weighted, power_term = particle_terms(particles, defocus_bin, contrast_table, noise_power)
    score_table, turn_table = angle_tables(M, R)
    columns = particles.shape[1]
    dev_count = lax.axis_size("dev")
    classes_total = CLS_DEV * dev_count

    copies = jnp.broadcast_to(references[None], (dev_count,) + references.shape)
    gathered = lax.all_to_all(copies, "dev", 0, 0, tiled=True).reshape(
        dev_count * references.shape[0], references.shape[1]
    )
    stacked, cycle_power = class_rows(gathered)
    crossed = jnp.einsum(
        "pkmc,mcb->mpkb", stacked, weighted, preferred_element_type=jnp.float32
    ).astype(jnp.bfloat16)
    rows = 2 * M
    width = classes_total * columns
    crossed = crossed.reshape(rows, width)
    penalty = jnp.dot(cycle_power, power_term, precision=lax.Precision.HIGHEST)
    half = (0.5 * penalty).reshape(1, width)
    prior = jnp.broadcast_to(class_prior[:, None], (classes_total, columns)).reshape(1, width)
    table = jnp.transpose(score_table, (2, 1, 0)).reshape(R, rows)
    turn = jnp.transpose(turn_table, (1, 0, 2)).reshape(rows, R)

    block = CLS_STEP * columns
    steps = width // block
    table_spec = pl.BlockSpec((R, rows), lambda i: (0, 0))
    crossed_spec = pl.BlockSpec((rows, block), lambda i: (0, i))
    row_spec = pl.BlockSpec((1, block), lambda i: (0, i))
    log_norm = pl.pallas_call(
        functools.partial(norm_kernel, columns),
        grid=(steps,),
        in_specs=[table_spec, crossed_spec, row_spec, row_spec],
        out_specs=pl.BlockSpec((1, columns), lambda i: (0, 0)),
        out_shape=jax.ShapeDtypeStruct((1, columns), jnp.float32),
        scratch_shapes=[pltpu.VMEM((1, columns), jnp.float32)] * 2,
        compiler_params=pltpu.CompilerParams(dimension_semantics=("arbitrary",)),
    )(table, crossed, half, prior)
    norm_row = jnp.tile(log_norm, (1, classes_total))
    spectra, class_weight = pl.pallas_call(
        spectra_kernel,
        grid=(steps,),
        in_specs=[
            table_spec,
            crossed_spec,
            row_spec,
            row_spec,
            row_spec,
            pl.BlockSpec((rows, R), lambda i: (0, 0)),
        ],
        out_specs=[crossed_spec, row_spec],
        out_shape=[
            jax.ShapeDtypeStruct((rows, width), jnp.bfloat16),
            jax.ShapeDtypeStruct((1, width), jnp.float32),
        ],
        compiler_params=pltpu.CompilerParams(dimension_semantics=("arbitrary",)),
    )(table, crossed, half, prior, norm_row, turn)

    spectra = spectra.reshape(M, 2, classes_total, columns)
    products = jnp.einsum(
        "mpkb,mcb->kpmc", spectra, weighted, preferred_element_type=jnp.float32
    )
    real_sum = products[:, 0, :, :Q] + products[:, 1, :, Q:]
    imag_sum = products[:, 0, :, Q:] - products[:, 1, :, :Q]
    numer_all = jnp.stack([real_sum, imag_sum], 2).reshape(classes_total, 2 * M * Q)
    class_weight = class_weight.reshape(classes_total, columns)
    cycles_all = jnp.dot(class_weight, power_term.T, precision=lax.Precision.HIGHEST)
    mass_all = jnp.sum(class_weight, axis=1)

    width = numer_all.shape[1]
    packed = jnp.concatenate(
        [numer_all, cycles_all, mass_all[:, None], jnp.zeros((classes_total, 95), jnp.float32)], 1
    )
    packed = packed.reshape(dev_count, CLS_DEV, packed.shape[1])
    own = jnp.sum(lax.all_to_all(packed, "dev", 0, 0, tiled=True), 0)
    own = jnp.sum(lax.all_gather(own, "grp", axis=0, tiled=False), 0)
    numerator = own[:, :width]
    cycle_sum = own[:, width : width + Q]
    class_mass = own[:, width + Q]
    new_references = (numerator.reshape(CLS_DEV, M, 2, Q) / cycle_sum[:, None, None, :]).reshape(
        CLS_DEV, 2 * M * Q
    )
    particle_total = columns * lax.axis_size("grp") * lax.axis_size("dev")
    occupancy = class_mass * (classes_total / particle_total)
    return (new_references, occupancy)


def solution(mesh):
    return jax.shard_map(
        local,
        mesh=mesh,
        in_specs=(P("dev", None), P(None, ("grp", "dev")), P(("grp", "dev")), P(), P(), P()),
        out_specs=(P("dev", None), P("dev")),
        check_vma=False,
    )
```

```python
import functools
import math

import jax
import jax.numpy as jnp
from jax import lax
from jax.experimental import pallas as pl
from jax.experimental.pallas import tpu as pltpu
from jax.sharding import PartitionSpec as P

Q = 32
M = 32
R = 128
CLS_DEV = 6
CLS_STEP = 8


def angle_tables(cycle_freqs, count_turns):
    freq_index = jnp.arange(cycle_freqs, dtype=jnp.int32)
    turn_index = jnp.arange(count_turns, dtype=jnp.int32)
    wrapped = freq_index[:, None] * turn_index[None, :] % count_turns
    phases = 2.0 * math.pi / count_turns * wrapped.astype(jnp.float32)
    factor = jnp.where(freq_index == 0, 1.0, 2.0).astype(jnp.float32)[:, None]
    cosine = jnp.cos(phases)
    sine_part = jnp.sin(phases)
    score_table = jnp.stack([factor * cosine, factor * sine_part], 0).astype(jnp.bfloat16)
    turn_table = jnp.stack([cosine, sine_part], 0).astype(jnp.bfloat16)
    return (score_table, turn_table)


def particle_terms(particles, defocus_bin, contrast_table, noise_power):
    columns = particles.shape[1]
    cycle_count = contrast_table.shape[1]
    freq_count = particles.shape[0] // (2 * cycle_count)
    onehot = (
        defocus_bin[None, :] == jnp.arange(contrast_table.shape[0], dtype=jnp.int32)[:, None]
    ).astype(jnp.float32)
    contrast = jnp.dot(contrast_table.T, onehot, precision=lax.Precision.HIGHEST)
    scaled = contrast / noise_power[:, None]
    power_term = contrast * scaled
    weighted = (
        particles.astype(jnp.float32).reshape(freq_count, 2, cycle_count, columns)
        * scaled[None, None]
    ).astype(jnp.bfloat16)
    return (weighted.reshape(freq_count, 2 * cycle_count, columns), power_term)


def block_scores(table_ref, real_ref, imag_ref, half_ref, prior_ref):
    raw = jnp.dot(table_ref[0], real_ref[...], preferred_element_type=jnp.float32)
    raw = raw + jnp.dot(table_ref[1], imag_ref[...], preferred_element_type=jnp.float32)
    return raw - half_ref[...] + prior_ref[...]


def norm_kernel(
    cols, table_ref, real_ref, imag_ref, half_ref, prior_ref, out_ref, top_ref, total_ref
):
    step = pl.program_id(0)

    @pl.when(step == 0)
    def _():
        top_ref[...] = jnp.full(top_ref.shape, -1e30, jnp.float32)
        total_ref[...] = jnp.zeros(total_ref.shape, jnp.float32)

    scores = block_scores(table_ref, real_ref, imag_ref, half_ref, prior_ref)
    parts = [scores[:, j * cols : (j + 1) * cols] for j in range(scores.shape[1] // cols)]
    block_top = functools.reduce(jnp.maximum, [jnp.max(s, axis=0, keepdims=True) for s in parts])
    old_top = top_ref[...]
    new_top = jnp.maximum(old_top, block_top)
    block_total = functools.reduce(
        jnp.add, [jnp.sum(jnp.exp(s - new_top), axis=0, keepdims=True) for s in parts]
    )
    total_ref[...] = total_ref[...] * jnp.exp(old_top - new_top) + block_total
    top_ref[...] = new_top

    @pl.when(step == pl.num_programs(0) - 1)
    def _():
        out_ref[...] = top_ref[...] + jnp.log(total_ref[...])


def spectra_kernel(
    table_ref, real_ref, imag_ref, half_ref, prior_ref, norm_ref, turn_ref, spectra_ref, weight_ref
):
    scores = block_scores(table_ref, real_ref, imag_ref, half_ref, prior_ref)
    responsibility = jnp.exp(scores - norm_ref[...]).astype(jnp.bfloat16)
    spectra_ref[...] = jnp.dot(
        turn_ref[...], responsibility, preferred_element_type=jnp.float32
    ).astype(jnp.bfloat16)
    weight_ref[...] = jnp.sum(responsibility.astype(jnp.float32), axis=0, keepdims=True)


def local(references, particles, defocus_bin, contrast_table, noise_power, class_prior):
    weighted, power_term = particle_terms(particles, defocus_bin, contrast_table, noise_power)
    score_table, turn_table = angle_tables(M, R)
    columns = particles.shape[1]
    dev_count = lax.axis_size("dev")
    classes_total = CLS_DEV * dev_count

    own_rows = jnp.transpose(references.reshape(CLS_DEV, M, 2 * Q), (1, 0, 2))
    copies = jnp.broadcast_to(own_rows[None], (dev_count,) + own_rows.shape)
    gathered = lax.all_to_all(copies, "dev", 0, 0, tiled=True)
    grid_rows = jnp.transpose(gathered, (1, 0, 2, 3)).reshape(M, classes_total, 2 * Q)
    factor = jnp.where(jnp.arange(M) == 0, 1.0, 2.0).astype(jnp.float32)
    squares = jnp.sum(grid_rows.astype(jnp.float32) ** 2 * factor[:, None, None], axis=0)
    cycle_power = squares[:, :Q] + squares[:, Q:]
    swapped = jnp.concatenate([weighted[:, Q:], -weighted[:, :Q]], 1)
    rows = M
    width = classes_total * columns
    crossed_real = jnp.einsum(
        "mkc,mcb->mkb", grid_rows, weighted, preferred_element_type=jnp.float32
    ).astype(jnp.bfloat16).reshape(rows, width)
    crossed_imag = jnp.einsum(
        "mkc,mcb->mkb", grid_rows, swapped, preferred_element_type=jnp.float32
    ).astype(jnp.bfloat16).reshape(rows, width)
    penalty = jnp.dot(cycle_power, power_term, precision=lax.Precision.HIGHEST)
    half = (0.5 * penalty).reshape(1, width)
    prior = jnp.broadcast_to(class_prior[:, None], (classes_total, columns)).reshape(1, width)
    table = jnp.transpose(score_table, (0, 2, 1))
    turn = turn_table.reshape(2 * M, R)

    block = CLS_STEP * columns
    steps = width // block
    table_spec = pl.BlockSpec((2, R, rows), lambda i: (0, 0, 0))
    crossed_spec = pl.BlockSpec((rows, block), lambda i: (0, i))
    row_spec = pl.BlockSpec((1, block), lambda i: (0, i))
    log_norm = pl.pallas_call(
        functools.partial(norm_kernel, columns),
        grid=(steps,),
        in_specs=[table_spec, crossed_spec, crossed_spec, row_spec, row_spec],
        out_specs=pl.BlockSpec((1, columns), lambda i: (0, 0)),
        out_shape=jax.ShapeDtypeStruct((1, columns), jnp.float32),
        scratch_shapes=[pltpu.VMEM((1, columns), jnp.float32)] * 2,
        compiler_params=pltpu.CompilerParams(dimension_semantics=("arbitrary",)),
    )(table, crossed_real, crossed_imag, half, prior)
    norm_row = jnp.tile(log_norm, (1, classes_total))
    spectra, class_weight = pl.pallas_call(
        spectra_kernel,
        grid=(steps,),
        in_specs=[
            table_spec,
            crossed_spec,
            crossed_spec,
            row_spec,
            row_spec,
            row_spec,
            pl.BlockSpec((2 * rows, R), lambda i: (0, 0)),
        ],
        out_specs=[pl.BlockSpec((2 * rows, block), lambda i: (0, i)), row_spec],
        out_shape=[
            jax.ShapeDtypeStruct((2 * rows, width), jnp.bfloat16),
            jax.ShapeDtypeStruct((1, width), jnp.float32),
        ],
        compiler_params=pltpu.CompilerParams(dimension_semantics=("arbitrary",)),
    )(table, crossed_real, crossed_imag, half, prior, norm_row, turn)

    spectra = spectra.reshape(2, M, classes_total, columns)
    numer_all = jnp.einsum(
        "mkb,mcb->kmc", spectra[0], weighted, preferred_element_type=jnp.float32
    ) + jnp.einsum("mkb,mcb->kmc", spectra[1], swapped, preferred_element_type=jnp.float32)
    numer_all = numer_all.reshape(classes_total, 2 * M * Q)
    class_weight = class_weight.reshape(classes_total, columns)
    cycles_all = jnp.dot(class_weight, power_term.T, precision=lax.Precision.HIGHEST)
    mass_all = jnp.sum(class_weight, axis=1)

    width = numer_all.shape[1]
    packed = jnp.concatenate(
        [numer_all, cycles_all, mass_all[:, None], jnp.zeros((classes_total, 95), jnp.float32)], 1
    )
    packed = packed.reshape(dev_count, CLS_DEV, packed.shape[1])
    own = jnp.sum(lax.all_to_all(packed, "dev", 0, 0, tiled=True), 0)
    own = jnp.sum(lax.all_gather(own, "grp", axis=0, tiled=False), 0)
    numerator = own[:, :width]
    cycle_sum = own[:, width : width + Q]
    class_mass = own[:, width + Q]
    new_references = (numerator.reshape(CLS_DEV, M, 2, Q) / cycle_sum[:, None, None, :]).reshape(
        CLS_DEV, 2 * M * Q
    )
    particle_total = columns * lax.axis_size("grp") * lax.axis_size("dev")
    occupancy = class_mass * (classes_total / particle_total)
    return (new_references, occupancy)


def solution(mesh):
    return jax.shard_map(
        local,
        mesh=mesh,
        in_specs=(P("dev", None), P(None, ("grp", "dev")), P(("grp", "dev")), P(), P(), P()),
        out_specs=(P("dev", None), P("dev")),
        check_vma=False,
    )
```

```python
import functools
import math

import jax
import jax.numpy as jnp
from jax import lax
from jax.experimental import pallas as pl
from jax.experimental.pallas import tpu as pltpu
from jax.sharding import PartitionSpec as P

Q = 32
M = 32
R = 128
CLS_DEV = 6
CLS_STEP = 8
GRP = ("x", "core")
DEV = ("z", "y")


def angle_tables(cycle_freqs, count_turns):
    freq_index = jnp.arange(cycle_freqs, dtype=jnp.int32)
    turn_index = jnp.arange(count_turns, dtype=jnp.int32)
    wrapped = freq_index[:, None] * turn_index[None, :] % count_turns
    phases = 2.0 * math.pi / count_turns * wrapped.astype(jnp.float32)
    factor = jnp.where(freq_index == 0, 1.0, 2.0).astype(jnp.float32)[:, None]
    cosine = jnp.cos(phases)
    sine_part = jnp.sin(phases)
    score_table = jnp.stack([factor * cosine, factor * sine_part], 0).astype(jnp.bfloat16)
    turn_table = jnp.stack([cosine, sine_part], 0).astype(jnp.bfloat16)
    return (score_table, turn_table)


def particle_terms(particles, defocus_bin, contrast_table, noise_power):
    columns = particles.shape[1]
    cycle_count = contrast_table.shape[1]
    freq_count = particles.shape[0] // (2 * cycle_count)
    onehot = (
        defocus_bin[None, :] == jnp.arange(contrast_table.shape[0], dtype=jnp.int32)[:, None]
    ).astype(jnp.float32)
    contrast = jnp.dot(contrast_table.T, onehot, precision=lax.Precision.HIGHEST)
    scaled = contrast / noise_power[:, None]
    power_term = contrast * scaled
    weighted = (
        particles.astype(jnp.float32).reshape(freq_count, 2, cycle_count, columns)
        * scaled[None, None]
    ).astype(jnp.bfloat16)
    return (weighted.reshape(freq_count, 2 * cycle_count, columns), power_term)


def block_scores(table_ref, real_ref, imag_ref, half_ref, prior_ref):
    raw = jnp.dot(table_ref[0], real_ref[...], preferred_element_type=jnp.float32)
    raw = raw + jnp.dot(table_ref[1], imag_ref[...], preferred_element_type=jnp.float32)
    return raw - half_ref[...] + prior_ref[...]


def norm_kernel(
    cols, table_ref, real_ref, imag_ref, half_ref, prior_ref, out_ref, top_ref, total_ref
):
    step = pl.program_id(0)

    @pl.when(step == 0)
    def _():
        top_ref[...] = jnp.full(top_ref.shape, -1e30, jnp.float32)
        total_ref[...] = jnp.zeros(total_ref.shape, jnp.float32)

    scores = block_scores(table_ref, real_ref, imag_ref, half_ref, prior_ref)
    parts = [scores[:, j * cols : (j + 1) * cols] for j in range(scores.shape[1] // cols)]
    block_top = functools.reduce(jnp.maximum, [jnp.max(s, axis=0, keepdims=True) for s in parts])
    old_top = top_ref[...]
    new_top = jnp.maximum(old_top, block_top)
    block_total = functools.reduce(
        jnp.add, [jnp.sum(jnp.exp(s - new_top), axis=0, keepdims=True) for s in parts]
    )
    total_ref[...] = total_ref[...] * jnp.exp(old_top - new_top) + block_total
    top_ref[...] = new_top

    @pl.when(step == pl.num_programs(0) - 1)
    def _():
        out_ref[...] = top_ref[...] + jnp.log(total_ref[...])


def spectra_kernel(
    table_ref, real_ref, imag_ref, half_ref, prior_ref, norm_ref, turn_ref, spectra_ref, weight_ref
):
    scores = block_scores(table_ref, real_ref, imag_ref, half_ref, prior_ref)
    responsibility = jnp.exp(scores - norm_ref[...]).astype(jnp.bfloat16)
    spectra_ref[...] = jnp.dot(
        turn_ref[...], responsibility, preferred_element_type=jnp.float32
    ).astype(jnp.bfloat16)
    weight_ref[...] = jnp.sum(responsibility.astype(jnp.float32), axis=0, keepdims=True)


def local(references, particles, defocus_bin, contrast_table, noise_power, class_prior):
    weighted, power_term = particle_terms(particles, defocus_bin, contrast_table, noise_power)
    score_table, turn_table = angle_tables(M, R)
    columns = particles.shape[1]
    dev_count = lax.axis_size(DEV)
    classes_total = CLS_DEV * dev_count

    own_rows = jnp.transpose(references.reshape(CLS_DEV, M, 2 * Q), (1, 0, 2))
    copies = jnp.broadcast_to(own_rows[None], (dev_count,) + own_rows.shape)
    gathered = lax.all_to_all(copies, DEV, 0, 0, tiled=True)
    grid_rows = jnp.transpose(gathered, (1, 0, 2, 3)).reshape(M, classes_total, 2 * Q)
    factor = jnp.where(jnp.arange(M) == 0, 1.0, 2.0).astype(jnp.float32)
    squares = jnp.sum(grid_rows.astype(jnp.float32) ** 2 * factor[:, None, None], axis=0)
    cycle_power = squares[:, :Q] + squares[:, Q:]
    swapped = jnp.concatenate([weighted[:, Q:], -weighted[:, :Q]], 1)
    rows = M
    width = classes_total * columns
    crossed_real = jnp.einsum(
        "mkc,mcb->mkb", grid_rows, weighted, preferred_element_type=jnp.float32
    ).astype(jnp.bfloat16).reshape(rows, width)
    crossed_imag = jnp.einsum(
        "mkc,mcb->mkb", grid_rows, swapped, preferred_element_type=jnp.float32
    ).astype(jnp.bfloat16).reshape(rows, width)
    penalty = jnp.dot(cycle_power, power_term, precision=lax.Precision.HIGHEST)
    half = (0.5 * penalty).reshape(1, width)
    prior = jnp.broadcast_to(class_prior[:, None], (classes_total, columns)).reshape(1, width)
    table = jnp.transpose(score_table, (0, 2, 1))
    turn = turn_table.reshape(2 * M, R)

    block = CLS_STEP * columns
    steps = width // block
    table_spec = pl.BlockSpec((2, R, rows), lambda i: (0, 0, 0))
    crossed_spec = pl.BlockSpec((rows, block), lambda i: (0, i))
    row_spec = pl.BlockSpec((1, block), lambda i: (0, i))
    log_norm = pl.pallas_call(
        functools.partial(norm_kernel, columns),
        grid=(steps,),
        in_specs=[table_spec, crossed_spec, crossed_spec, row_spec, row_spec],
        out_specs=pl.BlockSpec((1, columns), lambda i: (0, 0)),
        out_shape=jax.ShapeDtypeStruct((1, columns), jnp.float32),
        scratch_shapes=[pltpu.VMEM((1, columns), jnp.float32)] * 2,
        compiler_params=pltpu.CompilerParams(dimension_semantics=("arbitrary",)),
    )(table, crossed_real, crossed_imag, half, prior)
    norm_row = jnp.tile(log_norm, (1, classes_total))
    spectra, class_weight = pl.pallas_call(
        spectra_kernel,
        grid=(steps,),
        in_specs=[
            table_spec,
            crossed_spec,
            crossed_spec,
            row_spec,
            row_spec,
            row_spec,
            pl.BlockSpec((2 * rows, R), lambda i: (0, 0)),
        ],
        out_specs=[pl.BlockSpec((2 * rows, block), lambda i: (0, i)), row_spec],
        out_shape=[
            jax.ShapeDtypeStruct((2 * rows, width), jnp.bfloat16),
            jax.ShapeDtypeStruct((1, width), jnp.float32),
        ],
        compiler_params=pltpu.CompilerParams(dimension_semantics=("arbitrary",)),
    )(table, crossed_real, crossed_imag, half, prior, norm_row, turn)

    spectra = spectra.reshape(2, M, classes_total, columns)
    numer_all = jnp.einsum(
        "mkb,mcb->kmc", spectra[0], weighted, preferred_element_type=jnp.float32
    ) + jnp.einsum("mkb,mcb->kmc", spectra[1], swapped, preferred_element_type=jnp.float32)
    numer_all = numer_all.reshape(classes_total, 2 * M * Q)
    class_weight = class_weight.reshape(classes_total, columns)
    cycles_all = jnp.dot(class_weight, power_term.T, precision=lax.Precision.HIGHEST)
    mass_all = jnp.sum(class_weight, axis=1)

    width = numer_all.shape[1]
    packed = jnp.concatenate(
        [numer_all, cycles_all, mass_all[:, None], jnp.zeros((classes_total, 95), jnp.float32)], 1
    )
    packed = packed.reshape(lax.axis_size("z"), lax.axis_size("y"), CLS_DEV, packed.shape[1])
    own = jnp.sum(lax.all_to_all(packed, "y", 1, 1, tiled=True), 1)
    own = jnp.sum(lax.all_to_all(own, "z", 0, 0, tiled=True), 0)
    own = jnp.sum(lax.all_gather(own, GRP, axis=0, tiled=False), 0)
    numerator = own[:, :width]
    cycle_sum = own[:, width : width + Q]
    class_mass = own[:, width + Q]
    new_references = (numerator.reshape(CLS_DEV, M, 2, Q) / cycle_sum[:, None, None, :]).reshape(
        CLS_DEV, 2 * M * Q
    )
    particle_total = columns * lax.axis_size(GRP) * lax.axis_size(DEV)
    occupancy = class_mass * (classes_total / particle_total)
    return (new_references, occupancy)


def solution(mesh):
    grp_count, dev_count = mesh.devices.shape
    core_count = 2
    y_count = 4
    split = jax.sharding.Mesh(
        mesh.devices.reshape(
            grp_count // core_count, core_count, dev_count // y_count, y_count
        ),
        GRP + DEV,
    )
    return jax.shard_map(
        local,
        mesh=split,
        in_specs=(P(DEV, None), P(None, GRP + DEV), P(GRP + DEV), P(), P(), P()),
        out_specs=(P(DEV, None), P(DEV)),
        check_vma=False,
    )
```

```python
import functools
import math

import jax
import jax.numpy as jnp
from jax import lax
from jax.experimental import pallas as pl
from jax.experimental.pallas import tpu as pltpu
from jax.sharding import PartitionSpec as P

Q = 32
M = 32
R = 128
CLS_DEV = 6
CLS_STEP = 24
GRP = ("x", "core")
DEV = ("z", "y")


def angle_tables(cycle_freqs, count_turns):
    freq_index = jnp.arange(cycle_freqs, dtype=jnp.int32)
    turn_index = jnp.arange(count_turns, dtype=jnp.int32)
    wrapped = freq_index[:, None] * turn_index[None, :] % count_turns
    phases = 2.0 * math.pi / count_turns * wrapped.astype(jnp.float32)
    factor = jnp.where(freq_index == 0, 1.0, 2.0).astype(jnp.float32)[:, None]
    cosine = jnp.cos(phases)
    sine_part = jnp.sin(phases)
    score_table = jnp.stack([factor * cosine, factor * sine_part], 0).astype(jnp.bfloat16)
    turn_table = jnp.stack([cosine, sine_part], 0).astype(jnp.bfloat16)
    return (score_table, turn_table)


def particle_terms(particles, defocus_bin, contrast_table, noise_power):
    columns = particles.shape[1]
    cycle_count = contrast_table.shape[1]
    freq_count = particles.shape[0] // (2 * cycle_count)
    onehot = (
        defocus_bin[None, :] == jnp.arange(contrast_table.shape[0], dtype=jnp.int32)[:, None]
    ).astype(jnp.float32)
    contrast = jnp.dot(contrast_table.T, onehot, precision=lax.Precision.HIGHEST)
    scaled = contrast / noise_power[:, None]
    power_term = contrast * scaled
    weighted = (
        particles.astype(jnp.float32).reshape(freq_count, 2, cycle_count, columns)
        * scaled[None, None]
    ).astype(jnp.bfloat16)
    return (weighted.reshape(freq_count, 2 * cycle_count, columns), power_term)


def block_scores(table_ref, real_ref, imag_ref, shift_ref):
    crossed = jnp.concatenate([real_ref[...], imag_ref[...]], 0)
    raw = jnp.dot(table_ref[...], crossed, preferred_element_type=jnp.float32)
    return raw + shift_ref[...]


def norm_kernel(cols, table_ref, real_ref, imag_ref, bias_ref, out_ref, top_ref, total_ref):
    step = pl.program_id(0)

    @pl.when(step == 0)
    def _():
        top_ref[...] = jnp.full(top_ref.shape, -1e30, jnp.float32)
        total_ref[...] = jnp.zeros(total_ref.shape, jnp.float32)

    scores = block_scores(table_ref, real_ref, imag_ref, bias_ref)
    parts = [scores[:, j * cols : (j + 1) * cols] for j in range(scores.shape[1] // cols)]
    block_top = functools.reduce(jnp.maximum, [jnp.max(s, axis=0, keepdims=True) for s in parts])
    old_top = top_ref[...]
    new_top = jnp.maximum(old_top, block_top)
    block_total = functools.reduce(
        jnp.add, [jnp.sum(jnp.exp(s - new_top), axis=0, keepdims=True) for s in parts]
    )
    total_ref[...] = total_ref[...] * jnp.exp(old_top - new_top) + block_total
    top_ref[...] = new_top

    @pl.when(step == pl.num_programs(0) - 1)
    def _():
        out_ref[...] = top_ref[...] + jnp.log(total_ref[...])


def spectra_kernel(table_ref, real_ref, imag_ref, shift_ref, turn_ref, spectra_ref, weight_ref):
    responsibility = jnp.exp(block_scores(table_ref, real_ref, imag_ref, shift_ref))
    full = jnp.dot(
        turn_ref[...], responsibility.astype(jnp.bfloat16), preferred_element_type=jnp.float32
    )
    rows = spectra_ref.shape[0]
    spectra_ref[...] = full[:rows].astype(jnp.bfloat16)
    weight_ref[...] = full[rows : rows + 1]


def local(references, particles, defocus_bin, contrast_table, noise_power, class_prior):
    weighted, power_term = particle_terms(particles, defocus_bin, contrast_table, noise_power)
    score_table, turn_table = angle_tables(M, R)
    columns = particles.shape[1]
    dev_count = lax.axis_size(DEV)
    classes_total = CLS_DEV * dev_count

    own_rows = jnp.transpose(references.reshape(CLS_DEV, M, 2 * Q), (1, 0, 2))
    copies = jnp.broadcast_to(own_rows[None], (dev_count,) + own_rows.shape)
    gathered = lax.all_to_all(copies, DEV, 0, 0, tiled=True)
    grid_rows = jnp.transpose(gathered, (1, 0, 2, 3)).reshape(M, classes_total, 2 * Q)
    factor = jnp.where(jnp.arange(M) == 0, 1.0, 2.0).astype(jnp.float32)
    squares = jnp.sum(grid_rows.astype(jnp.float32) ** 2 * factor[:, None, None], axis=0)
    cycle_power = squares[:, :Q] + squares[:, Q:]
    swapped = jnp.concatenate([weighted[:, Q:], -weighted[:, :Q]], 1)
    rows = M
    width = classes_total * columns
    crossed_real = jnp.einsum(
        "mkc,mcb->mkb", grid_rows, weighted, preferred_element_type=jnp.float32
    ).astype(jnp.bfloat16).reshape(rows, width)
    crossed_imag = jnp.einsum(
        "mkc,mcb->mkb", grid_rows, swapped, preferred_element_type=jnp.float32
    ).astype(jnp.bfloat16).reshape(rows, width)
    penalty = jnp.dot(cycle_power, power_term, precision=lax.Precision.HIGHEST)
    bias = (class_prior[:, None] - 0.5 * penalty).reshape(1, width)
    table = jnp.transpose(score_table, (2, 0, 1)).reshape(R, 2 * M)
    turn = jnp.concatenate(
        [turn_table.reshape(2 * M, R), jnp.ones((1, R), jnp.bfloat16), jnp.zeros((15, R), jnp.bfloat16)], 0
    )

    block = CLS_STEP * columns
    steps = width // block
    table_spec = pl.BlockSpec((R, 2 * rows), lambda i: (0, 0))
    crossed_spec = pl.BlockSpec((rows, block), lambda i: (0, i))
    row_spec = pl.BlockSpec((1, block), lambda i: (0, i))
    log_norm = pl.pallas_call(
        functools.partial(norm_kernel, columns),
        grid=(steps,),
        in_specs=[table_spec, crossed_spec, crossed_spec, row_spec],
        out_specs=pl.BlockSpec((1, columns), lambda i: (0, 0)),
        out_shape=jax.ShapeDtypeStruct((1, columns), jnp.float32),
        scratch_shapes=[pltpu.VMEM((1, columns), jnp.float32)] * 2,
        compiler_params=pltpu.CompilerParams(dimension_semantics=("arbitrary",)),
    )(table, crossed_real, crossed_imag, bias)
    shift = bias - jnp.tile(log_norm, (1, classes_total))
    spectra, class_weight = pl.pallas_call(
        spectra_kernel,
        grid=(steps,),
        in_specs=[
            table_spec,
            crossed_spec,
            crossed_spec,
            row_spec,
            pl.BlockSpec(turn.shape, lambda i: (0, 0)),
        ],
        out_specs=[pl.BlockSpec((2 * rows, block), lambda i: (0, i)), row_spec],
        out_shape=[
            jax.ShapeDtypeStruct((2 * rows, width), jnp.bfloat16),
            jax.ShapeDtypeStruct((1, width), jnp.float32),
        ],
        compiler_params=pltpu.CompilerParams(dimension_semantics=("arbitrary",)),
    )(table, crossed_real, crossed_imag, shift, turn)

    spectra = spectra.reshape(2, M, classes_total, columns)
    numer_all = jnp.einsum(
        "mkb,mcb->kmc", spectra[0], weighted, preferred_element_type=jnp.float32
    ) + jnp.einsum("mkb,mcb->kmc", spectra[1], swapped, preferred_element_type=jnp.float32)
    numer_all = numer_all.reshape(classes_total, 2 * M * Q)
    class_weight = class_weight.reshape(classes_total, columns)
    cycles_all = jnp.dot(class_weight, power_term.T, precision=lax.Precision.HIGHEST)
    mass_all = jnp.sum(class_weight, axis=1)

    width = numer_all.shape[1]
    packed = jnp.concatenate(
        [numer_all, cycles_all, mass_all[:, None], jnp.zeros((classes_total, 95), jnp.float32)], 1
    )
    packed = packed.reshape(lax.axis_size("z"), lax.axis_size("y"), CLS_DEV, packed.shape[1])
    own = jnp.sum(lax.all_to_all(packed, "y", 1, 1, tiled=True), 1)
    own = jnp.sum(lax.all_to_all(own, "z", 0, 0, tiled=True), 0)
    own = jnp.sum(lax.all_gather(own, GRP, axis=0, tiled=False), 0)
    numerator = own[:, :width]
    cycle_sum = own[:, width : width + Q]
    class_mass = own[:, width + Q]
    new_references = (numerator.reshape(CLS_DEV, M, 2, Q) / cycle_sum[:, None, None, :]).reshape(
        CLS_DEV, 2 * M * Q
    )
    particle_total = columns * lax.axis_size(GRP) * lax.axis_size(DEV)
    occupancy = class_mass * (classes_total / particle_total)
    return (new_references, occupancy)


def solution(mesh):
    grp_count, dev_count = mesh.devices.shape
    core_count = 2
    y_count = 4
    split = jax.sharding.Mesh(
        mesh.devices.reshape(
            grp_count // core_count, core_count, dev_count // y_count, y_count
        ),
        GRP + DEV,
    )
    return jax.shard_map(
        local,
        mesh=split,
        in_specs=(P(DEV, None), P(None, GRP + DEV), P(GRP + DEV), P(), P(), P()),
        out_specs=(P(DEV, None), P(DEV)),
        check_vma=False,
    )
```

```python
import functools
import math

import jax
import jax.numpy as jnp
from jax import lax
from jax.experimental import pallas as pl
from jax.experimental.pallas import tpu as pltpu
from jax.sharding import PartitionSpec as P

Q = 32
M = 32
R = 128
CLS_DEV = 6
CLS_STEP = 24
GRP = ("x", "core")
DEV = ("z", "y")


def angle_tables(cycle_freqs, count_turns):
    freq_index = jnp.arange(cycle_freqs, dtype=jnp.int32)
    turn_index = jnp.arange(count_turns, dtype=jnp.int32)
    wrapped = freq_index[:, None] * turn_index[None, :] % count_turns
    phases = 2.0 * math.pi / count_turns * wrapped.astype(jnp.float32)
    factor = jnp.where(freq_index == 0, 1.0, 2.0).astype(jnp.float32)[:, None]
    cosine = jnp.cos(phases)
    sine_part = jnp.sin(phases)
    score_table = jnp.stack([factor * cosine, factor * sine_part], 0).astype(jnp.bfloat16)
    turn_table = jnp.stack([cosine, sine_part], 0).astype(jnp.bfloat16)
    return (score_table, turn_table)


def particle_terms(particles, defocus_bin, contrast_table, noise_power):
    columns = particles.shape[1]
    cycle_count = contrast_table.shape[1]
    freq_count = particles.shape[0] // (2 * cycle_count)
    onehot = (
        defocus_bin[None, :] == jnp.arange(contrast_table.shape[0], dtype=jnp.int32)[:, None]
    ).astype(jnp.float32)
    contrast = jnp.dot(contrast_table.T, onehot, precision=lax.Precision.HIGHEST)
    scaled = contrast / noise_power[:, None]
    power_term = contrast * scaled
    weighted = (
        particles.astype(jnp.float32).reshape(freq_count, 2, cycle_count, columns)
        * scaled[None, None]
    ).astype(jnp.bfloat16)
    return (weighted.reshape(freq_count, 2 * cycle_count, columns), power_term)


def block_scores(table_ref, real_ref, imag_ref, shift_ref):
    crossed = jnp.concatenate([real_ref[...], imag_ref[...]], 0)
    raw = jnp.dot(table_ref[...], crossed, preferred_element_type=jnp.float32)
    return raw + shift_ref[...]


def norm_kernel(cols, table_ref, real_ref, imag_ref, bias_ref, out_ref, top_ref, total_ref):
    step = pl.program_id(0)

    @pl.when(step == 0)
    def _():
        top_ref[...] = jnp.full(top_ref.shape, -1e30, jnp.float32)
        total_ref[...] = jnp.zeros(total_ref.shape, jnp.float32)

    scores = block_scores(table_ref, real_ref, imag_ref, bias_ref)
    parts = [scores[:, j * cols : (j + 1) * cols] for j in range(scores.shape[1] // cols)]
    block_top = functools.reduce(jnp.maximum, [jnp.max(s, axis=0, keepdims=True) for s in parts])
    old_top = top_ref[...]
    new_top = jnp.maximum(old_top, block_top)
    block_total = functools.reduce(
        jnp.add, [jnp.sum(jnp.exp(s - new_top), axis=0, keepdims=True) for s in parts]
    )
    total_ref[...] = total_ref[...] * jnp.exp(old_top - new_top) + block_total
    top_ref[...] = new_top

    @pl.when(step == pl.num_programs(0) - 1)
    def _():
        out_ref[...] = top_ref[...] + jnp.log(total_ref[...])


def spectra_kernel(
    table_ref, real_ref, imag_ref, shift_ref, turn_ref, cos_ref, sin_ref, weight_ref
):
    responsibility = jnp.exp(block_scores(table_ref, real_ref, imag_ref, shift_ref))
    full = jnp.dot(
        turn_ref[...], responsibility.astype(jnp.bfloat16), preferred_element_type=jnp.float32
    )
    rows = cos_ref.shape[0]
    cos_ref[...] = full[:rows].astype(jnp.bfloat16)
    sin_ref[...] = full[rows : 2 * rows].astype(jnp.bfloat16)
    weight_ref[...] = full[2 * rows : 2 * rows + 1]


def local(references, particles, defocus_bin, contrast_table, noise_power, class_prior):
    weighted, power_term = particle_terms(particles, defocus_bin, contrast_table, noise_power)
    score_table, turn_table = angle_tables(M, R)
    columns = particles.shape[1]
    dev_count = lax.axis_size(DEV)
    classes_total = CLS_DEV * dev_count

    own_rows = jnp.transpose(references.reshape(CLS_DEV, M, 2 * Q), (1, 0, 2))
    copies = jnp.broadcast_to(own_rows[None], (dev_count,) + own_rows.shape)
    gathered = lax.all_to_all(copies, DEV, 0, 0, tiled=True)
    grid_rows = jnp.transpose(gathered, (1, 0, 2, 3)).reshape(M, classes_total, 2 * Q)
    factor = jnp.where(jnp.arange(M) == 0, 1.0, 2.0).astype(jnp.float32)
    squares = jnp.sum(grid_rows.astype(jnp.float32) ** 2 * factor[:, None, None], axis=0)
    cycle_power = squares[:, :Q] + squares[:, Q:]
    swapped = jnp.concatenate([weighted[:, Q:], -weighted[:, :Q]], 1)
    rows = M
    width = classes_total * columns
    crossed_real = jnp.einsum(
        "mkc,mcb->mkb", grid_rows, weighted, preferred_element_type=jnp.float32
    ).astype(jnp.bfloat16).reshape(rows, width)
    crossed_imag = jnp.einsum(
        "mkc,mcb->mkb", grid_rows, swapped, preferred_element_type=jnp.float32
    ).astype(jnp.bfloat16).reshape(rows, width)
    penalty = jnp.dot(cycle_power, power_term, precision=lax.Precision.HIGHEST)
    bias = (class_prior[:, None] - 0.5 * penalty).reshape(1, width)
    table = jnp.transpose(score_table, (2, 0, 1)).reshape(R, 2 * M)
    turn = jnp.concatenate(
        [turn_table.reshape(2 * M, R), jnp.ones((1, R), jnp.bfloat16), jnp.zeros((15, R), jnp.bfloat16)], 0
    )

    block = CLS_STEP * columns
    steps = width // block
    table_spec = pl.BlockSpec((R, 2 * rows), lambda i: (0, 0))
    crossed_spec = pl.BlockSpec((rows, block), lambda i: (0, i))
    row_spec = pl.BlockSpec((1, block), lambda i: (0, i))
    log_norm = pl.pallas_call(
        functools.partial(norm_kernel, columns),
        grid=(steps,),
        in_specs=[table_spec, crossed_spec, crossed_spec, row_spec],
        out_specs=pl.BlockSpec((1, columns), lambda i: (0, 0)),
        out_shape=jax.ShapeDtypeStruct((1, columns), jnp.float32),
        scratch_shapes=[pltpu.VMEM((1, columns), jnp.float32)] * 2,
        compiler_params=pltpu.CompilerParams(dimension_semantics=("arbitrary",)),
    )(table, crossed_real, crossed_imag, bias)
    shift = bias - jnp.tile(log_norm, (1, classes_total))
    spectra_cos, spectra_sin, class_weight = pl.pallas_call(
        spectra_kernel,
        grid=(steps,),
        in_specs=[
            table_spec,
            crossed_spec,
            crossed_spec,
            row_spec,
            pl.BlockSpec(turn.shape, lambda i: (0, 0)),
        ],
        out_specs=[crossed_spec, crossed_spec, row_spec],
        out_shape=[
            jax.ShapeDtypeStruct((rows, width), jnp.bfloat16),
            jax.ShapeDtypeStruct((rows, width), jnp.bfloat16),
            jax.ShapeDtypeStruct((1, width), jnp.float32),
        ],
        compiler_params=pltpu.CompilerParams(dimension_semantics=("arbitrary",)),
    )(table, crossed_real, crossed_imag, shift, turn)

    spectra_cos = spectra_cos.reshape(M, classes_total, columns)
    spectra_sin = spectra_sin.reshape(M, classes_total, columns)
    numer_all = jnp.einsum(
        "mkb,mcb->kmc", spectra_cos, weighted, preferred_element_type=jnp.float32
    ) + jnp.einsum("mkb,mcb->kmc", spectra_sin, swapped, preferred_element_type=jnp.float32)
    numer_all = numer_all.reshape(classes_total, 2 * M * Q)
    class_weight = class_weight.reshape(classes_total, columns)
    cycles_all = jnp.dot(class_weight, power_term.T, precision=lax.Precision.HIGHEST)
    mass_all = jnp.sum(class_weight, axis=1)

    width = numer_all.shape[1]
    packed = jnp.concatenate(
        [numer_all, cycles_all, mass_all[:, None], jnp.zeros((classes_total, 95), jnp.float32)], 1
    )
    packed = packed.reshape(lax.axis_size("z"), lax.axis_size("y"), CLS_DEV, packed.shape[1])
    own = jnp.sum(lax.all_to_all(packed, "y", 1, 1, tiled=True), 1)
    own = jnp.sum(lax.all_to_all(own, "z", 0, 0, tiled=True), 0)
    own = jnp.sum(lax.all_gather(own, GRP, axis=0, tiled=False), 0)
    numerator = own[:, :width]
    cycle_sum = own[:, width : width + Q]
    class_mass = own[:, width + Q]
    new_references = (numerator.reshape(CLS_DEV, M, 2, Q) / cycle_sum[:, None, None, :]).reshape(
        CLS_DEV, 2 * M * Q
    )
    particle_total = columns * lax.axis_size(GRP) * lax.axis_size(DEV)
    occupancy = class_mass * (classes_total / particle_total)
    return (new_references, occupancy)


def solution(mesh):
    grp_count, dev_count = mesh.devices.shape
    core_count = 2
    y_count = 4
    split = jax.sharding.Mesh(
        mesh.devices.reshape(
            grp_count // core_count, core_count, dev_count // y_count, y_count
        ),
        GRP + DEV,
    )
    return jax.shard_map(
        local,
        mesh=split,
        in_specs=(P(DEV, None), P(None, GRP + DEV), P(GRP + DEV), P(), P(), P()),
        out_specs=(P(DEV, None), P(DEV)),
        check_vma=False,
    )
```

```python
import functools
import math

import jax
import jax.numpy as jnp
from jax import lax
from jax.experimental import pallas as pl
from jax.experimental.pallas import tpu as pltpu
from jax.sharding import PartitionSpec as P

Q = 32
M = 32
R = 128
CLS_DEV = 6
CLS_STEP = 24
GRP = ("x", "core")
DEV = ("z", "y")


def angle_tables(cycle_freqs, count_turns):
    freq_index = jnp.arange(cycle_freqs, dtype=jnp.int32)
    turn_index = jnp.arange(count_turns, dtype=jnp.int32)
    wrapped = freq_index[:, None] * turn_index[None, :] % count_turns
    phases = 2.0 * math.pi / count_turns * wrapped.astype(jnp.float32)
    factor = jnp.where(freq_index == 0, 1.0, 2.0).astype(jnp.float32)[:, None]
    cosine = jnp.cos(phases)
    sine_part = jnp.sin(phases)
    score_table = jnp.stack([factor * cosine, factor * sine_part], 0).astype(jnp.bfloat16)
    turn_table = jnp.stack([cosine, sine_part], 0).astype(jnp.bfloat16)
    return (score_table, turn_table)


def particle_terms(particles, defocus_bin, contrast_table, noise_power):
    columns = particles.shape[1]
    cycle_count = contrast_table.shape[1]
    freq_count = particles.shape[0] // (2 * cycle_count)
    onehot = (
        defocus_bin[None, :] == jnp.arange(contrast_table.shape[0], dtype=jnp.int32)[:, None]
    ).astype(jnp.float32)
    contrast = jnp.dot(contrast_table.T, onehot, precision=lax.Precision.HIGHEST)
    scaled = contrast / noise_power[:, None]
    power_term = contrast * scaled
    weighted = (
        particles.astype(jnp.float32).reshape(freq_count, 2, cycle_count, columns)
        * scaled[None, None]
    ).astype(jnp.bfloat16)
    return (weighted.reshape(freq_count, 2 * cycle_count, columns), power_term)


def class_scores(table_ref, real_ref, imag_ref, shift_ref, j):
    crossed = jnp.concatenate([real_ref[j], imag_ref[j]], 0)
    raw = jnp.dot(table_ref[...], crossed, preferred_element_type=jnp.float32)
    return raw + shift_ref[pl.ds(j, 1), :]


def norm_kernel(table_ref, real_ref, imag_ref, bias_ref, out_ref, top_ref, total_ref):
    step = pl.program_id(0)

    @pl.when(step == 0)
    def _():
        top_ref[...] = jnp.full(top_ref.shape, -1e30, jnp.float32)
        total_ref[...] = jnp.zeros(total_ref.shape, jnp.float32)

    parts = [class_scores(table_ref, real_ref, imag_ref, bias_ref, j) for j in range(real_ref.shape[0])]
    block_top = functools.reduce(jnp.maximum, [jnp.max(s, axis=0, keepdims=True) for s in parts])
    old_top = top_ref[...]
    new_top = jnp.maximum(old_top, block_top)
    block_total = functools.reduce(
        jnp.add, [jnp.sum(jnp.exp(s - new_top), axis=0, keepdims=True) for s in parts]
    )
    total_ref[...] = total_ref[...] * jnp.exp(old_top - new_top) + block_total
    top_ref[...] = new_top

    @pl.when(step == pl.num_programs(0) - 1)
    def _():
        out_ref[...] = top_ref[...] + jnp.log(total_ref[...])


def spectra_kernel(
    table_ref, real_ref, imag_ref, shift_ref, turn_ref, cos_ref, sin_ref, weight_ref
):
    rows = cos_ref.shape[1]
    for j in range(real_ref.shape[0]):
        responsibility = jnp.exp(class_scores(table_ref, real_ref, imag_ref, shift_ref, j))
        full = jnp.dot(
            turn_ref[...], responsibility.astype(jnp.bfloat16), preferred_element_type=jnp.float32
        )
        cos_ref[j] = full[:rows].astype(jnp.bfloat16)
        sin_ref[j] = full[rows : 2 * rows].astype(jnp.bfloat16)
        weight_ref[pl.ds(j, 1), :] = full[2 * rows : 2 * rows + 1]


def local(references, particles, defocus_bin, contrast_table, noise_power, class_prior):
    weighted, power_term = particle_terms(particles, defocus_bin, contrast_table, noise_power)
    score_table, turn_table = angle_tables(M, R)
    columns = particles.shape[1]
    dev_count = lax.axis_size(DEV)
    classes_total = CLS_DEV * dev_count

    copies = jnp.broadcast_to(references[None], (dev_count,) + references.shape)
    gathered = lax.all_to_all(copies, DEV, 0, 0, tiled=True)
    class_grid = gathered.reshape(classes_total, M, 2 * Q)
    factor = jnp.where(jnp.arange(M) == 0, 1.0, 2.0).astype(jnp.float32)
    squares = jnp.sum(class_grid.astype(jnp.float32) ** 2 * factor[None, :, None], axis=1)
    cycle_power = squares[:, :Q] + squares[:, Q:]
    swapped = jnp.concatenate([weighted[:, Q:], -weighted[:, :Q]], 1)
    rows = M
    crossed_real = jnp.einsum(
        "kmc,mcb->kmb", class_grid, weighted, preferred_element_type=jnp.float32
    ).astype(jnp.bfloat16)
    crossed_imag = jnp.einsum(
        "kmc,mcb->kmb", class_grid, swapped, preferred_element_type=jnp.float32
    ).astype(jnp.bfloat16)
    penalty = jnp.dot(cycle_power, power_term, precision=lax.Precision.HIGHEST)
    bias = class_prior[:, None] - 0.5 * penalty
    table = jnp.transpose(score_table, (2, 0, 1)).reshape(R, 2 * M)
    turn = jnp.concatenate(
        [turn_table.reshape(2 * M, R), jnp.ones((1, R), jnp.bfloat16), jnp.zeros((15, R), jnp.bfloat16)], 0
    )

    steps = classes_total // CLS_STEP
    table_spec = pl.BlockSpec((R, 2 * rows), lambda i: (0, 0))
    crossed_spec = pl.BlockSpec((CLS_STEP, rows, columns), lambda i: (i, 0, 0))
    row_spec = pl.BlockSpec((CLS_STEP, columns), lambda i: (i, 0))
    log_norm = pl.pallas_call(
        norm_kernel,
        grid=(steps,),
        in_specs=[table_spec, crossed_spec, crossed_spec, row_spec],
        out_specs=pl.BlockSpec((1, columns), lambda i: (0, 0)),
        out_shape=jax.ShapeDtypeStruct((1, columns), jnp.float32),
        scratch_shapes=[pltpu.VMEM((1, columns), jnp.float32)] * 2,
        compiler_params=pltpu.CompilerParams(dimension_semantics=("arbitrary",)),
    )(table, crossed_real, crossed_imag, bias)
    shift = bias - log_norm
    spectra_cos, spectra_sin, class_weight = pl.pallas_call(
        spectra_kernel,
        grid=(steps,),
        in_specs=[
            table_spec,
            crossed_spec,
            crossed_spec,
            row_spec,
            pl.BlockSpec(turn.shape, lambda i: (0, 0)),
        ],
        out_specs=[crossed_spec, crossed_spec, row_spec],
        out_shape=[
            jax.ShapeDtypeStruct((classes_total, rows, columns), jnp.bfloat16),
            jax.ShapeDtypeStruct((classes_total, rows, columns), jnp.bfloat16),
            jax.ShapeDtypeStruct((classes_total, columns), jnp.float32),
        ],
        compiler_params=pltpu.CompilerParams(dimension_semantics=("arbitrary",)),
    )(table, crossed_real, crossed_imag, shift, turn)

    numer_all = jnp.einsum(
        "kmb,mcb->kmc", spectra_cos, weighted, preferred_element_type=jnp.float32
    ) + jnp.einsum("kmb,mcb->kmc", spectra_sin, swapped, preferred_element_type=jnp.float32)
    numer_all = numer_all.reshape(classes_total, 2 * M * Q)
    class_weight = class_weight.reshape(classes_total, columns)
    cycles_all = jnp.dot(class_weight, power_term.T, precision=lax.Precision.HIGHEST)
    mass_all = jnp.sum(class_weight, axis=1)

    width = numer_all.shape[1]
    packed = jnp.concatenate(
        [numer_all, cycles_all, mass_all[:, None], jnp.zeros((classes_total, 95), jnp.float32)], 1
    )
    packed = packed.reshape(lax.axis_size("z"), lax.axis_size("y"), CLS_DEV, packed.shape[1])
    own = jnp.sum(lax.all_to_all(packed, "y", 1, 1, tiled=True), 1)
    own = jnp.sum(lax.all_to_all(own, "z", 0, 0, tiled=True), 0)
    own = jnp.sum(lax.all_gather(own, GRP, axis=0, tiled=False), 0)
    numerator = own[:, :width]
    cycle_sum = own[:, width : width + Q]
    class_mass = own[:, width + Q]
    new_references = (numerator.reshape(CLS_DEV, M, 2, Q) / cycle_sum[:, None, None, :]).reshape(
        CLS_DEV, 2 * M * Q
    )
    particle_total = columns * lax.axis_size(GRP) * lax.axis_size(DEV)
    occupancy = class_mass * (classes_total / particle_total)
    return (new_references, occupancy)


def solution(mesh):
    grp_count, dev_count = mesh.devices.shape
    core_count = 2
    y_count = 4
    split = jax.sharding.Mesh(
        mesh.devices.reshape(
            grp_count // core_count, core_count, dev_count // y_count, y_count
        ),
        GRP + DEV,
    )
    return jax.shard_map(
        local,
        mesh=split,
        in_specs=(P(DEV, None), P(None, GRP + DEV), P(GRP + DEV), P(), P(), P()),
        out_specs=(P(DEV, None), P(DEV)),
        check_vma=False,
    )
```

```python
import functools
import math

import jax
import jax.numpy as jnp
from jax import lax
from jax.experimental import pallas as pl
from jax.experimental.pallas import tpu as pltpu
from jax.sharding import PartitionSpec as P

Q = 32
M = 32
R = 128
CLS_DEV = 6
CLS_STEP = 24
GRP = ("x", "core")
DEV = ("z", "y")


def angle_tables(cycle_freqs, count_turns):
    freq_index = jnp.arange(cycle_freqs, dtype=jnp.int32)
    turn_index = jnp.arange(count_turns, dtype=jnp.int32)
    wrapped = freq_index[:, None] * turn_index[None, :] % count_turns
    phases = 2.0 * math.pi / count_turns * wrapped.astype(jnp.float32)
    factor = jnp.where(freq_index == 0, 1.0, 2.0).astype(jnp.float32)[:, None]
    cosine = jnp.cos(phases)
    sine_part = jnp.sin(phases)
    score_table = jnp.stack([factor * cosine, factor * sine_part], 0).astype(jnp.bfloat16)
    turn_table = jnp.stack([cosine, sine_part], 0).astype(jnp.bfloat16)
    return (score_table, turn_table)


def particle_terms(particles, defocus_bin, contrast_table, noise_power):
    columns = particles.shape[1]
    cycle_count = contrast_table.shape[1]
    freq_count = particles.shape[0] // (2 * cycle_count)
    onehot = (
        defocus_bin[None, :] == jnp.arange(contrast_table.shape[0], dtype=jnp.int32)[:, None]
    ).astype(jnp.float32)
    contrast = jnp.dot(contrast_table.T, onehot, precision=lax.Precision.HIGHEST)
    scaled = contrast / noise_power[:, None]
    power_term = contrast * scaled
    weighted = (
        particles.astype(jnp.float32).reshape(freq_count, 2, cycle_count, columns)
        * scaled[None, None]
    ).astype(jnp.bfloat16)
    return (weighted.reshape(freq_count, 2 * cycle_count, columns), power_term)


def block_scores(table_ref, real_ref, imag_ref, shift_ref):
    classes = real_ref.shape[0]
    crossed = jnp.concatenate(
        [jnp.concatenate([real_ref[j], imag_ref[j]], 0) for j in range(classes)], 1
    )
    raw = jnp.dot(table_ref[...], crossed, preferred_element_type=jnp.float32)
    shift = jnp.concatenate([shift_ref[pl.ds(j, 1), :] for j in range(classes)], 1)
    return raw + shift


def norm_kernel(cols, table_ref, real_ref, imag_ref, bias_ref, out_ref, top_ref, total_ref):
    step = pl.program_id(0)

    @pl.when(step == 0)
    def _():
        top_ref[...] = jnp.full(top_ref.shape, -1e30, jnp.float32)
        total_ref[...] = jnp.zeros(total_ref.shape, jnp.float32)

    scores = block_scores(table_ref, real_ref, imag_ref, bias_ref)
    parts = [scores[:, j * cols : (j + 1) * cols] for j in range(scores.shape[1] // cols)]
    block_top = functools.reduce(jnp.maximum, [jnp.max(s, axis=0, keepdims=True) for s in parts])
    old_top = top_ref[...]
    new_top = jnp.maximum(old_top, block_top)
    block_total = functools.reduce(
        jnp.add, [jnp.sum(jnp.exp(s - new_top), axis=0, keepdims=True) for s in parts]
    )
    total_ref[...] = total_ref[...] * jnp.exp(old_top - new_top) + block_total
    top_ref[...] = new_top

    @pl.when(step == pl.num_programs(0) - 1)
    def _():
        out_ref[...] = top_ref[...] + jnp.log(total_ref[...])


def spectra_kernel(
    cols, table_ref, real_ref, imag_ref, shift_ref, turn_ref, cos_ref, sin_ref, weight_ref
):
    responsibility = jnp.exp(block_scores(table_ref, real_ref, imag_ref, shift_ref))
    full = jnp.dot(
        turn_ref[...], responsibility.astype(jnp.bfloat16), preferred_element_type=jnp.float32
    )
    rows = cos_ref.shape[1]
    for j in range(cos_ref.shape[0]):
        part = full[:, j * cols : (j + 1) * cols]
        cos_ref[j] = part[:rows].astype(jnp.bfloat16)
        sin_ref[j] = part[rows : 2 * rows].astype(jnp.bfloat16)
        weight_ref[pl.ds(j, 1), :] = part[2 * rows : 2 * rows + 1]


def local(references, particles, defocus_bin, contrast_table, noise_power, class_prior):
    weighted, power_term = particle_terms(particles, defocus_bin, contrast_table, noise_power)
    score_table, turn_table = angle_tables(M, R)
    columns = particles.shape[1]
    dev_count = lax.axis_size(DEV)
    classes_total = CLS_DEV * dev_count

    copies = jnp.broadcast_to(references[None], (dev_count,) + references.shape)
    gathered = lax.all_to_all(copies, DEV, 0, 0, tiled=True)
    class_grid = gathered.reshape(classes_total, M, 2 * Q)
    factor = jnp.where(jnp.arange(M) == 0, 1.0, 2.0).astype(jnp.float32)
    squares = jnp.sum(class_grid.astype(jnp.float32) ** 2 * factor[None, :, None], axis=1)
    cycle_power = squares[:, :Q] + squares[:, Q:]
    swapped = jnp.concatenate([weighted[:, Q:], -weighted[:, :Q]], 1)
    rows = M
    crossed_real = jnp.einsum(
        "kmc,mcb->kmb", class_grid, weighted, preferred_element_type=jnp.float32
    ).astype(jnp.bfloat16)
    crossed_imag = jnp.einsum(
        "kmc,mcb->kmb", class_grid, swapped, preferred_element_type=jnp.float32
    ).astype(jnp.bfloat16)
    penalty = jnp.dot(cycle_power, power_term, precision=lax.Precision.HIGHEST)
    bias = class_prior[:, None] - 0.5 * penalty
    table = jnp.transpose(score_table, (2, 0, 1)).reshape(R, 2 * M)
    turn = jnp.concatenate(
        [turn_table.reshape(2 * M, R), jnp.ones((1, R), jnp.bfloat16), jnp.zeros((15, R), jnp.bfloat16)], 0
    )

    steps = classes_total // CLS_STEP
    table_spec = pl.BlockSpec((R, 2 * rows), lambda i: (0, 0))
    crossed_spec = pl.BlockSpec((CLS_STEP, rows, columns), lambda i: (i, 0, 0))
    row_spec = pl.BlockSpec((CLS_STEP, columns), lambda i: (i, 0))
    log_norm = pl.pallas_call(
        functools.partial(norm_kernel, columns),
        grid=(steps,),
        in_specs=[table_spec, crossed_spec, crossed_spec, row_spec],
        out_specs=pl.BlockSpec((1, columns), lambda i: (0, 0)),
        out_shape=jax.ShapeDtypeStruct((1, columns), jnp.float32),
        scratch_shapes=[pltpu.VMEM((1, columns), jnp.float32)] * 2,
        compiler_params=pltpu.CompilerParams(dimension_semantics=("arbitrary",)),
    )(table, crossed_real, crossed_imag, bias)
    shift = bias - log_norm
    spectra_cos, spectra_sin, class_weight = pl.pallas_call(
        functools.partial(spectra_kernel, columns),
        grid=(steps,),
        in_specs=[
            table_spec,
            crossed_spec,
            crossed_spec,
            row_spec,
            pl.BlockSpec(turn.shape, lambda i: (0, 0)),
        ],
        out_specs=[crossed_spec, crossed_spec, row_spec],
        out_shape=[
            jax.ShapeDtypeStruct((classes_total, rows, columns), jnp.bfloat16),
            jax.ShapeDtypeStruct((classes_total, rows, columns), jnp.bfloat16),
            jax.ShapeDtypeStruct((classes_total, columns), jnp.float32),
        ],
        compiler_params=pltpu.CompilerParams(dimension_semantics=("arbitrary",)),
    )(table, crossed_real, crossed_imag, shift, turn)

    numer_all = jnp.einsum(
        "kmb,mcb->kmc", spectra_cos, weighted, preferred_element_type=jnp.float32
    ) + jnp.einsum("kmb,mcb->kmc", spectra_sin, swapped, preferred_element_type=jnp.float32)
    numer_all = numer_all.reshape(classes_total, 2 * M * Q)
    class_weight = class_weight.reshape(classes_total, columns)
    cycles_all = jnp.dot(class_weight, power_term.T, precision=lax.Precision.HIGHEST)
    mass_all = jnp.sum(class_weight, axis=1)

    width = numer_all.shape[1]
    packed = jnp.concatenate(
        [numer_all, cycles_all, mass_all[:, None], jnp.zeros((classes_total, 95), jnp.float32)], 1
    )
    packed = packed.reshape(lax.axis_size("z"), lax.axis_size("y"), CLS_DEV, packed.shape[1])
    own = jnp.sum(lax.all_to_all(packed, "y", 1, 1, tiled=True), 1)
    own = jnp.sum(lax.all_to_all(own, "z", 0, 0, tiled=True), 0)
    own = jnp.sum(lax.all_gather(own, GRP, axis=0, tiled=False), 0)
    numerator = own[:, :width]
    cycle_sum = own[:, width : width + Q]
    class_mass = own[:, width + Q]
    new_references = (numerator.reshape(CLS_DEV, M, 2, Q) / cycle_sum[:, None, None, :]).reshape(
        CLS_DEV, 2 * M * Q
    )
    particle_total = columns * lax.axis_size(GRP) * lax.axis_size(DEV)
    occupancy = class_mass * (classes_total / particle_total)
    return (new_references, occupancy)


def solution(mesh):
    grp_count, dev_count = mesh.devices.shape
    core_count = 2
    y_count = 4
    split = jax.sharding.Mesh(
        mesh.devices.reshape(
            grp_count // core_count, core_count, dev_count // y_count, y_count
        ),
        GRP + DEV,
    )
    return jax.shard_map(
        local,
        mesh=split,
        in_specs=(P(DEV, None), P(None, GRP + DEV), P(GRP + DEV), P(), P(), P()),
        out_specs=(P(DEV, None), P(DEV)),
        check_vma=False,
    )
```

```python
import functools
import math

import jax
import jax.numpy as jnp
from jax import lax
from jax.experimental import pallas as pl
from jax.experimental.pallas import tpu as pltpu
from jax.sharding import PartitionSpec as P

Q = 32
M = 32
R = 128
CLS_DEV = 6
CLS_STEP = 48
GRP = ("x", "core")
DEV = ("z", "y")


def angle_tables(cycle_freqs, count_turns):
    freq_index = jnp.arange(cycle_freqs, dtype=jnp.int32)
    turn_index = jnp.arange(count_turns, dtype=jnp.int32)
    wrapped = freq_index[:, None] * turn_index[None, :] % count_turns
    phases = 2.0 * math.pi / count_turns * wrapped.astype(jnp.float32)
    factor = jnp.where(freq_index == 0, 1.0, 2.0).astype(jnp.float32)[:, None]
    cosine = jnp.cos(phases)
    sine_part = jnp.sin(phases)
    score_table = jnp.stack([factor * cosine, factor * sine_part], 0).astype(jnp.bfloat16)
    turn_table = jnp.stack([cosine, sine_part], 0).astype(jnp.bfloat16)
    return (score_table, turn_table)


def particle_terms(particles, defocus_bin, contrast_table, noise_power):
    columns = particles.shape[1]
    cycle_count = contrast_table.shape[1]
    freq_count = particles.shape[0] // (2 * cycle_count)
    onehot = (
        defocus_bin[None, :] == jnp.arange(contrast_table.shape[0], dtype=jnp.int32)[:, None]
    ).astype(jnp.float32)
    contrast = jnp.dot(contrast_table.T, onehot, precision=lax.Precision.HIGHEST)
    scaled = contrast / noise_power[:, None]
    power_term = contrast * scaled
    weighted = (
        particles.astype(jnp.float32).reshape(freq_count, 2, cycle_count, columns)
        * scaled[None, None]
    ).astype(jnp.bfloat16)
    return (weighted.reshape(freq_count, 2 * cycle_count, columns), power_term)


def block_scores(table_ref, real_ref, imag_ref, shift_ref):
    crossed = jnp.concatenate([real_ref[...], imag_ref[...]], 0)
    raw = jnp.dot(table_ref[...], crossed, preferred_element_type=jnp.float32)
    return raw + shift_ref[...]


def norm_kernel(cols, table_ref, real_ref, imag_ref, bias_ref, out_ref, top_ref, total_ref):
    step = pl.program_id(0)

    @pl.when(step == 0)
    def _():
        top_ref[...] = jnp.full(top_ref.shape, -1e30, jnp.float32)
        total_ref[...] = jnp.zeros(total_ref.shape, jnp.float32)

    scores = block_scores(table_ref, real_ref, imag_ref, bias_ref)
    parts = [scores[:, j * cols : (j + 1) * cols] for j in range(scores.shape[1] // cols)]
    block_top = functools.reduce(jnp.maximum, [jnp.max(s, axis=0, keepdims=True) for s in parts])
    old_top = top_ref[...]
    new_top = jnp.maximum(old_top, block_top)
    block_total = functools.reduce(
        jnp.add, [jnp.sum(jnp.exp(s - new_top), axis=0, keepdims=True) for s in parts]
    )
    total_ref[...] = total_ref[...] * jnp.exp(old_top - new_top) + block_total
    top_ref[...] = new_top

    @pl.when(step == pl.num_programs(0) - 1)
    def _():
        out_ref[...] = top_ref[...] + jnp.log(total_ref[...])


def spectra_kernel(
    cols, table_ref, real_ref, imag_ref, bias_ref, norm_ref, turn_ref, cos_ref, sin_ref, weight_ref
):
    norm_row = jnp.concatenate([norm_ref[...]] * (bias_ref.shape[1] // cols), 1)
    scores = block_scores(table_ref, real_ref, imag_ref, bias_ref)
    responsibility = jnp.exp(scores - norm_row)
    full = jnp.dot(
        turn_ref[...], responsibility.astype(jnp.bfloat16), preferred_element_type=jnp.float32
    )
    rows = cos_ref.shape[0]
    cos_ref[...] = full[:rows].astype(jnp.bfloat16)
    sin_ref[...] = full[rows : 2 * rows].astype(jnp.bfloat16)
    weight_ref[...] = full[2 * rows : 2 * rows + 1]


def local(references, particles, defocus_bin, contrast_table, noise_power, class_prior):
    weighted, power_term = particle_terms(particles, defocus_bin, contrast_table, noise_power)
    score_table, turn_table = angle_tables(M, R)
    columns = particles.shape[1]
    dev_count = lax.axis_size(DEV)
    classes_total = CLS_DEV * dev_count

    own_rows = jnp.transpose(references.reshape(CLS_DEV, M, 2 * Q), (1, 0, 2))
    copies = jnp.broadcast_to(own_rows[None], (dev_count,) + own_rows.shape)
    gathered = lax.all_to_all(copies, DEV, 0, 0, tiled=True)
    grid_rows = jnp.transpose(gathered, (1, 0, 2, 3)).reshape(M, classes_total, 2 * Q)
    factor = jnp.where(jnp.arange(M) == 0, 1.0, 2.0).astype(jnp.float32)
    squares = jnp.sum(grid_rows.astype(jnp.float32) ** 2 * factor[:, None, None], axis=0)
    cycle_power = squares[:, :Q] + squares[:, Q:]
    swapped = jnp.concatenate([weighted[:, Q:], -weighted[:, :Q]], 1)
    rows = M
    width = classes_total * columns
    crossed_real = jnp.einsum(
        "mkc,mcb->mkb", grid_rows, weighted, preferred_element_type=jnp.float32
    ).astype(jnp.bfloat16).reshape(rows, width)
    crossed_imag = jnp.einsum(
        "mkc,mcb->mkb", grid_rows, swapped, preferred_element_type=jnp.float32
    ).astype(jnp.bfloat16).reshape(rows, width)
    penalty = jnp.dot(cycle_power, power_term, precision=lax.Precision.HIGHEST)
    bias = (class_prior[:, None] - 0.5 * penalty).reshape(1, width)
    table = jnp.transpose(score_table, (2, 0, 1)).reshape(R, 2 * M)
    turn = jnp.concatenate(
        [turn_table.reshape(2 * M, R), jnp.ones((1, R), jnp.bfloat16), jnp.zeros((15, R), jnp.bfloat16)], 0
    )

    block = CLS_STEP * columns
    steps = width // block
    table_spec = pl.BlockSpec((R, 2 * rows), lambda i: (0, 0))
    crossed_spec = pl.BlockSpec((rows, block), lambda i: (0, i))
    row_spec = pl.BlockSpec((1, block), lambda i: (0, i))
    log_norm = pl.pallas_call(
        functools.partial(norm_kernel, columns),
        grid=(steps,),
        in_specs=[table_spec, crossed_spec, crossed_spec, row_spec],
        out_specs=pl.BlockSpec((1, columns), lambda i: (0, 0)),
        out_shape=jax.ShapeDtypeStruct((1, columns), jnp.float32),
        scratch_shapes=[pltpu.VMEM((1, columns), jnp.float32)] * 2,
        compiler_params=pltpu.CompilerParams(dimension_semantics=("arbitrary",)),
    )(table, crossed_real, crossed_imag, bias)
    spectra_cos, spectra_sin, class_weight = pl.pallas_call(
        functools.partial(spectra_kernel, columns),
        grid=(steps,),
        in_specs=[
            table_spec,
            crossed_spec,
            crossed_spec,
            row_spec,
            pl.BlockSpec((1, columns), lambda i: (0, 0)),
            pl.BlockSpec(turn.shape, lambda i: (0, 0)),
        ],
        out_specs=[crossed_spec, crossed_spec, row_spec],
        out_shape=[
            jax.ShapeDtypeStruct((rows, width), jnp.bfloat16),
            jax.ShapeDtypeStruct((rows, width), jnp.bfloat16),
            jax.ShapeDtypeStruct((1, width), jnp.float32),
        ],
        compiler_params=pltpu.CompilerParams(dimension_semantics=("arbitrary",)),
    )(table, crossed_real, crossed_imag, bias, log_norm, turn)

    spectra_cos = spectra_cos.reshape(M, classes_total, columns)
    spectra_sin = spectra_sin.reshape(M, classes_total, columns)
    numer_all = jnp.einsum(
        "mkb,mcb->kmc", spectra_cos, weighted, preferred_element_type=jnp.float32
    ) + jnp.einsum("mkb,mcb->kmc", spectra_sin, swapped, preferred_element_type=jnp.float32)
    numer_all = numer_all.reshape(classes_total, 2 * M * Q)
    class_weight = class_weight.reshape(classes_total, columns)
    cycles_all = jnp.dot(class_weight, power_term.T, precision=lax.Precision.HIGHEST)
    mass_all = jnp.sum(class_weight, axis=1)

    width = numer_all.shape[1]
    packed = jnp.concatenate(
        [numer_all, cycles_all, mass_all[:, None], jnp.zeros((classes_total, 95), jnp.float32)], 1
    )
    packed = packed.reshape(lax.axis_size("z"), lax.axis_size("y"), CLS_DEV, packed.shape[1])
    own = jnp.sum(lax.all_to_all(packed, "y", 1, 1, tiled=True), 1)
    own = jnp.sum(lax.all_to_all(own, "z", 0, 0, tiled=True), 0)
    own = jnp.sum(lax.all_gather(own, GRP, axis=0, tiled=False), 0)
    numerator = own[:, :width]
    cycle_sum = own[:, width : width + Q]
    class_mass = own[:, width + Q]
    new_references = (numerator.reshape(CLS_DEV, M, 2, Q) / cycle_sum[:, None, None, :]).reshape(
        CLS_DEV, 2 * M * Q
    )
    particle_total = columns * lax.axis_size(GRP) * lax.axis_size(DEV)
    occupancy = class_mass * (classes_total / particle_total)
    return (new_references, occupancy)


def solution(mesh):
    grp_count, dev_count = mesh.devices.shape
    core_count = 2
    y_count = 4
    split = jax.sharding.Mesh(
        mesh.devices.reshape(
            grp_count // core_count, core_count, dev_count // y_count, y_count
        ),
        GRP + DEV,
    )
    return jax.shard_map(
        local,
        mesh=split,
        in_specs=(P(DEV, None), P(None, GRP + DEV), P(GRP + DEV), P(), P(), P()),
        out_specs=(P(DEV, None), P(DEV)),
        check_vma=False,
    )
```

```python
import functools
import math

import jax
import jax.numpy as jnp
from jax import lax
from jax.experimental import pallas as pl
from jax.experimental.pallas import tpu as pltpu
from jax.sharding import PartitionSpec as P

Q = 32
M = 32
R = 128
CLS_DEV = 6
CLS_STEP = 48
GRP = ("x", "core")
DEV = ("z", "y")


def angle_tables(cycle_freqs, count_turns):
    freq_index = jnp.arange(cycle_freqs, dtype=jnp.int32)
    turn_index = jnp.arange(count_turns, dtype=jnp.int32)
    wrapped = freq_index[:, None] * turn_index[None, :] % count_turns
    phases = 2.0 * math.pi / count_turns * wrapped.astype(jnp.float32)
    factor = jnp.where(freq_index == 0, 1.0, 2.0).astype(jnp.float32)[:, None]
    cosine = jnp.cos(phases)
    sine_part = jnp.sin(phases)
    score_table = jnp.stack([factor * cosine, factor * sine_part], 0).astype(jnp.bfloat16)
    turn_table = jnp.stack([cosine, sine_part], 0).astype(jnp.bfloat16)
    return (score_table, turn_table)


def particle_terms(particles, defocus_bin, contrast_table, noise_power):
    columns = particles.shape[1]
    cycle_count = contrast_table.shape[1]
    freq_count = particles.shape[0] // (2 * cycle_count)
    onehot = (
        defocus_bin[None, :] == jnp.arange(contrast_table.shape[0], dtype=jnp.int32)[:, None]
    ).astype(jnp.float32)
    contrast = jnp.dot(contrast_table.T, onehot, precision=lax.Precision.HIGHEST)
    scaled = contrast / noise_power[:, None]
    power_term = contrast * scaled
    weighted = (
        particles.astype(jnp.float32).reshape(freq_count, 2, cycle_count, columns)
        * scaled[None, None]
    ).astype(jnp.bfloat16)
    return (weighted.reshape(freq_count, 2 * cycle_count, columns), power_term)


def block_scores(table_ref, real_ref, imag_ref, shift_ref):
    crossed = jnp.concatenate([real_ref[...], imag_ref[...]], 0)
    raw = jnp.dot(table_ref[...], crossed, preferred_element_type=jnp.float32)
    return raw + shift_ref[...]


def norm_kernel(cols, table_ref, real_ref, imag_ref, bias_ref, out_ref, top_ref, total_ref):
    step = pl.program_id(0)

    @pl.when(step == 0)
    def _():
        top_ref[...] = jnp.full(top_ref.shape, -1e30, jnp.float32)
        total_ref[...] = jnp.zeros(total_ref.shape, jnp.float32)

    scores = block_scores(table_ref, real_ref, imag_ref, bias_ref)
    parts = [scores[:, j * cols : (j + 1) * cols] for j in range(scores.shape[1] // cols)]
    block_top = functools.reduce(jnp.maximum, [jnp.max(s, axis=0, keepdims=True) for s in parts])
    old_top = top_ref[...]
    new_top = jnp.maximum(old_top, block_top)
    block_total = functools.reduce(
        jnp.add, [jnp.sum(jnp.exp(s - new_top), axis=0, keepdims=True) for s in parts]
    )
    total_ref[...] = total_ref[...] * jnp.exp(old_top - new_top) + block_total
    top_ref[...] = new_top

    @pl.when(step == pl.num_programs(0) - 1)
    def _():
        out_ref[...] = top_ref[...] + jnp.log(total_ref[...])


def spectra_kernel(
    cols, table_ref, real_ref, imag_ref, bias_ref, norm_ref, turn_ref, cos_ref, sin_ref, weight_ref
):
    norm_row = jnp.concatenate([norm_ref[...]] * (bias_ref.shape[1] // cols), 1)
    scores = block_scores(table_ref, real_ref, imag_ref, bias_ref)
    responsibility = jnp.exp(scores - norm_row)
    full = jnp.dot(
        turn_ref[...], responsibility.astype(jnp.bfloat16), preferred_element_type=jnp.float32
    )
    rows = cos_ref.shape[0]
    cos_ref[...] = full[:rows].astype(jnp.bfloat16)
    sin_ref[...] = full[rows : 2 * rows].astype(jnp.bfloat16)
    weight_ref[...] = full[2 * rows : 2 * rows + 1]


def local(references, particles, defocus_bin, contrast_table, noise_power, class_prior):
    weighted, power_term = particle_terms(particles, defocus_bin, contrast_table, noise_power)
    score_table, turn_table = angle_tables(M, R)
    columns = particles.shape[1]
    dev_count = lax.axis_size(DEV)
    classes_total = CLS_DEV * dev_count

    own_rows = jnp.transpose(references.reshape(CLS_DEV, M, 2 * Q), (1, 0, 2))
    copies = jnp.broadcast_to(own_rows[None], (dev_count,) + own_rows.shape)
    gathered = lax.all_to_all(copies, DEV, 0, 0, tiled=True)
    grid_rows = jnp.transpose(gathered, (1, 0, 2, 3)).reshape(M, classes_total, 2 * Q)
    factor = jnp.where(jnp.arange(M) == 0, 1.0, 2.0).astype(jnp.float32)
    squares = jnp.sum(grid_rows.astype(jnp.float32) ** 2 * factor[:, None, None], axis=0)
    cycle_power = squares[:, :Q] + squares[:, Q:]
    swapped = jnp.concatenate([weighted[:, Q:], -weighted[:, :Q]], 1)
    rows = M
    width = classes_total * columns
    crossed_real = jnp.einsum(
        "mkc,mcb->mkb", grid_rows, weighted, preferred_element_type=jnp.float32
    ).astype(jnp.bfloat16).reshape(rows, width)
    crossed_imag = jnp.einsum(
        "mkc,mcb->mkb", grid_rows, swapped, preferred_element_type=jnp.float32
    ).astype(jnp.bfloat16).reshape(rows, width)
    penalty = jnp.dot(cycle_power, power_term, precision=lax.Precision.HIGHEST)
    bias = (class_prior[:, None] - 0.5 * penalty).reshape(1, width)
    table = jnp.transpose(score_table, (2, 0, 1)).reshape(R, 2 * M)
    turn = jnp.concatenate(
        [turn_table.reshape(2 * M, R), jnp.ones((1, R), jnp.bfloat16), jnp.zeros((15, R), jnp.bfloat16)], 0
    )

    block = CLS_STEP * columns
    steps = width // block
    table_spec = pl.BlockSpec((R, 2 * rows), lambda i: (0, 0))
    crossed_spec = pl.BlockSpec((rows, block), lambda i: (0, i))
    row_spec = pl.BlockSpec((1, block), lambda i: (0, i))
    log_norm = pl.pallas_call(
        functools.partial(norm_kernel, columns),
        grid=(steps,),
        in_specs=[table_spec, crossed_spec, crossed_spec, row_spec],
        out_specs=pl.BlockSpec((1, columns), lambda i: (0, 0)),
        out_shape=jax.ShapeDtypeStruct((1, columns), jnp.float32),
        scratch_shapes=[pltpu.VMEM((1, columns), jnp.float32)] * 2,
        compiler_params=pltpu.CompilerParams(dimension_semantics=("arbitrary",)),
    )(table, crossed_real, crossed_imag, bias)
    spectra_cos, spectra_sin, class_weight = pl.pallas_call(
        functools.partial(spectra_kernel, columns),
        grid=(steps,),
        in_specs=[
            table_spec,
            crossed_spec,
            crossed_spec,
            row_spec,
            pl.BlockSpec((1, columns), lambda i: (0, 0)),
            pl.BlockSpec(turn.shape, lambda i: (0, 0)),
        ],
        out_specs=[crossed_spec, crossed_spec, row_spec],
        out_shape=[
            jax.ShapeDtypeStruct((rows, width), jnp.bfloat16),
            jax.ShapeDtypeStruct((rows, width), jnp.bfloat16),
            jax.ShapeDtypeStruct((1, width), jnp.float32),
        ],
        compiler_params=pltpu.CompilerParams(dimension_semantics=("arbitrary",)),
    )(table, crossed_real, crossed_imag, bias, log_norm, turn)

    spectra_cos = spectra_cos.reshape(M, classes_total, columns)
    spectra_sin = spectra_sin.reshape(M, classes_total, columns)
    numer_all = jnp.einsum(
        "mkb,mcb->kmc", spectra_cos, weighted, preferred_element_type=jnp.float32
    ) + jnp.einsum("mkb,mcb->kmc", spectra_sin, swapped, preferred_element_type=jnp.float32)
    numer_all = numer_all.reshape(classes_total, 2 * M * Q)
    class_weight = class_weight.reshape(classes_total, columns)
    cycles_all = jnp.dot(class_weight, power_term.T, precision=lax.Precision.HIGHEST)
    mass_all = jnp.sum(class_weight, axis=1)

    width = numer_all.shape[1]
    packed = jnp.concatenate(
        [numer_all, cycles_all, mass_all[:, None], jnp.zeros((classes_total, 223), jnp.float32)], 1
    )
    core = lax.axis_index("core")
    core_count = lax.axis_size("core")
    half = packed.shape[1] // core_count
    mine = lax.dynamic_slice_in_dim(packed, core * half, half, 1)
    other = lax.dynamic_slice_in_dim(packed, (1 - core) * half, half, 1)
    packed = mine + lax.ppermute(other, "core", [(0, 1), (1, 0)])
    packed = packed.reshape(lax.axis_size("z"), lax.axis_size("y"), CLS_DEV, half)
    own = jnp.sum(lax.all_to_all(packed, "y", 1, 1, tiled=True), 1)
    own = jnp.sum(lax.all_to_all(own, "z", 0, 0, tiled=True), 0)
    own = lax.all_gather(own, GRP, axis=0, tiled=False)
    own = jnp.sum(own.reshape(lax.axis_size("x"), core_count, CLS_DEV, half), 0)
    own = jnp.concatenate([own[0], own[1]], 1)
    numerator = own[:, :width]
    cycle_sum = own[:, width : width + Q]
    class_mass = own[:, width + Q]
    new_references = (numerator.reshape(CLS_DEV, M, 2, Q) / cycle_sum[:, None, None, :]).reshape(
        CLS_DEV, 2 * M * Q
    )
    particle_total = columns * lax.axis_size(GRP) * lax.axis_size(DEV)
    occupancy = class_mass * (classes_total / particle_total)
    return (new_references, occupancy)


def solution(mesh):
    grp_count, dev_count = mesh.devices.shape
    core_count = 2
    y_count = 4
    split = jax.sharding.Mesh(
        mesh.devices.reshape(
            grp_count // core_count, core_count, dev_count // y_count, y_count
        ),
        GRP + DEV,
    )
    return jax.shard_map(
        local,
        mesh=split,
        in_specs=(P(DEV, None), P(None, GRP + DEV), P(GRP + DEV), P(), P(), P()),
        out_specs=(P(DEV, None), P(DEV)),
        check_vma=False,
    )
```

```python
import functools
import math

import jax
import jax.numpy as jnp
from jax import lax
from jax.experimental import pallas as pl
from jax.experimental.pallas import tpu as pltpu
from jax.sharding import PartitionSpec as P

Q = 32
M = 32
R = 128
CLS_DEV = 6
CLS_STEP = 48
GRP = ("x", "core")
DEV = ("z", "y")


def angle_tables(cycle_freqs, count_turns):
    freq_index = jnp.arange(cycle_freqs, dtype=jnp.int32)
    turn_index = jnp.arange(count_turns, dtype=jnp.int32)
    wrapped = freq_index[:, None] * turn_index[None, :] % count_turns
    phases = 2.0 * math.pi / count_turns * wrapped.astype(jnp.float32)
    factor = jnp.where(freq_index == 0, 1.0, 2.0).astype(jnp.float32)[:, None]
    cosine = jnp.cos(phases)
    sine_part = jnp.sin(phases)
    score_table = jnp.stack([factor * cosine, factor * sine_part], 0).astype(jnp.bfloat16)
    turn_table = jnp.stack([cosine, sine_part], 0).astype(jnp.bfloat16)
    return (score_table, turn_table)


def particle_terms(particles, defocus_bin, contrast_table, noise_power):
    columns = particles.shape[1]
    cycle_count = contrast_table.shape[1]
    freq_count = particles.shape[0] // (2 * cycle_count)
    onehot = (
        defocus_bin[None, :] == jnp.arange(contrast_table.shape[0], dtype=jnp.int32)[:, None]
    ).astype(jnp.float32)
    contrast = jnp.dot(contrast_table.T, onehot, precision=lax.Precision.HIGHEST)
    scaled = contrast / noise_power[:, None]
    power_term = contrast * scaled
    weighted = (
        particles.astype(jnp.float32).reshape(freq_count, 2, cycle_count, columns)
        * scaled[None, None]
    ).astype(jnp.bfloat16)
    return (weighted.reshape(freq_count, 2 * cycle_count, columns), power_term)


def block_scores(table_ref, real_ref, imag_ref, shift_ref):
    crossed = jnp.concatenate([real_ref[...], imag_ref[...]], 0)
    raw = jnp.dot(table_ref[...], crossed, preferred_element_type=jnp.float32)
    return raw + shift_ref[...]


def norm_kernel(cols, table_ref, real_ref, imag_ref, bias_ref, out_ref, top_ref, total_ref):
    step = pl.program_id(0)

    @pl.when(step == 0)
    def _():
        top_ref[...] = jnp.full(top_ref.shape, -1e30, jnp.float32)
        total_ref[...] = jnp.zeros(total_ref.shape, jnp.float32)

    scores = block_scores(table_ref, real_ref, imag_ref, bias_ref)
    parts = [scores[:, j * cols : (j + 1) * cols] for j in range(scores.shape[1] // cols)]
    block_top = functools.reduce(jnp.maximum, [jnp.max(s, axis=0, keepdims=True) for s in parts])
    old_top = top_ref[...]
    new_top = jnp.maximum(old_top, block_top)
    block_total = functools.reduce(
        jnp.add, [jnp.sum(jnp.exp(s - new_top), axis=0, keepdims=True) for s in parts]
    )
    total_ref[...] = total_ref[...] * jnp.exp(old_top - new_top) + block_total
    top_ref[...] = new_top

    @pl.when(step == pl.num_programs(0) - 1)
    def _():
        out_ref[...] = top_ref[...] + jnp.log(total_ref[...])


def spectra_kernel(
    cols, table_ref, real_ref, imag_ref, bias_ref, norm_ref, turn_ref, cos_ref, sin_ref, weight_ref
):
    norm_row = jnp.concatenate([norm_ref[...]] * (bias_ref.shape[1] // cols), 1)
    scores = block_scores(table_ref, real_ref, imag_ref, bias_ref)
    responsibility = jnp.exp(scores - norm_row)
    full = jnp.dot(
        turn_ref[...], responsibility.astype(jnp.bfloat16), preferred_element_type=jnp.float32
    )
    rows = cos_ref.shape[0]
    cos_ref[...] = full[:rows].astype(jnp.bfloat16)
    sin_ref[...] = full[rows : 2 * rows].astype(jnp.bfloat16)
    weight_ref[...] = full[2 * rows : 2 * rows + 1]


def local(references, particles, defocus_bin, contrast_table, noise_power, class_prior):
    weighted, power_term = particle_terms(particles, defocus_bin, contrast_table, noise_power)
    score_table, turn_table = angle_tables(M, R)
    columns = particles.shape[1]
    dev_count = lax.axis_size(DEV)
    classes_total = CLS_DEV * dev_count

    core = lax.axis_index("core")
    own_rows = jnp.transpose(references.reshape(CLS_DEV, M, 2 * Q), (1, 0, 2))
    freq_half = M // 2
    own_half = lax.dynamic_slice_in_dim(own_rows, core * freq_half, freq_half, 0)
    copies = jnp.broadcast_to(own_half[None], (dev_count,) + own_half.shape)
    gathered = lax.all_to_all(copies, DEV, 0, 0, tiled=True)
    partner = lax.ppermute(gathered, "core", [(0, 1), (1, 0)])
    low = jnp.where(core == 0, gathered, partner)
    high = jnp.where(core == 0, partner, gathered)
    gathered = jnp.concatenate([low, high], 1)
    grid_rows = jnp.transpose(gathered, (1, 0, 2, 3)).reshape(M, classes_total, 2 * Q)
    factor = jnp.where(jnp.arange(M) == 0, 1.0, 2.0).astype(jnp.float32)
    squares = jnp.sum(grid_rows.astype(jnp.float32) ** 2 * factor[:, None, None], axis=0)
    cycle_power = squares[:, :Q] + squares[:, Q:]
    swapped = jnp.concatenate([weighted[:, Q:], -weighted[:, :Q]], 1)
    rows = M
    width = classes_total * columns
    crossed_real = jnp.einsum(
        "mkc,mcb->mkb", grid_rows, weighted, preferred_element_type=jnp.float32
    ).astype(jnp.bfloat16).reshape(rows, width)
    crossed_imag = jnp.einsum(
        "mkc,mcb->mkb", grid_rows, swapped, preferred_element_type=jnp.float32
    ).astype(jnp.bfloat16).reshape(rows, width)
    penalty = jnp.dot(cycle_power, power_term, precision=lax.Precision.HIGHEST)
    bias = (class_prior[:, None] - 0.5 * penalty).reshape(1, width)
    table = jnp.transpose(score_table, (2, 0, 1)).reshape(R, 2 * M)
    turn = jnp.concatenate(
        [turn_table.reshape(2 * M, R), jnp.ones((1, R), jnp.bfloat16), jnp.zeros((15, R), jnp.bfloat16)], 0
    )

    block = CLS_STEP * columns
    steps = width // block
    table_spec = pl.BlockSpec((R, 2 * rows), lambda i: (0, 0))
    crossed_spec = pl.BlockSpec((rows, block), lambda i: (0, i))
    row_spec = pl.BlockSpec((1, block), lambda i: (0, i))
    log_norm = pl.pallas_call(
        functools.partial(norm_kernel, columns),
        grid=(steps,),
        in_specs=[table_spec, crossed_spec, crossed_spec, row_spec],
        out_specs=pl.BlockSpec((1, columns), lambda i: (0, 0)),
        out_shape=jax.ShapeDtypeStruct((1, columns), jnp.float32),
        scratch_shapes=[pltpu.VMEM((1, columns), jnp.float32)] * 2,
        compiler_params=pltpu.CompilerParams(dimension_semantics=("arbitrary",)),
    )(table, crossed_real, crossed_imag, bias)
    spectra_cos, spectra_sin, class_weight = pl.pallas_call(
        functools.partial(spectra_kernel, columns),
        grid=(steps,),
        in_specs=[
            table_spec,
            crossed_spec,
            crossed_spec,
            row_spec,
            pl.BlockSpec((1, columns), lambda i: (0, 0)),
            pl.BlockSpec(turn.shape, lambda i: (0, 0)),
        ],
        out_specs=[crossed_spec, crossed_spec, row_spec],
        out_shape=[
            jax.ShapeDtypeStruct((rows, width), jnp.bfloat16),
            jax.ShapeDtypeStruct((rows, width), jnp.bfloat16),
            jax.ShapeDtypeStruct((1, width), jnp.float32),
        ],
        compiler_params=pltpu.CompilerParams(dimension_semantics=("arbitrary",)),
    )(table, crossed_real, crossed_imag, bias, log_norm, turn)

    spectra_cos = spectra_cos.reshape(M, classes_total, columns)
    spectra_sin = spectra_sin.reshape(M, classes_total, columns)
    numer_all = jnp.einsum(
        "mkb,mcb->kmc", spectra_cos, weighted, preferred_element_type=jnp.float32
    ) + jnp.einsum("mkb,mcb->kmc", spectra_sin, swapped, preferred_element_type=jnp.float32)
    numer_all = numer_all.reshape(classes_total, 2 * M * Q)
    class_weight = class_weight.reshape(classes_total, columns)
    cycles_all = jnp.dot(class_weight, power_term.T, precision=lax.Precision.HIGHEST)
    mass_all = jnp.sum(class_weight, axis=1)

    width = numer_all.shape[1]
    packed = jnp.concatenate(
        [numer_all, cycles_all, mass_all[:, None], jnp.zeros((classes_total, 223), jnp.float32)], 1
    )
    core_count = lax.axis_size("core")
    half = packed.shape[1] // core_count
    mine = lax.dynamic_slice_in_dim(packed, core * half, half, 1)
    other = lax.dynamic_slice_in_dim(packed, (1 - core) * half, half, 1)
    packed = mine + lax.ppermute(other, "core", [(0, 1), (1, 0)])
    packed = packed.reshape(lax.axis_size("z"), lax.axis_size("y"), CLS_DEV, half)
    own = jnp.sum(lax.all_to_all(packed, "y", 1, 1, tiled=True), 1)
    own = jnp.sum(lax.all_to_all(own, "z", 0, 0, tiled=True), 0)
    own = lax.all_gather(own, GRP, axis=0, tiled=False)
    own = jnp.sum(own.reshape(lax.axis_size("x"), core_count, CLS_DEV, half), 0)
    own = jnp.concatenate([own[0], own[1]], 1)
    numerator = own[:, :width]
    cycle_sum = own[:, width : width + Q]
    class_mass = own[:, width + Q]
    new_references = (numerator.reshape(CLS_DEV, M, 2, Q) / cycle_sum[:, None, None, :]).reshape(
        CLS_DEV, 2 * M * Q
    )
    particle_total = columns * lax.axis_size(GRP) * lax.axis_size(DEV)
    occupancy = class_mass * (classes_total / particle_total)
    return (new_references, occupancy)


def solution(mesh):
    grp_count, dev_count = mesh.devices.shape
    core_count = 2
    y_count = 4
    split = jax.sharding.Mesh(
        mesh.devices.reshape(
            grp_count // core_count, core_count, dev_count // y_count, y_count
        ),
        GRP + DEV,
    )
    return jax.shard_map(
        local,
        mesh=split,
        in_specs=(P(DEV, None), P(None, GRP + DEV), P(GRP + DEV), P(), P(), P()),
        out_specs=(P(DEV, None), P(DEV)),
        check_vma=False,
    )
```

```python
import functools
import math

import jax
import jax.numpy as jnp
from jax import lax
from jax.experimental import pallas as pl
from jax.experimental.pallas import tpu as pltpu
from jax.sharding import PartitionSpec as P

Q = 32
M = 32
R = 128
CLS_DEV = 6
CLS_STEP = 48
GRP = ("x", "core")
DEV = ("z", "y")


def angle_tables(cycle_freqs, count_turns):
    freq_index = jnp.arange(cycle_freqs, dtype=jnp.int32)
    turn_index = jnp.arange(count_turns, dtype=jnp.int32)
    wrapped = freq_index[:, None] * turn_index[None, :] % count_turns
    phases = 2.0 * math.pi / count_turns * wrapped.astype(jnp.float32)
    factor = jnp.where(freq_index == 0, 1.0, 2.0).astype(jnp.float32)[:, None]
    cosine = jnp.cos(phases)
    sine_part = jnp.sin(phases)
    score_table = jnp.stack([factor * cosine, factor * sine_part], 0).astype(jnp.bfloat16)
    turn_table = jnp.stack([cosine, sine_part], 0).astype(jnp.bfloat16)
    return (score_table, turn_table)


def particle_terms(particles, defocus_bin, contrast_table, noise_power):
    columns = particles.shape[1]
    cycle_count = contrast_table.shape[1]
    freq_count = particles.shape[0] // (2 * cycle_count)
    onehot = (
        defocus_bin[None, :] == jnp.arange(contrast_table.shape[0], dtype=jnp.int32)[:, None]
    ).astype(jnp.float32)
    contrast = jnp.dot(contrast_table.T, onehot, precision=lax.Precision.HIGHEST)
    scaled = contrast / noise_power[:, None]
    power_term = contrast * scaled
    weighted = (
        particles.astype(jnp.float32).reshape(freq_count, 2, cycle_count, columns)
        * scaled[None, None]
    ).astype(jnp.bfloat16)
    return (weighted.reshape(freq_count, 2 * cycle_count, columns), power_term)


def block_scores(table_ref, real_ref, imag_ref, shift_ref):
    crossed = jnp.concatenate([real_ref[...], imag_ref[...]], 0)
    raw = jnp.dot(table_ref[...], crossed, preferred_element_type=jnp.float32)
    return raw + shift_ref[...]


def norm_kernel(cols, table_ref, real_ref, imag_ref, bias_ref, out_ref, top_ref, total_ref):
    step = pl.program_id(0)

    @pl.when(step == 0)
    def _():
        top_ref[...] = jnp.full(top_ref.shape, -1e30, jnp.float32)
        total_ref[...] = jnp.zeros(total_ref.shape, jnp.float32)

    scores = block_scores(table_ref, real_ref, imag_ref, bias_ref)
    parts = [scores[:, j * cols : (j + 1) * cols] for j in range(scores.shape[1] // cols)]
    block_top = functools.reduce(jnp.maximum, [jnp.max(s, axis=0, keepdims=True) for s in parts])
    old_top = top_ref[...]
    new_top = jnp.maximum(old_top, block_top)
    block_total = functools.reduce(
        jnp.add, [jnp.sum(jnp.exp(s - new_top), axis=0, keepdims=True) for s in parts]
    )
    total_ref[...] = total_ref[...] * jnp.exp(old_top - new_top) + block_total
    top_ref[...] = new_top

    @pl.when(step == pl.num_programs(0) - 1)
    def _():
        out_ref[...] = top_ref[...] + jnp.log(total_ref[...])


def spectra_kernel(
    cols, table_ref, real_ref, imag_ref, bias_ref, norm_ref, turn_ref, cos_ref, sin_ref, weight_ref
):
    norm_row = jnp.concatenate([norm_ref[...]] * (bias_ref.shape[1] // cols), 1)
    scores = block_scores(table_ref, real_ref, imag_ref, bias_ref)
    responsibility = jnp.exp(scores - norm_row)
    full = jnp.dot(
        turn_ref[...], responsibility.astype(jnp.bfloat16), preferred_element_type=jnp.float32
    )
    rows = cos_ref.shape[0]
    cos_ref[...] = full[:rows].astype(jnp.bfloat16)
    sin_ref[...] = full[rows : 2 * rows].astype(jnp.bfloat16)
    weight_ref[...] = full[2 * rows : 2 * rows + 1]


def local(references, particles, defocus_bin, contrast_table, noise_power, class_prior):
    weighted, power_term = particle_terms(particles, defocus_bin, contrast_table, noise_power)
    score_table, turn_table = angle_tables(M, R)
    columns = particles.shape[1]
    dev_count = lax.axis_size(DEV)
    classes_total = CLS_DEV * dev_count

    core = lax.axis_index("core")
    own_rows = jnp.transpose(references.reshape(CLS_DEV, M, 2 * Q), (1, 0, 2))
    freq_half = M // 2
    own_half = lax.dynamic_slice_in_dim(own_rows, core * freq_half, freq_half, 0)
    copies = jnp.broadcast_to(own_half[None], (dev_count,) + own_half.shape)
    gathered = lax.all_to_all(copies, DEV, 0, 2, tiled=True)[0]
    partner = lax.ppermute(gathered, "core", [(0, 1), (1, 0)])
    low = jnp.where(core == 0, gathered, partner)
    high = jnp.where(core == 0, partner, gathered)
    grid_rows = jnp.concatenate([low, high], 0)
    factor = jnp.where(jnp.arange(M) == 0, 1.0, 2.0).astype(jnp.float32)
    squares = jnp.sum(grid_rows.astype(jnp.float32) ** 2 * factor[:, None, None], axis=0)
    cycle_power = squares[:, :Q] + squares[:, Q:]
    swapped = jnp.concatenate([weighted[:, Q:], -weighted[:, :Q]], 1)
    rows = M
    width = classes_total * columns
    crossed_real = jnp.einsum(
        "mkc,mcb->mkb", grid_rows, weighted, preferred_element_type=jnp.float32
    ).astype(jnp.bfloat16).reshape(rows, width)
    crossed_imag = jnp.einsum(
        "mkc,mcb->mkb", grid_rows, swapped, preferred_element_type=jnp.float32
    ).astype(jnp.bfloat16).reshape(rows, width)
    penalty = jnp.dot(cycle_power, power_term, precision=lax.Precision.HIGHEST)
    bias = (class_prior[:, None] - 0.5 * penalty).reshape(1, width)
    table = jnp.transpose(score_table, (2, 0, 1)).reshape(R, 2 * M)
    turn = jnp.concatenate(
        [turn_table.reshape(2 * M, R), jnp.ones((1, R), jnp.bfloat16), jnp.zeros((15, R), jnp.bfloat16)], 0
    )

    block = CLS_STEP * columns
    steps = width // block
    table_spec = pl.BlockSpec((R, 2 * rows), lambda i: (0, 0))
    crossed_spec = pl.BlockSpec((rows, block), lambda i: (0, i))
    row_spec = pl.BlockSpec((1, block), lambda i: (0, i))
    log_norm = pl.pallas_call(
        functools.partial(norm_kernel, columns),
        grid=(steps,),
        in_specs=[table_spec, crossed_spec, crossed_spec, row_spec],
        out_specs=pl.BlockSpec((1, columns), lambda i: (0, 0)),
        out_shape=jax.ShapeDtypeStruct((1, columns), jnp.float32),
        scratch_shapes=[pltpu.VMEM((1, columns), jnp.float32)] * 2,
        compiler_params=pltpu.CompilerParams(dimension_semantics=("arbitrary",)),
    )(table, crossed_real, crossed_imag, bias)
    spectra_cos, spectra_sin, class_weight = pl.pallas_call(
        functools.partial(spectra_kernel, columns),
        grid=(steps,),
        in_specs=[
            table_spec,
            crossed_spec,
            crossed_spec,
            row_spec,
            pl.BlockSpec((1, columns), lambda i: (0, 0)),
            pl.BlockSpec(turn.shape, lambda i: (0, 0)),
        ],
        out_specs=[crossed_spec, crossed_spec, row_spec],
        out_shape=[
            jax.ShapeDtypeStruct((rows, width), jnp.bfloat16),
            jax.ShapeDtypeStruct((rows, width), jnp.bfloat16),
            jax.ShapeDtypeStruct((1, width), jnp.float32),
        ],
        compiler_params=pltpu.CompilerParams(dimension_semantics=("arbitrary",)),
    )(table, crossed_real, crossed_imag, bias, log_norm, turn)

    spectra_cos = spectra_cos.reshape(M, classes_total, columns)
    spectra_sin = spectra_sin.reshape(M, classes_total, columns)
    numer_all = jnp.einsum(
        "mkb,mcb->kmc", spectra_cos, weighted, preferred_element_type=jnp.float32
    ) + jnp.einsum("mkb,mcb->kmc", spectra_sin, swapped, preferred_element_type=jnp.float32)
    numer_all = numer_all.reshape(classes_total, 2 * M * Q)
    class_weight = class_weight.reshape(classes_total, columns)
    cycles_all = jnp.dot(class_weight, power_term.T, precision=lax.Precision.HIGHEST)
    mass_all = jnp.sum(class_weight, axis=1)

    width = numer_all.shape[1]
    packed = jnp.concatenate(
        [numer_all, cycles_all, mass_all[:, None], jnp.zeros((classes_total, 223), jnp.float32)], 1
    )
    core_count = lax.axis_size("core")
    half = packed.shape[1] // core_count
    mine = lax.dynamic_slice_in_dim(packed, core * half, half, 1)
    other = lax.dynamic_slice_in_dim(packed, (1 - core) * half, half, 1)
    packed = mine + lax.ppermute(other, "core", [(0, 1), (1, 0)])
    packed = packed.reshape(lax.axis_size("z"), lax.axis_size("y"), CLS_DEV, half)
    own = jnp.sum(lax.all_to_all(packed, "y", 1, 1, tiled=True), 1)
    own = jnp.sum(lax.all_to_all(own, "z", 0, 0, tiled=True), 0)
    own = lax.all_gather(own, GRP, axis=0, tiled=False)
    own = jnp.sum(own.reshape(lax.axis_size("x"), core_count, CLS_DEV, half), 0)
    own = jnp.concatenate([own[0], own[1]], 1)
    numerator = own[:, :width]
    cycle_sum = own[:, width : width + Q]
    class_mass = own[:, width + Q]
    new_references = (numerator.reshape(CLS_DEV, M, 2, Q) / cycle_sum[:, None, None, :]).reshape(
        CLS_DEV, 2 * M * Q
    )
    particle_total = columns * lax.axis_size(GRP) * lax.axis_size(DEV)
    occupancy = class_mass * (classes_total / particle_total)
    return (new_references, occupancy)


def solution(mesh):
    grp_count, dev_count = mesh.devices.shape
    core_count = 2
    y_count = 4
    split = jax.sharding.Mesh(
        mesh.devices.reshape(
            grp_count // core_count, core_count, dev_count // y_count, y_count
        ),
        GRP + DEV,
    )
    return jax.shard_map(
        local,
        mesh=split,
        in_specs=(P(DEV, None), P(None, GRP + DEV), P(GRP + DEV), P(), P(), P()),
        out_specs=(P(DEV, None), P(DEV)),
        check_vma=False,
    )
```

```python
import functools
import math

import jax
import jax.numpy as jnp
from jax import lax
from jax.experimental import pallas as pl
from jax.experimental.pallas import tpu as pltpu
from jax.sharding import PartitionSpec as P

Q = 32
M = 32
R = 128
CLS_DEV = 6
CLS_STEP = 48
GRP = ("x", "core")
DEV = ("z", "y")


def angle_tables(cycle_freqs, count_turns):
    freq_index = jnp.arange(cycle_freqs, dtype=jnp.int32)
    turn_index = jnp.arange(count_turns, dtype=jnp.int32)
    wrapped = freq_index[:, None] * turn_index[None, :] % count_turns
    phases = 2.0 * math.pi / count_turns * wrapped.astype(jnp.float32)
    factor = jnp.where(freq_index == 0, 1.0, 2.0).astype(jnp.float32)[:, None]
    cosine = jnp.cos(phases)
    sine_part = jnp.sin(phases)
    score_table = jnp.stack([factor * cosine, factor * sine_part], 0).astype(jnp.bfloat16)
    turn_table = jnp.stack([cosine, sine_part], 0).astype(jnp.bfloat16)
    return (score_table, turn_table)


def particle_terms(particles, defocus_bin, contrast_table, noise_power):
    columns = particles.shape[1]
    cycle_count = contrast_table.shape[1]
    freq_count = particles.shape[0] // (2 * cycle_count)
    onehot = (
        defocus_bin[None, :] == jnp.arange(contrast_table.shape[0], dtype=jnp.int32)[:, None]
    ).astype(jnp.float32)
    contrast = jnp.dot(contrast_table.T, onehot, precision=lax.Precision.HIGHEST)
    scaled = contrast / noise_power[:, None]
    power_term = contrast * scaled
    weighted = (
        particles.astype(jnp.float32).reshape(freq_count, 2, cycle_count, columns)
        * scaled[None, None]
    ).astype(jnp.bfloat16)
    return (weighted.reshape(freq_count, 2 * cycle_count, columns), power_term)


def block_scores(table_ref, real_ref, imag_ref, shift_ref):
    classes = real_ref.shape[1]
    crossed = jnp.concatenate(
        [jnp.concatenate([real_ref[:, j, :], imag_ref[:, j, :]], 0) for j in range(classes)], 1
    )
    raw = jnp.dot(table_ref[...], crossed, preferred_element_type=jnp.float32)
    return raw + shift_ref[...]


def norm_kernel(cols, table_ref, real_ref, imag_ref, bias_ref, out_ref, top_ref, total_ref):
    step = pl.program_id(0)

    @pl.when(step == 0)
    def _():
        top_ref[...] = jnp.full(top_ref.shape, -1e30, jnp.float32)
        total_ref[...] = jnp.zeros(total_ref.shape, jnp.float32)

    scores = block_scores(table_ref, real_ref, imag_ref, bias_ref)
    parts = [scores[:, j * cols : (j + 1) * cols] for j in range(scores.shape[1] // cols)]
    block_top = functools.reduce(jnp.maximum, [jnp.max(s, axis=0, keepdims=True) for s in parts])
    old_top = top_ref[...]
    new_top = jnp.maximum(old_top, block_top)
    block_total = functools.reduce(
        jnp.add, [jnp.sum(jnp.exp(s - new_top), axis=0, keepdims=True) for s in parts]
    )
    total_ref[...] = total_ref[...] * jnp.exp(old_top - new_top) + block_total
    top_ref[...] = new_top

    @pl.when(step == pl.num_programs(0) - 1)
    def _():
        out_ref[...] = top_ref[...] + jnp.log(total_ref[...])


def spectra_kernel(
    cols, table_ref, real_ref, imag_ref, bias_ref, norm_ref, turn_ref, cos_ref, sin_ref, weight_ref
):
    norm_row = jnp.concatenate([norm_ref[...]] * (bias_ref.shape[1] // cols), 1)
    scores = block_scores(table_ref, real_ref, imag_ref, bias_ref)
    responsibility = jnp.exp(scores - norm_row)
    full = jnp.dot(
        turn_ref[...], responsibility.astype(jnp.bfloat16), preferred_element_type=jnp.float32
    )
    rows = cos_ref.shape[0]
    for j in range(cos_ref.shape[1]):
        part = full[:, j * cols : (j + 1) * cols]
        cos_ref[:, j, :] = part[:rows].astype(jnp.bfloat16)
        sin_ref[:, j, :] = part[rows : 2 * rows].astype(jnp.bfloat16)
    weight_ref[...] = full[2 * rows : 2 * rows + 1]


def local(references, particles, defocus_bin, contrast_table, noise_power, class_prior):
    weighted, power_term = particle_terms(particles, defocus_bin, contrast_table, noise_power)
    score_table, turn_table = angle_tables(M, R)
    columns = particles.shape[1]
    dev_count = lax.axis_size(DEV)
    classes_total = CLS_DEV * dev_count

    core = lax.axis_index("core")
    own_rows = jnp.transpose(references.reshape(CLS_DEV, M, 2 * Q), (1, 0, 2))
    freq_half = M // 2
    own_half = lax.dynamic_slice_in_dim(own_rows, core * freq_half, freq_half, 0)
    copies = jnp.broadcast_to(own_half[None], (dev_count,) + own_half.shape)
    gathered = lax.all_to_all(copies, DEV, 0, 2, tiled=True)[0]
    partner = lax.ppermute(gathered, "core", [(0, 1), (1, 0)])
    low = jnp.where(core == 0, gathered, partner)
    high = jnp.where(core == 0, partner, gathered)
    grid_rows = jnp.concatenate([low, high], 0)
    factor = jnp.where(jnp.arange(M) == 0, 1.0, 2.0).astype(jnp.float32)
    squares = jnp.sum(grid_rows.astype(jnp.float32) ** 2 * factor[:, None, None], axis=0)
    cycle_power = squares[:, :Q] + squares[:, Q:]
    swapped = jnp.concatenate([weighted[:, Q:], -weighted[:, :Q]], 1)
    rows = M
    width = classes_total * columns
    crossed_real = jnp.einsum(
        "mkc,mcb->mkb", grid_rows, weighted, preferred_element_type=jnp.float32
    ).astype(jnp.bfloat16)
    crossed_imag = jnp.einsum(
        "mkc,mcb->mkb", grid_rows, swapped, preferred_element_type=jnp.float32
    ).astype(jnp.bfloat16)
    penalty = jnp.dot(cycle_power, power_term, precision=lax.Precision.HIGHEST)
    bias = (class_prior[:, None] - 0.5 * penalty).reshape(1, width)
    table = jnp.transpose(score_table, (2, 0, 1)).reshape(R, 2 * M)
    turn = jnp.concatenate(
        [turn_table.reshape(2 * M, R), jnp.ones((1, R), jnp.bfloat16), jnp.zeros((15, R), jnp.bfloat16)], 0
    )

    block = CLS_STEP * columns
    steps = width // block
    table_spec = pl.BlockSpec((R, 2 * rows), lambda i: (0, 0))
    crossed_spec = pl.BlockSpec((rows, CLS_STEP, columns), lambda i: (0, i, 0))
    row_spec = pl.BlockSpec((1, block), lambda i: (0, i))
    log_norm = pl.pallas_call(
        functools.partial(norm_kernel, columns),
        grid=(steps,),
        in_specs=[table_spec, crossed_spec, crossed_spec, row_spec],
        out_specs=pl.BlockSpec((1, columns), lambda i: (0, 0)),
        out_shape=jax.ShapeDtypeStruct((1, columns), jnp.float32),
        scratch_shapes=[pltpu.VMEM((1, columns), jnp.float32)] * 2,
        compiler_params=pltpu.CompilerParams(dimension_semantics=("arbitrary",)),
    )(table, crossed_real, crossed_imag, bias)
    spectra_cos, spectra_sin, class_weight = pl.pallas_call(
        functools.partial(spectra_kernel, columns),
        grid=(steps,),
        in_specs=[
            table_spec,
            crossed_spec,
            crossed_spec,
            row_spec,
            pl.BlockSpec((1, columns), lambda i: (0, 0)),
            pl.BlockSpec(turn.shape, lambda i: (0, 0)),
        ],
        out_specs=[crossed_spec, crossed_spec, row_spec],
        out_shape=[
            jax.ShapeDtypeStruct((rows, classes_total, columns), jnp.bfloat16),
            jax.ShapeDtypeStruct((rows, classes_total, columns), jnp.bfloat16),
            jax.ShapeDtypeStruct((1, width), jnp.float32),
        ],
        compiler_params=pltpu.CompilerParams(dimension_semantics=("arbitrary",)),
    )(table, crossed_real, crossed_imag, bias, log_norm, turn)

    numer_all = jnp.einsum(
        "mkb,mcb->kmc", spectra_cos, weighted, preferred_element_type=jnp.float32
    ) + jnp.einsum("mkb,mcb->kmc", spectra_sin, swapped, preferred_element_type=jnp.float32)
    numer_all = numer_all.reshape(classes_total, 2 * M * Q)
    class_weight = class_weight.reshape(classes_total, columns)
    cycles_all = jnp.dot(class_weight, power_term.T, precision=lax.Precision.HIGHEST)
    mass_all = jnp.sum(class_weight, axis=1)

    width = numer_all.shape[1]
    packed = jnp.concatenate(
        [numer_all, cycles_all, mass_all[:, None], jnp.zeros((classes_total, 223), jnp.float32)], 1
    )
    core_count = lax.axis_size("core")
    half = packed.shape[1] // core_count
    mine = lax.dynamic_slice_in_dim(packed, core * half, half, 1)
    other = lax.dynamic_slice_in_dim(packed, (1 - core) * half, half, 1)
    packed = mine + lax.ppermute(other, "core", [(0, 1), (1, 0)])
    packed = packed.reshape(lax.axis_size("z"), lax.axis_size("y"), CLS_DEV, half)
    own = jnp.sum(lax.all_to_all(packed, "y", 1, 1, tiled=True), 1)
    own = jnp.sum(lax.all_to_all(own, "z", 0, 0, tiled=True), 0)
    own = lax.all_gather(own, GRP, axis=0, tiled=False)
    own = jnp.sum(own.reshape(lax.axis_size("x"), core_count, CLS_DEV, half), 0)
    own = jnp.concatenate([own[0], own[1]], 1)
    numerator = own[:, :width]
    cycle_sum = own[:, width : width + Q]
    class_mass = own[:, width + Q]
    new_references = (numerator.reshape(CLS_DEV, M, 2, Q) / cycle_sum[:, None, None, :]).reshape(
        CLS_DEV, 2 * M * Q
    )
    particle_total = columns * lax.axis_size(GRP) * lax.axis_size(DEV)
    occupancy = class_mass * (classes_total / particle_total)
    return (new_references, occupancy)


def solution(mesh):
    grp_count, dev_count = mesh.devices.shape
    core_count = 2
    y_count = 4
    split = jax.sharding.Mesh(
        mesh.devices.reshape(
            grp_count // core_count, core_count, dev_count // y_count, y_count
        ),
        GRP + DEV,
    )
    return jax.shard_map(
        local,
        mesh=split,
        in_specs=(P(DEV, None), P(None, GRP + DEV), P(GRP + DEV), P(), P(), P()),
        out_specs=(P(DEV, None), P(DEV)),
        check_vma=False,
    )
```

```python
import functools
import math

import jax
import jax.numpy as jnp
from jax import lax
from jax.experimental import pallas as pl
from jax.experimental.pallas import tpu as pltpu
from jax.sharding import PartitionSpec as P

Q = 32
M = 32
R = 128
CLS_DEV = 6
CLS_STEP = 48
GRP = ("x", "core")
DEV = ("z", "y")


def angle_tables(cycle_freqs, count_turns):
    freq_index = jnp.arange(cycle_freqs, dtype=jnp.int32)
    turn_index = jnp.arange(count_turns, dtype=jnp.int32)
    wrapped = freq_index[:, None] * turn_index[None, :] % count_turns
    phases = 2.0 * math.pi / count_turns * wrapped.astype(jnp.float32)
    factor = jnp.where(freq_index == 0, 1.0, 2.0).astype(jnp.float32)[:, None]
    cosine = jnp.cos(phases)
    sine_part = jnp.sin(phases)
    score_table = jnp.stack([factor * cosine, factor * sine_part], 0).astype(jnp.bfloat16)
    turn_table = jnp.stack([cosine, sine_part], 0).astype(jnp.bfloat16)
    return (score_table, turn_table)


def particle_terms(particles, defocus_bin, contrast_table, noise_power):
    columns = particles.shape[1]
    cycle_count = contrast_table.shape[1]
    freq_count = particles.shape[0] // (2 * cycle_count)
    onehot = (
        defocus_bin[None, :] == jnp.arange(contrast_table.shape[0], dtype=jnp.int32)[:, None]
    ).astype(jnp.float32)
    contrast = jnp.dot(contrast_table.T, onehot, precision=lax.Precision.HIGHEST)
    scaled = contrast / noise_power[:, None]
    power_term = contrast * scaled
    weighted = (
        particles.astype(jnp.float32).reshape(freq_count, 2, cycle_count, columns)
        * scaled[None, None]
    ).astype(jnp.bfloat16)
    return (weighted.reshape(freq_count, 2 * cycle_count, columns), power_term)


def block_scores(table_ref, real_ref, imag_ref, shift_ref):
    crossed = jnp.concatenate([real_ref[...], imag_ref[...]], 0)
    raw = jnp.dot(table_ref[...], crossed, preferred_element_type=jnp.float32)
    return raw + shift_ref[...]


def norm_kernel(cols, table_ref, real_ref, imag_ref, bias_ref, out_ref, top_ref, total_ref):
    step = pl.program_id(0)

    @pl.when(step == 0)
    def _():
        top_ref[...] = jnp.full(top_ref.shape, -1e30, jnp.float32)
        total_ref[...] = jnp.zeros(total_ref.shape, jnp.float32)

    scores = block_scores(table_ref, real_ref, imag_ref, bias_ref)
    parts = [scores[:, j * cols : (j + 1) * cols] for j in range(scores.shape[1] // cols)]
    block_top = functools.reduce(jnp.maximum, [jnp.max(s, axis=0, keepdims=True) for s in parts])
    old_top = top_ref[...]
    new_top = jnp.maximum(old_top, block_top)
    block_total = functools.reduce(
        jnp.add, [jnp.sum(jnp.exp(s - new_top), axis=0, keepdims=True) for s in parts]
    )
    total_ref[...] = total_ref[...] * jnp.exp(old_top - new_top) + block_total
    top_ref[...] = new_top

    @pl.when(step == pl.num_programs(0) - 1)
    def _():
        out_ref[...] = top_ref[...] + jnp.log(total_ref[...])


def spectra_kernel(
    cols, table_ref, real_ref, imag_ref, bias_ref, norm_ref, turn_ref, cos_ref, sin_ref, weight_ref
):
    norm_row = jnp.concatenate([norm_ref[...]] * (bias_ref.shape[1] // cols), 1)
    scores = block_scores(table_ref, real_ref, imag_ref, bias_ref)
    responsibility = jnp.exp(scores - norm_row)
    full = jnp.dot(
        turn_ref[...], responsibility.astype(jnp.bfloat16), preferred_element_type=jnp.float32
    )
    rows = cos_ref.shape[0]
    cos_ref[...] = full[:rows].astype(jnp.bfloat16)
    sin_ref[...] = full[rows : 2 * rows].astype(jnp.bfloat16)
    weight_ref[...] = full[2 * rows : 2 * rows + 1]


def local(references, particles, defocus_bin, contrast_table, noise_power, class_prior):
    weighted, power_term = particle_terms(particles, defocus_bin, contrast_table, noise_power)
    score_table, turn_table = angle_tables(M, R)
    columns = particles.shape[1]
    dev_count = lax.axis_size(DEV)
    classes_total = CLS_DEV * dev_count

    core = lax.axis_index("core")
    own_rows = jnp.transpose(references.reshape(CLS_DEV, M, 2 * Q), (1, 0, 2))
    freq_half = M // 2
    own_half = lax.dynamic_slice_in_dim(own_rows, core * freq_half, freq_half, 0)
    copies = jnp.broadcast_to(own_half[None], (dev_count,) + own_half.shape)
    gathered = lax.all_to_all(copies, DEV, 0, 2, tiled=True)[0]
    partner = lax.ppermute(gathered, "core", [(0, 1), (1, 0)])
    low = jnp.where(core == 0, gathered, partner)
    high = jnp.where(core == 0, partner, gathered)
    grid_rows = jnp.concatenate([low, high], 0)
    factor = jnp.where(jnp.arange(M) == 0, 1.0, 2.0).astype(jnp.float32)
    squares = jnp.sum(grid_rows.astype(jnp.float32) ** 2 * factor[:, None, None], axis=0)
    cycle_power = squares[:, :Q] + squares[:, Q:]
    swapped = jnp.concatenate([weighted[:, Q:], -weighted[:, :Q]], 1)
    weighted, swapped, power_term = lax.optimization_barrier((weighted, swapped, power_term))
    rows = M
    width = classes_total * columns
    crossed_real = jnp.einsum(
        "mkc,mcb->mkb", grid_rows, weighted, preferred_element_type=jnp.float32
    ).astype(jnp.bfloat16).reshape(rows, width)
    crossed_imag = jnp.einsum(
        "mkc,mcb->mkb", grid_rows, swapped, preferred_element_type=jnp.float32
    ).astype(jnp.bfloat16).reshape(rows, width)
    penalty = jnp.dot(cycle_power, power_term, precision=lax.Precision.HIGHEST)
    bias = (class_prior[:, None] - 0.5 * penalty).reshape(1, width)
    table = jnp.transpose(score_table, (2, 0, 1)).reshape(R, 2 * M)
    turn = jnp.concatenate(
        [turn_table.reshape(2 * M, R), jnp.ones((1, R), jnp.bfloat16), jnp.zeros((15, R), jnp.bfloat16)], 0
    )

    block = CLS_STEP * columns
    steps = width // block
    table_spec = pl.BlockSpec((R, 2 * rows), lambda i: (0, 0))
    crossed_spec = pl.BlockSpec((rows, block), lambda i: (0, i))
    row_spec = pl.BlockSpec((1, block), lambda i: (0, i))
    log_norm = pl.pallas_call(
        functools.partial(norm_kernel, columns),
        grid=(steps,),
        in_specs=[table_spec, crossed_spec, crossed_spec, row_spec],
        out_specs=pl.BlockSpec((1, columns), lambda i: (0, 0)),
        out_shape=jax.ShapeDtypeStruct((1, columns), jnp.float32),
        scratch_shapes=[pltpu.VMEM((1, columns), jnp.float32)] * 2,
        compiler_params=pltpu.CompilerParams(dimension_semantics=("arbitrary",)),
    )(table, crossed_real, crossed_imag, bias)
    spectra_cos, spectra_sin, class_weight = pl.pallas_call(
        functools.partial(spectra_kernel, columns),
        grid=(steps,),
        in_specs=[
            table_spec,
            crossed_spec,
            crossed_spec,
            row_spec,
            pl.BlockSpec((1, columns), lambda i: (0, 0)),
            pl.BlockSpec(turn.shape, lambda i: (0, 0)),
        ],
        out_specs=[crossed_spec, crossed_spec, row_spec],
        out_shape=[
            jax.ShapeDtypeStruct((rows, width), jnp.bfloat16),
            jax.ShapeDtypeStruct((rows, width), jnp.bfloat16),
            jax.ShapeDtypeStruct((1, width), jnp.float32),
        ],
        compiler_params=pltpu.CompilerParams(dimension_semantics=("arbitrary",)),
    )(table, crossed_real, crossed_imag, bias, log_norm, turn)

    spectra_cos = spectra_cos.reshape(M, classes_total, columns)
    spectra_sin = spectra_sin.reshape(M, classes_total, columns)
    numer_all = jnp.einsum(
        "mkb,mcb->kmc", spectra_cos, weighted, preferred_element_type=jnp.float32
    ) + jnp.einsum("mkb,mcb->kmc", spectra_sin, swapped, preferred_element_type=jnp.float32)
    numer_all = numer_all.reshape(classes_total, 2 * M * Q)
    class_weight = class_weight.reshape(classes_total, columns)
    cycles_all = jnp.dot(class_weight, power_term.T, precision=lax.Precision.HIGHEST)
    mass_all = jnp.sum(class_weight, axis=1)

    width = numer_all.shape[1]
    packed = jnp.concatenate(
        [numer_all, cycles_all, mass_all[:, None], jnp.zeros((classes_total, 223), jnp.float32)], 1
    )
    core_count = lax.axis_size("core")
    half = packed.shape[1] // core_count
    mine = lax.dynamic_slice_in_dim(packed, core * half, half, 1)
    other = lax.dynamic_slice_in_dim(packed, (1 - core) * half, half, 1)
    packed = mine + lax.ppermute(other, "core", [(0, 1), (1, 0)])
    packed = packed.reshape(lax.axis_size("z"), lax.axis_size("y"), CLS_DEV, half)
    own = jnp.sum(lax.all_to_all(packed, "y", 1, 1, tiled=True), 1)
    own = jnp.sum(lax.all_to_all(own, "z", 0, 0, tiled=True), 0)
    own = lax.all_gather(own, GRP, axis=0, tiled=False)
    own = jnp.sum(own.reshape(lax.axis_size("x"), core_count, CLS_DEV, half), 0)
    own = jnp.concatenate([own[0], own[1]], 1)
    numerator = own[:, :width]
    cycle_sum = own[:, width : width + Q]
    class_mass = own[:, width + Q]
    new_references = (numerator.reshape(CLS_DEV, M, 2, Q) / cycle_sum[:, None, None, :]).reshape(
        CLS_DEV, 2 * M * Q
    )
    particle_total = columns * lax.axis_size(GRP) * lax.axis_size(DEV)
    occupancy = class_mass * (classes_total / particle_total)
    return (new_references, occupancy)


def solution(mesh):
    grp_count, dev_count = mesh.devices.shape
    core_count = 2
    y_count = 4
    split = jax.sharding.Mesh(
        mesh.devices.reshape(
            grp_count // core_count, core_count, dev_count // y_count, y_count
        ),
        GRP + DEV,
    )
    return jax.shard_map(
        local,
        mesh=split,
        in_specs=(P(DEV, None), P(None, GRP + DEV), P(GRP + DEV), P(), P(), P()),
        out_specs=(P(DEV, None), P(DEV)),
        check_vma=False,
    )
```

```python
import functools
import math

import jax
import jax.numpy as jnp
from jax import lax
from jax.experimental import pallas as pl
from jax.experimental.pallas import tpu as pltpu
from jax.sharding import PartitionSpec as P

Q = 32
M = 32
R = 128
CLS_DEV = 6
CLS_STEP = 48
GRP = ("x", "core")
DEV = ("z", "y")


def angle_tables(cycle_freqs, count_turns):
    freq_index = jnp.arange(cycle_freqs, dtype=jnp.int32)
    turn_index = jnp.arange(count_turns, dtype=jnp.int32)
    wrapped = freq_index[:, None] * turn_index[None, :] % count_turns
    phases = 2.0 * math.pi / count_turns * wrapped.astype(jnp.float32)
    factor = jnp.where(freq_index == 0, 1.0, 2.0).astype(jnp.float32)[:, None]
    cosine = jnp.cos(phases)
    sine_part = jnp.sin(phases)
    score_table = jnp.stack([factor * cosine, factor * sine_part], 0).astype(jnp.bfloat16)
    turn_table = jnp.stack([cosine, sine_part], 0).astype(jnp.bfloat16)
    return (score_table, turn_table)


def particle_terms(particles, defocus_bin, contrast_table, noise_power):
    columns = particles.shape[1]
    cycle_count = contrast_table.shape[1]
    freq_count = particles.shape[0] // (2 * cycle_count)
    onehot = (
        defocus_bin[None, :] == jnp.arange(contrast_table.shape[0], dtype=jnp.int32)[:, None]
    ).astype(jnp.float32)
    contrast = jnp.dot(contrast_table.T, onehot, precision=lax.Precision.HIGHEST)
    scaled = contrast / noise_power[:, None]
    power_term = contrast * scaled
    weighted = (
        particles.astype(jnp.float32).reshape(freq_count, 2, cycle_count, columns)
        * scaled[None, None]
    ).astype(jnp.bfloat16)
    return (weighted.reshape(freq_count, 2 * cycle_count, columns), power_term)


def block_scores(table_ref, real_ref, imag_ref, shift_ref):
    crossed = jnp.concatenate([real_ref[...], imag_ref[...]], 0)
    raw = jnp.dot(table_ref[...], crossed, preferred_element_type=jnp.float32)
    return raw + shift_ref[...]


def norm_kernel(cols, table_ref, real_ref, imag_ref, bias_ref, out_ref, top_ref, total_ref):
    step = pl.program_id(0)

    @pl.when(step == 0)
    def _():
        top_ref[...] = jnp.full(top_ref.shape, -1e30, jnp.float32)
        total_ref[...] = jnp.zeros(total_ref.shape, jnp.float32)

    scores = block_scores(table_ref, real_ref, imag_ref, bias_ref)
    parts = [scores[:, j * cols : (j + 1) * cols] for j in range(scores.shape[1] // cols)]
    block_top = functools.reduce(jnp.maximum, [jnp.max(s, axis=0, keepdims=True) for s in parts])
    old_top = top_ref[...]
    new_top = jnp.maximum(old_top, block_top)
    block_total = functools.reduce(
        jnp.add, [jnp.sum(jnp.exp(s - new_top), axis=0, keepdims=True) for s in parts]
    )
    total_ref[...] = total_ref[...] * jnp.exp(old_top - new_top) + block_total
    top_ref[...] = new_top

    @pl.when(step == pl.num_programs(0) - 1)
    def _():
        out_ref[...] = top_ref[...] + jnp.log(total_ref[...])


def spectra_kernel(
    cols, table_ref, real_ref, imag_ref, bias_ref, norm_ref, turn_ref, cos_ref, sin_ref, weight_ref
):
    norm_row = jnp.concatenate([norm_ref[...]] * (bias_ref.shape[1] // cols), 1)
    scores = block_scores(table_ref, real_ref, imag_ref, bias_ref)
    responsibility = jnp.exp(scores - norm_row)
    full = jnp.dot(
        turn_ref[...], responsibility.astype(jnp.bfloat16), preferred_element_type=jnp.float32
    )
    rows = cos_ref.shape[0]
    cos_ref[...] = full[:rows].astype(jnp.bfloat16)
    sin_ref[...] = full[rows : 2 * rows].astype(jnp.bfloat16)
    weight_ref[...] = full[2 * rows : 2 * rows + 1]


def local(references, particles, defocus_bin, contrast_table, noise_power, class_prior):
    weighted, power_term = particle_terms(particles, defocus_bin, contrast_table, noise_power)
    score_table, turn_table = angle_tables(M, R)
    columns = particles.shape[1]
    dev_count = lax.axis_size(DEV)
    classes_total = CLS_DEV * dev_count

    core = lax.axis_index("core")
    own_rows = jnp.transpose(references.reshape(CLS_DEV, M, 2 * Q), (1, 0, 2))
    freq_half = M // 2
    own_half = lax.dynamic_slice_in_dim(own_rows, core * freq_half, freq_half, 0)
    copies = jnp.broadcast_to(own_half[None], (dev_count,) + own_half.shape)
    gathered = lax.all_to_all(copies, DEV, 0, 2, tiled=True)[0]
    grid_rows = lax.all_gather(gathered, "core", axis=0, tiled=True)
    factor = jnp.where(jnp.arange(M) == 0, 1.0, 2.0).astype(jnp.float32)
    squares = jnp.sum(grid_rows.astype(jnp.float32) ** 2 * factor[:, None, None], axis=0)
    cycle_power = squares[:, :Q] + squares[:, Q:]
    swapped = jnp.concatenate([weighted[:, Q:], -weighted[:, :Q]], 1)
    weighted, swapped, power_term = lax.optimization_barrier((weighted, swapped, power_term))
    rows = M
    width = classes_total * columns
    crossed_real = jnp.einsum(
        "mkc,mcb->mkb", grid_rows, weighted, preferred_element_type=jnp.float32
    ).astype(jnp.bfloat16).reshape(rows, width)
    crossed_imag = jnp.einsum(
        "mkc,mcb->mkb", grid_rows, swapped, preferred_element_type=jnp.float32
    ).astype(jnp.bfloat16).reshape(rows, width)
    penalty = jnp.dot(cycle_power, power_term, precision=lax.Precision.HIGHEST)
    bias = (class_prior[:, None] - 0.5 * penalty).reshape(1, width)
    table = jnp.transpose(score_table, (2, 0, 1)).reshape(R, 2 * M)
    turn = jnp.concatenate(
        [turn_table.reshape(2 * M, R), jnp.ones((1, R), jnp.bfloat16), jnp.zeros((15, R), jnp.bfloat16)], 0
    )

    block = CLS_STEP * columns
    steps = width // block
    table_spec = pl.BlockSpec((R, 2 * rows), lambda i: (0, 0))
    crossed_spec = pl.BlockSpec((rows, block), lambda i: (0, i))
    row_spec = pl.BlockSpec((1, block), lambda i: (0, i))
    log_norm = pl.pallas_call(
        functools.partial(norm_kernel, columns),
        grid=(steps,),
        in_specs=[table_spec, crossed_spec, crossed_spec, row_spec],
        out_specs=pl.BlockSpec((1, columns), lambda i: (0, 0)),
        out_shape=jax.ShapeDtypeStruct((1, columns), jnp.float32),
        scratch_shapes=[pltpu.VMEM((1, columns), jnp.float32)] * 2,
        compiler_params=pltpu.CompilerParams(dimension_semantics=("arbitrary",)),
    )(table, crossed_real, crossed_imag, bias)
    spectra_cos, spectra_sin, class_weight = pl.pallas_call(
        functools.partial(spectra_kernel, columns),
        grid=(steps,),
        in_specs=[
            table_spec,
            crossed_spec,
            crossed_spec,
            row_spec,
            pl.BlockSpec((1, columns), lambda i: (0, 0)),
            pl.BlockSpec(turn.shape, lambda i: (0, 0)),
        ],
        out_specs=[crossed_spec, crossed_spec, row_spec],
        out_shape=[
            jax.ShapeDtypeStruct((rows, width), jnp.bfloat16),
            jax.ShapeDtypeStruct((rows, width), jnp.bfloat16),
            jax.ShapeDtypeStruct((1, width), jnp.float32),
        ],
        compiler_params=pltpu.CompilerParams(dimension_semantics=("arbitrary",)),
    )(table, crossed_real, crossed_imag, bias, log_norm, turn)

    spectra_cos = spectra_cos.reshape(M, classes_total, columns)
    spectra_sin = spectra_sin.reshape(M, classes_total, columns)
    numer_all = jnp.einsum(
        "mkb,mcb->kmc", spectra_cos, weighted, preferred_element_type=jnp.float32
    ) + jnp.einsum("mkb,mcb->kmc", spectra_sin, swapped, preferred_element_type=jnp.float32)
    numer_all = numer_all.reshape(classes_total, 2 * M * Q)
    class_weight = class_weight.reshape(classes_total, columns)
    cycles_all = jnp.dot(class_weight, power_term.T, precision=lax.Precision.HIGHEST)
    mass_all = jnp.sum(class_weight, axis=1)

    width = numer_all.shape[1]
    packed = jnp.concatenate(
        [numer_all, cycles_all, mass_all[:, None], jnp.zeros((classes_total, 223), jnp.float32)], 1
    )
    core_count = lax.axis_size("core")
    half = packed.shape[1] // core_count
    mine = lax.dynamic_slice_in_dim(packed, core * half, half, 1)
    other = lax.dynamic_slice_in_dim(packed, (1 - core) * half, half, 1)
    packed = mine + lax.ppermute(other, "core", [(0, 1), (1, 0)])
    packed = packed.reshape(lax.axis_size("z"), lax.axis_size("y"), CLS_DEV, half)
    own = jnp.sum(lax.all_to_all(packed, "y", 1, 1, tiled=True), 1)
    own = jnp.sum(lax.all_to_all(own, "z", 0, 0, tiled=True), 0)
    own = lax.all_gather(own, GRP, axis=0, tiled=False)
    own = jnp.sum(own.reshape(lax.axis_size("x"), core_count, CLS_DEV, half), 0)
    own = jnp.concatenate([own[0], own[1]], 1)
    numerator = own[:, :width]
    cycle_sum = own[:, width : width + Q]
    class_mass = own[:, width + Q]
    new_references = (numerator.reshape(CLS_DEV, M, 2, Q) / cycle_sum[:, None, None, :]).reshape(
        CLS_DEV, 2 * M * Q
    )
    particle_total = columns * lax.axis_size(GRP) * lax.axis_size(DEV)
    occupancy = class_mass * (classes_total / particle_total)
    return (new_references, occupancy)


def solution(mesh):
    grp_count, dev_count = mesh.devices.shape
    core_count = 2
    y_count = 4
    split = jax.sharding.Mesh(
        mesh.devices.reshape(
            grp_count // core_count, core_count, dev_count // y_count, y_count
        ),
        GRP + DEV,
    )
    return jax.shard_map(
        local,
        mesh=split,
        in_specs=(P(DEV, None), P(None, GRP + DEV), P(GRP + DEV), P(), P(), P()),
        out_specs=(P(DEV, None), P(DEV)),
        check_vma=False,
    )
```

```python
import functools
import math

import jax
import jax.numpy as jnp
from jax import lax
from jax.experimental import pallas as pl
from jax.experimental.pallas import tpu as pltpu
from jax.sharding import PartitionSpec as P

Q = 32
M = 32
R = 128
CLS_DEV = 6
CLS_STEP = 48
GRP = ("x", "core")
DEV = ("z", "y")


def angle_tables(cycle_freqs, count_turns):
    freq_index = jnp.arange(cycle_freqs, dtype=jnp.int32)
    turn_index = jnp.arange(count_turns, dtype=jnp.int32)
    wrapped = freq_index[:, None] * turn_index[None, :] % count_turns
    phases = 2.0 * math.pi / count_turns * wrapped.astype(jnp.float32)
    factor = jnp.where(freq_index == 0, 1.0, 2.0).astype(jnp.float32)[:, None]
    cosine = jnp.cos(phases)
    sine_part = jnp.sin(phases)
    score_table = jnp.stack([factor * cosine, factor * sine_part], 0).astype(jnp.bfloat16)
    turn_table = jnp.stack([cosine, sine_part], 0).astype(jnp.bfloat16)
    return (score_table, turn_table)


def particle_terms(particles, defocus_bin, contrast_table, noise_power):
    columns = particles.shape[1]
    cycle_count = contrast_table.shape[1]
    freq_count = particles.shape[0] // (2 * cycle_count)
    onehot = (
        defocus_bin[None, :] == jnp.arange(contrast_table.shape[0], dtype=jnp.int32)[:, None]
    ).astype(jnp.float32)
    contrast = jnp.dot(contrast_table.T, onehot, precision=lax.Precision.HIGHEST)
    scaled = contrast / noise_power[:, None]
    power_term = contrast * scaled
    weighted = (
        particles.astype(jnp.float32).reshape(freq_count, 2, cycle_count, columns)
        * scaled[None, None]
    ).astype(jnp.bfloat16)
    return (weighted.reshape(freq_count, 2 * cycle_count, columns), power_term)


def block_scores(table_ref, real_ref, imag_ref, shift_ref):
    crossed = jnp.concatenate([real_ref[...], imag_ref[...]], 0)
    raw = jnp.dot(table_ref[...], crossed, preferred_element_type=jnp.float32)
    return raw + shift_ref[...]


def norm_kernel(cols, table_ref, real_ref, imag_ref, bias_ref, out_ref, top_ref, total_ref):
    step = pl.program_id(0)

    @pl.when(step == 0)
    def _():
        top_ref[...] = jnp.full(top_ref.shape, -1e30, jnp.float32)
        total_ref[...] = jnp.zeros(total_ref.shape, jnp.float32)

    scores = block_scores(table_ref, real_ref, imag_ref, bias_ref)
    parts = [scores[:, j * cols : (j + 1) * cols] for j in range(scores.shape[1] // cols)]
    block_top = functools.reduce(jnp.maximum, [jnp.max(s, axis=0, keepdims=True) for s in parts])
    old_top = top_ref[...]
    new_top = jnp.maximum(old_top, block_top)
    block_total = functools.reduce(
        jnp.add, [jnp.sum(jnp.exp(s - new_top), axis=0, keepdims=True) for s in parts]
    )
    total_ref[...] = total_ref[...] * jnp.exp(old_top - new_top) + block_total
    top_ref[...] = new_top

    @pl.when(step == pl.num_programs(0) - 1)
    def _():
        out_ref[...] = top_ref[...] + jnp.log(total_ref[...])


def spectra_kernel(
    cols, table_ref, real_ref, imag_ref, bias_ref, norm_ref, turn_ref, spectra_ref, weight_ref
):
    norm_row = jnp.concatenate([norm_ref[...]] * (bias_ref.shape[1] // cols), 1)
    scores = block_scores(table_ref, real_ref, imag_ref, bias_ref)
    responsibility = jnp.exp(scores - norm_row)
    full = jnp.dot(
        turn_ref[...], responsibility.astype(jnp.bfloat16), preferred_element_type=jnp.float32
    )
    rows = spectra_ref.shape[0]
    for j in range(full.shape[1] // cols):
        part = full[:, j * cols : (j + 1) * cols]
        spectra_ref[:, 2 * j * cols : (2 * j + 1) * cols] = part[:rows].astype(jnp.bfloat16)
        spectra_ref[:, (2 * j + 1) * cols : (2 * j + 2) * cols] = part[rows : 2 * rows].astype(
            jnp.bfloat16
        )
    weight_ref[...] = full[2 * rows : 2 * rows + 1]


def local(references, particles, defocus_bin, contrast_table, noise_power, class_prior):
    weighted, power_term = particle_terms(particles, defocus_bin, contrast_table, noise_power)
    score_table, turn_table = angle_tables(M, R)
    columns = particles.shape[1]
    dev_count = lax.axis_size(DEV)
    classes_total = CLS_DEV * dev_count

    core = lax.axis_index("core")
    own_rows = jnp.transpose(references.reshape(CLS_DEV, M, 2 * Q), (1, 0, 2))
    freq_half = M // 2
    own_half = lax.dynamic_slice_in_dim(own_rows, core * freq_half, freq_half, 0)
    copies = jnp.broadcast_to(own_half[None], (dev_count,) + own_half.shape)
    gathered = lax.all_to_all(copies, DEV, 0, 2, tiled=True)[0]
    grid_rows = lax.all_gather(gathered, "core", axis=0, tiled=True)
    factor = jnp.where(jnp.arange(M) == 0, 1.0, 2.0).astype(jnp.float32)
    squares = jnp.sum(grid_rows.astype(jnp.float32) ** 2 * factor[:, None, None], axis=0)
    cycle_power = squares[:, :Q] + squares[:, Q:]
    swapped = jnp.concatenate([weighted[:, Q:], -weighted[:, :Q]], 1)
    weighted, swapped, power_term = lax.optimization_barrier((weighted, swapped, power_term))
    rows = M
    width = classes_total * columns
    crossed_real = jnp.einsum(
        "mkc,mcb->mkb", grid_rows, weighted, preferred_element_type=jnp.float32
    ).astype(jnp.bfloat16).reshape(rows, width)
    crossed_imag = jnp.einsum(
        "mkc,mcb->mkb", grid_rows, swapped, preferred_element_type=jnp.float32
    ).astype(jnp.bfloat16).reshape(rows, width)
    penalty = jnp.dot(cycle_power, power_term, precision=lax.Precision.HIGHEST)
    bias = (class_prior[:, None] - 0.5 * penalty).reshape(1, width)
    table = jnp.transpose(score_table, (2, 0, 1)).reshape(R, 2 * M)
    turn = jnp.concatenate(
        [turn_table.reshape(2 * M, R), jnp.ones((1, R), jnp.bfloat16), jnp.zeros((15, R), jnp.bfloat16)], 0
    )

    block = CLS_STEP * columns
    steps = width // block
    table_spec = pl.BlockSpec((R, 2 * rows), lambda i: (0, 0))
    crossed_spec = pl.BlockSpec((rows, block), lambda i: (0, i))
    row_spec = pl.BlockSpec((1, block), lambda i: (0, i))
    log_norm = pl.pallas_call(
        functools.partial(norm_kernel, columns),
        grid=(steps,),
        in_specs=[table_spec, crossed_spec, crossed_spec, row_spec],
        out_specs=pl.BlockSpec((1, columns), lambda i: (0, 0)),
        out_shape=jax.ShapeDtypeStruct((1, columns), jnp.float32),
        scratch_shapes=[pltpu.VMEM((1, columns), jnp.float32)] * 2,
        compiler_params=pltpu.CompilerParams(dimension_semantics=("arbitrary",)),
    )(table, crossed_real, crossed_imag, bias)
    spectra, class_weight = pl.pallas_call(
        functools.partial(spectra_kernel, columns),
        grid=(steps,),
        in_specs=[
            table_spec,
            crossed_spec,
            crossed_spec,
            row_spec,
            pl.BlockSpec((1, columns), lambda i: (0, 0)),
            pl.BlockSpec(turn.shape, lambda i: (0, 0)),
        ],
        out_specs=[pl.BlockSpec((rows, 2 * block), lambda i: (0, i)), row_spec],
        out_shape=[
            jax.ShapeDtypeStruct((rows, 2 * width), jnp.bfloat16),
            jax.ShapeDtypeStruct((1, width), jnp.float32),
        ],
        compiler_params=pltpu.CompilerParams(dimension_semantics=("arbitrary",)),
    )(table, crossed_real, crossed_imag, bias, log_norm, turn)

    spectra = spectra.reshape(M, classes_total, 2 * columns)
    paired = jnp.concatenate([weighted, swapped], 2)
    numer_all = jnp.einsum("mkb,mcb->kmc", spectra, paired, preferred_element_type=jnp.float32)
    numer_all = numer_all.reshape(classes_total, 2 * M * Q)
    class_weight = class_weight.reshape(classes_total, columns)
    cycles_all = jnp.dot(class_weight, power_term.T, precision=lax.Precision.HIGHEST)
    mass_all = jnp.sum(class_weight, axis=1)

    width = numer_all.shape[1]
    packed = jnp.concatenate(
        [numer_all, cycles_all, mass_all[:, None], jnp.zeros((classes_total, 223), jnp.float32)], 1
    )
    core_count = lax.axis_size("core")
    half = packed.shape[1] // core_count
    mine = lax.dynamic_slice_in_dim(packed, core * half, half, 1)
    other = lax.dynamic_slice_in_dim(packed, (1 - core) * half, half, 1)
    packed = mine + lax.ppermute(other, "core", [(0, 1), (1, 0)])
    packed = packed.reshape(lax.axis_size("z"), lax.axis_size("y"), CLS_DEV, half)
    own = jnp.sum(lax.all_to_all(packed, "y", 1, 1, tiled=True), 1)
    own = jnp.sum(lax.all_to_all(own, "z", 0, 0, tiled=True), 0)
    own = lax.all_gather(own, GRP, axis=0, tiled=False)
    own = jnp.sum(own.reshape(lax.axis_size("x"), core_count, CLS_DEV, half), 0)
    own = jnp.concatenate([own[0], own[1]], 1)
    numerator = own[:, :width]
    cycle_sum = own[:, width : width + Q]
    class_mass = own[:, width + Q]
    new_references = (numerator.reshape(CLS_DEV, M, 2, Q) / cycle_sum[:, None, None, :]).reshape(
        CLS_DEV, 2 * M * Q
    )
    particle_total = columns * lax.axis_size(GRP) * lax.axis_size(DEV)
    occupancy = class_mass * (classes_total / particle_total)
    return (new_references, occupancy)


def solution(mesh):
    grp_count, dev_count = mesh.devices.shape
    core_count = 2
    y_count = 4
    split = jax.sharding.Mesh(
        mesh.devices.reshape(
            grp_count // core_count, core_count, dev_count // y_count, y_count
        ),
        GRP + DEV,
    )
    return jax.shard_map(
        local,
        mesh=split,
        in_specs=(P(DEV, None), P(None, GRP + DEV), P(GRP + DEV), P(), P(), P()),
        out_specs=(P(DEV, None), P(DEV)),
        check_vma=False,
    )
```

```python
import functools
import math

import jax
import jax.numpy as jnp
from jax import lax
from jax.experimental import pallas as pl
from jax.experimental.pallas import tpu as pltpu
from jax.sharding import PartitionSpec as P

Q = 32
M = 32
R = 128
CLS_DEV = 6
CLS_STEP = 48
GRP = ("x", "core")
DEV = ("z", "y")


def angle_tables(cycle_freqs, count_turns):
    freq_index = jnp.arange(cycle_freqs, dtype=jnp.int32)
    turn_index = jnp.arange(count_turns, dtype=jnp.int32)
    wrapped = freq_index[:, None] * turn_index[None, :] % count_turns
    phases = 2.0 * math.pi / count_turns * wrapped.astype(jnp.float32)
    factor = jnp.where(freq_index == 0, 1.0, 2.0).astype(jnp.float32)[:, None]
    cosine = jnp.cos(phases)
    sine_part = jnp.sin(phases)
    score_table = jnp.stack([factor * cosine, factor * sine_part], 0).astype(jnp.bfloat16)
    turn_table = jnp.stack([cosine, sine_part], 0).astype(jnp.bfloat16)
    return (score_table, turn_table)


def particle_terms(particles, defocus_bin, contrast_table, noise_power):
    columns = particles.shape[1]
    cycle_count = contrast_table.shape[1]
    freq_count = particles.shape[0] // (2 * cycle_count)
    onehot = (
        defocus_bin[None, :] == jnp.arange(contrast_table.shape[0], dtype=jnp.int32)[:, None]
    ).astype(jnp.float32)
    contrast = jnp.dot(contrast_table.T, onehot, precision=lax.Precision.HIGHEST)
    scaled = contrast / noise_power[:, None]
    power_term = contrast * scaled
    weighted = (
        particles.astype(jnp.float32).reshape(freq_count, 2, cycle_count, columns)
        * scaled[None, None]
    ).astype(jnp.bfloat16)
    return (weighted.reshape(freq_count, 2 * cycle_count, columns), power_term)


def block_scores(table_ref, real_ref, imag_ref, shift_ref):
    crossed = jnp.concatenate([real_ref[...], imag_ref[...]], 0)
    raw = jnp.dot(table_ref[...], crossed, preferred_element_type=jnp.float32)
    return raw + shift_ref[...]


def norm_kernel(cols, table_ref, real_ref, imag_ref, bias_ref, out_ref, top_ref, total_ref):
    step = pl.program_id(0)

    @pl.when(step == 0)
    def _():
        top_ref[...] = jnp.full(top_ref.shape, -1e30, jnp.float32)
        total_ref[...] = jnp.zeros(total_ref.shape, jnp.float32)

    scores = block_scores(table_ref, real_ref, imag_ref, bias_ref)
    parts = [scores[:, j * cols : (j + 1) * cols] for j in range(scores.shape[1] // cols)]
    block_top = functools.reduce(jnp.maximum, [jnp.max(s, axis=0, keepdims=True) for s in parts])
    old_top = top_ref[...]
    new_top = jnp.maximum(old_top, block_top)
    block_total = functools.reduce(
        jnp.add, [jnp.sum(jnp.exp(s - new_top), axis=0, keepdims=True) for s in parts]
    )
    total_ref[...] = total_ref[...] * jnp.exp(old_top - new_top) + block_total
    top_ref[...] = new_top

    @pl.when(step == pl.num_programs(0) - 1)
    def _():
        out_ref[...] = top_ref[...] + jnp.log(total_ref[...])


def spectra_kernel(
    cols, table_ref, real_ref, imag_ref, bias_ref, norm_ref, turn_ref, cos_ref, sin_ref, weight_ref
):
    norm_row = jnp.concatenate([norm_ref[...]] * (bias_ref.shape[1] // cols), 1)
    scores = block_scores(table_ref, real_ref, imag_ref, bias_ref)
    responsibility = jnp.exp(scores - norm_row)
    full = jnp.dot(
        turn_ref[...], responsibility.astype(jnp.bfloat16), preferred_element_type=jnp.float32
    )
    rows = cos_ref.shape[0]
    cos_ref[...] = full[:rows].astype(jnp.bfloat16)
    sin_ref[...] = full[rows : 2 * rows].astype(jnp.bfloat16)
    weight_ref[...] = full[2 * rows : 2 * rows + 1]


def local(references, particles, defocus_bin, contrast_table, noise_power, class_prior):
    weighted, power_term = particle_terms(particles, defocus_bin, contrast_table, noise_power)
    score_table, turn_table = angle_tables(M, R)
    columns = particles.shape[1]
    dev_count = lax.axis_size(DEV)
    classes_total = CLS_DEV * dev_count

    core = lax.axis_index("core")
    own_rows = jnp.transpose(references.reshape(CLS_DEV, M, 2 * Q), (1, 0, 2))
    freq_half = M // 2
    own_half = lax.dynamic_slice_in_dim(own_rows, core * freq_half, freq_half, 0)
    copies = jnp.broadcast_to(own_half[None], (dev_count,) + own_half.shape)
    gathered = lax.all_to_all(copies, DEV, 0, 2, tiled=True)[0]
    grid_rows = lax.all_gather(gathered, "core", axis=0, tiled=True)
    factor = jnp.where(jnp.arange(M) == 0, 1.0, 2.0).astype(jnp.float32)
    squares = jnp.sum(grid_rows.astype(jnp.float32) ** 2 * factor[:, None, None], axis=0)
    cycle_power = squares[:, :Q] + squares[:, Q:]
    swapped = jnp.concatenate([weighted[:, Q:], -weighted[:, :Q]], 1)
    weighted, swapped, power_term = lax.optimization_barrier((weighted, swapped, power_term))
    rows = M
    width = classes_total * columns
    crossed_real = jnp.einsum(
        "mkc,mcb->mkb", grid_rows, weighted, preferred_element_type=jnp.float32
    ).astype(jnp.bfloat16).reshape(rows, width)
    crossed_imag = jnp.einsum(
        "mkc,mcb->mkb", grid_rows, swapped, preferred_element_type=jnp.float32
    ).astype(jnp.bfloat16).reshape(rows, width)
    penalty = jnp.dot(cycle_power, power_term, precision=lax.Precision.HIGHEST)
    bias = (class_prior[:, None] - 0.5 * penalty).reshape(1, width)
    table = jnp.transpose(score_table, (2, 0, 1)).reshape(R, 2 * M)
    turn = jnp.concatenate(
        [turn_table.reshape(2 * M, R), jnp.ones((1, R), jnp.bfloat16), jnp.zeros((15, R), jnp.bfloat16)], 0
    )

    block = CLS_STEP * columns
    steps = width // block
    table_spec = pl.BlockSpec((R, 2 * rows), lambda i: (0, 0))
    crossed_spec = pl.BlockSpec((rows, block), lambda i: (0, i))
    row_spec = pl.BlockSpec((1, block), lambda i: (0, i))
    log_norm = pl.pallas_call(
        functools.partial(norm_kernel, columns),
        grid=(steps,),
        in_specs=[table_spec, crossed_spec, crossed_spec, row_spec],
        out_specs=pl.BlockSpec((1, columns), lambda i: (0, 0)),
        out_shape=jax.ShapeDtypeStruct((1, columns), jnp.float32),
        scratch_shapes=[pltpu.VMEM((1, columns), jnp.float32)] * 2,
        compiler_params=pltpu.CompilerParams(dimension_semantics=("arbitrary",)),
    )(table, crossed_real, crossed_imag, bias)
    spectra_cos, spectra_sin, class_weight = pl.pallas_call(
        functools.partial(spectra_kernel, columns),
        grid=(steps,),
        in_specs=[
            table_spec,
            crossed_spec,
            crossed_spec,
            row_spec,
            pl.BlockSpec((1, columns), lambda i: (0, 0)),
            pl.BlockSpec(turn.shape, lambda i: (0, 0)),
        ],
        out_specs=[crossed_spec, crossed_spec, row_spec],
        out_shape=[
            jax.ShapeDtypeStruct((rows, width), jnp.bfloat16),
            jax.ShapeDtypeStruct((rows, width), jnp.bfloat16),
            jax.ShapeDtypeStruct((1, width), jnp.float32),
        ],
        compiler_params=pltpu.CompilerParams(dimension_semantics=("arbitrary",)),
    )(table, crossed_real, crossed_imag, bias, log_norm, turn)

    spectra_cos = spectra_cos.reshape(M, classes_total, columns)
    spectra_sin = spectra_sin.reshape(M, classes_total, columns)
    numer_all = jnp.einsum(
        "mkb,mcb->kmc", spectra_cos, weighted, preferred_element_type=jnp.float32
    ) + jnp.einsum("mkb,mcb->kmc", spectra_sin, swapped, preferred_element_type=jnp.float32)
    numer_all = numer_all.reshape(classes_total, 2 * M * Q)
    class_weight = class_weight.reshape(classes_total, columns)
    cycles_all = jnp.dot(class_weight, power_term.T, precision=lax.Precision.HIGHEST)
    mass_all = jnp.sum(class_weight, axis=1)

    width = numer_all.shape[1]
    packed = jnp.concatenate(
        [numer_all, cycles_all, mass_all[:, None], jnp.zeros((classes_total, 223), jnp.float32)], 1
    )
    core_count = lax.axis_size("core")
    half = packed.shape[1] // core_count
    mine = lax.dynamic_slice_in_dim(packed, core * half, half, 1)
    other = lax.dynamic_slice_in_dim(packed, (1 - core) * half, half, 1)
    packed = mine + lax.ppermute(other, "core", [(0, 1), (1, 0)])
    packed = packed.reshape(lax.axis_size("z"), lax.axis_size("y"), CLS_DEV, half)
    own = jnp.sum(lax.all_to_all(packed, "y", 1, 1, tiled=True), 1)
    own = jnp.sum(lax.all_to_all(own, "z", 0, 0, tiled=True), 0)
    own = jnp.sum(lax.all_gather(own, "x", axis=0, tiled=False), 0)
    own = lax.all_gather(own, "core", axis=1, tiled=True)
    numerator = own[:, :width]
    cycle_sum = own[:, width : width + Q]
    class_mass = own[:, width + Q]
    new_references = (numerator.reshape(CLS_DEV, M, 2, Q) / cycle_sum[:, None, None, :]).reshape(
        CLS_DEV, 2 * M * Q
    )
    particle_total = columns * lax.axis_size(GRP) * lax.axis_size(DEV)
    occupancy = class_mass * (classes_total / particle_total)
    return (new_references, occupancy)


def solution(mesh):
    grp_count, dev_count = mesh.devices.shape
    core_count = 2
    y_count = 4
    split = jax.sharding.Mesh(
        mesh.devices.reshape(
            grp_count // core_count, core_count, dev_count // y_count, y_count
        ),
        GRP + DEV,
    )
    return jax.shard_map(
        local,
        mesh=split,
        in_specs=(P(DEV, None), P(None, GRP + DEV), P(GRP + DEV), P(), P(), P()),
        out_specs=(P(DEV, None), P(DEV)),
        check_vma=False,
    )
```

```python
import functools
import math

import jax
import jax.numpy as jnp
from jax import lax
from jax.experimental import pallas as pl
from jax.experimental.pallas import tpu as pltpu
from jax.sharding import PartitionSpec as P

Q = 32
M = 32
R = 128
CLS_DEV = 6
CLS_STEP = 96
GRP = ("x", "core")
DEV = ("z", "y")


def angle_tables(cycle_freqs, count_turns):
    freq_index = jnp.arange(cycle_freqs, dtype=jnp.int32)
    turn_index = jnp.arange(count_turns, dtype=jnp.int32)
    wrapped = freq_index[:, None] * turn_index[None, :] % count_turns
    phases = 2.0 * math.pi / count_turns * wrapped.astype(jnp.float32)
    factor = jnp.where(freq_index == 0, 1.0, 2.0).astype(jnp.float32)[:, None]
    cosine = jnp.cos(phases)
    sine_part = jnp.sin(phases)
    score_table = jnp.stack([factor * cosine, factor * sine_part], 0).astype(jnp.bfloat16)
    turn_table = jnp.stack([cosine, sine_part], 0).astype(jnp.bfloat16)
    return (score_table, turn_table)


def particle_terms(particles, defocus_bin, contrast_table, noise_power):
    columns = particles.shape[1]
    cycle_count = contrast_table.shape[1]
    freq_count = particles.shape[0] // (2 * cycle_count)
    onehot = (
        defocus_bin[None, :] == jnp.arange(contrast_table.shape[0], dtype=jnp.int32)[:, None]
    ).astype(jnp.float32)
    contrast = jnp.dot(contrast_table.T, onehot, precision=lax.Precision.HIGHEST)
    scaled = contrast / noise_power[:, None]
    power_term = contrast * scaled
    weighted = (
        particles.astype(jnp.float32).reshape(freq_count, 2, cycle_count, columns)
        * scaled[None, None]
    ).astype(jnp.bfloat16)
    return (weighted.reshape(freq_count, 2 * cycle_count, columns), power_term)


def block_scores(table_ref, real_ref, imag_ref, shift_ref):
    crossed = jnp.concatenate([real_ref[...], imag_ref[...]], 0)
    raw = jnp.dot(table_ref[...], crossed, preferred_element_type=jnp.float32)
    return raw + shift_ref[...]


def norm_kernel(cols, table_ref, real_ref, imag_ref, bias_ref, out_ref, top_ref, total_ref):
    step = pl.program_id(0)

    @pl.when(step == 0)
    def _():
        top_ref[...] = jnp.full(top_ref.shape, -1e30, jnp.float32)
        total_ref[...] = jnp.zeros(total_ref.shape, jnp.float32)

    scores = block_scores(table_ref, real_ref, imag_ref, bias_ref)
    parts = [scores[:, j * cols : (j + 1) * cols] for j in range(scores.shape[1] // cols)]
    block_top = functools.reduce(jnp.maximum, [jnp.max(s, axis=0, keepdims=True) for s in parts])
    old_top = top_ref[...]
    new_top = jnp.maximum(old_top, block_top)
    block_total = functools.reduce(
        jnp.add, [jnp.sum(jnp.exp(s - new_top), axis=0, keepdims=True) for s in parts]
    )
    total_ref[...] = total_ref[...] * jnp.exp(old_top - new_top) + block_total
    top_ref[...] = new_top

    @pl.when(step == pl.num_programs(0) - 1)
    def _():
        out_ref[...] = top_ref[...] + jnp.log(total_ref[...])


def spectra_kernel(
    cols, table_ref, real_ref, imag_ref, bias_ref, norm_ref, turn_ref, cos_ref, sin_ref, weight_ref
):
    norm_row = jnp.concatenate([norm_ref[...]] * (bias_ref.shape[1] // cols), 1)
    scores = block_scores(table_ref, real_ref, imag_ref, bias_ref)
    responsibility = jnp.exp(scores - norm_row)
    full = jnp.dot(
        turn_ref[...], responsibility.astype(jnp.bfloat16), preferred_element_type=jnp.float32
    )
    rows = cos_ref.shape[0]
    cos_ref[...] = full[:rows].astype(jnp.bfloat16)
    sin_ref[...] = full[rows : 2 * rows].astype(jnp.bfloat16)
    weight_ref[...] = full[2 * rows : 2 * rows + 1]


def local(references, particles, defocus_bin, contrast_table, noise_power, class_prior):
    weighted, power_term = particle_terms(particles, defocus_bin, contrast_table, noise_power)
    score_table, turn_table = angle_tables(M, R)
    columns = particles.shape[1]
    dev_count = lax.axis_size(DEV)
    classes_total = CLS_DEV * dev_count

    core = lax.axis_index("core")
    own_rows = jnp.transpose(references.reshape(CLS_DEV, M, 2 * Q), (1, 0, 2))
    freq_half = M // 2
    own_half = lax.dynamic_slice_in_dim(own_rows, core * freq_half, freq_half, 0)
    copies = jnp.broadcast_to(own_half[None], (dev_count,) + own_half.shape)
    gathered = lax.all_to_all(copies, DEV, 0, 2, tiled=True)[0]
    grid_rows = lax.all_gather(gathered, "core", axis=0, tiled=True)
    factor = jnp.where(jnp.arange(M) == 0, 1.0, 2.0).astype(jnp.float32)
    squares = jnp.sum(grid_rows.astype(jnp.float32) ** 2 * factor[:, None, None], axis=0)
    cycle_power = squares[:, :Q] + squares[:, Q:]
    swapped = jnp.concatenate([weighted[:, Q:], -weighted[:, :Q]], 1)
    weighted, swapped, power_term = lax.optimization_barrier((weighted, swapped, power_term))
    rows = M
    width = classes_total * columns
    crossed_real = jnp.einsum(
        "mkc,mcb->mkb", grid_rows, weighted, preferred_element_type=jnp.float32
    ).astype(jnp.bfloat16).reshape(rows, width)
    crossed_imag = jnp.einsum(
        "mkc,mcb->mkb", grid_rows, swapped, preferred_element_type=jnp.float32
    ).astype(jnp.bfloat16).reshape(rows, width)
    penalty = jnp.dot(cycle_power, power_term, precision=lax.Precision.HIGHEST)
    bias = (class_prior[:, None] - 0.5 * penalty).reshape(1, width)
    table = jnp.transpose(score_table, (2, 0, 1)).reshape(R, 2 * M)
    turn = jnp.concatenate(
        [turn_table.reshape(2 * M, R), jnp.ones((1, R), jnp.bfloat16), jnp.zeros((15, R), jnp.bfloat16)], 0
    )

    block = CLS_STEP * columns
    steps = width // block
    table_spec = pl.BlockSpec((R, 2 * rows), lambda i: (0, 0))
    crossed_spec = pl.BlockSpec((rows, block), lambda i: (0, i))
    row_spec = pl.BlockSpec((1, block), lambda i: (0, i))
    log_norm = pl.pallas_call(
        functools.partial(norm_kernel, columns),
        grid=(steps,),
        in_specs=[table_spec, crossed_spec, crossed_spec, row_spec],
        out_specs=pl.BlockSpec((1, columns), lambda i: (0, 0)),
        out_shape=jax.ShapeDtypeStruct((1, columns), jnp.float32),
        scratch_shapes=[pltpu.VMEM((1, columns), jnp.float32)] * 2,
        compiler_params=pltpu.CompilerParams(dimension_semantics=("arbitrary",)),
    )(table, crossed_real, crossed_imag, bias)
    spectra_cos, spectra_sin, class_weight = pl.pallas_call(
        functools.partial(spectra_kernel, columns),
        grid=(steps,),
        in_specs=[
            table_spec,
            crossed_spec,
            crossed_spec,
            row_spec,
            pl.BlockSpec((1, columns), lambda i: (0, 0)),
            pl.BlockSpec(turn.shape, lambda i: (0, 0)),
        ],
        out_specs=[crossed_spec, crossed_spec, row_spec],
        out_shape=[
            jax.ShapeDtypeStruct((rows, width), jnp.bfloat16),
            jax.ShapeDtypeStruct((rows, width), jnp.bfloat16),
            jax.ShapeDtypeStruct((1, width), jnp.float32),
        ],
        compiler_params=pltpu.CompilerParams(dimension_semantics=("arbitrary",)),
    )(table, crossed_real, crossed_imag, bias, log_norm, turn)

    spectra_cos = spectra_cos.reshape(M, classes_total, columns)
    spectra_sin = spectra_sin.reshape(M, classes_total, columns)
    numer_all = jnp.einsum(
        "mkb,mcb->kmc", spectra_cos, weighted, preferred_element_type=jnp.float32
    ) + jnp.einsum("mkb,mcb->kmc", spectra_sin, swapped, preferred_element_type=jnp.float32)
    numer_all = numer_all.reshape(classes_total, 2 * M * Q)
    class_weight = class_weight.reshape(classes_total, columns)
    cycles_all = jnp.dot(class_weight, power_term.T, precision=lax.Precision.HIGHEST)
    mass_all = jnp.sum(class_weight, axis=1)

    width = numer_all.shape[1]
    packed = jnp.concatenate(
        [numer_all, cycles_all, mass_all[:, None], jnp.zeros((classes_total, 223), jnp.float32)], 1
    )
    core_count = lax.axis_size("core")
    half = packed.shape[1] // core_count
    mine = lax.dynamic_slice_in_dim(packed, core * half, half, 1)
    other = lax.dynamic_slice_in_dim(packed, (1 - core) * half, half, 1)
    packed = mine + lax.ppermute(other, "core", [(0, 1), (1, 0)])
    packed = packed.reshape(lax.axis_size("z"), lax.axis_size("y"), CLS_DEV, half)
    own = jnp.sum(lax.all_to_all(packed, "y", 1, 1, tiled=True), 1)
    own = jnp.sum(lax.all_to_all(own, "z", 0, 0, tiled=True), 0)
    own = lax.all_gather(own, GRP, axis=0, tiled=False)
    own = jnp.sum(own.reshape(lax.axis_size("x"), core_count, CLS_DEV, half), 0)
    own = jnp.concatenate([own[0], own[1]], 1)
    numerator = own[:, :width]
    cycle_sum = own[:, width : width + Q]
    class_mass = own[:, width + Q]
    new_references = (numerator.reshape(CLS_DEV, M, 2, Q) / cycle_sum[:, None, None, :]).reshape(
        CLS_DEV, 2 * M * Q
    )
    particle_total = columns * lax.axis_size(GRP) * lax.axis_size(DEV)
    occupancy = class_mass * (classes_total / particle_total)
    return (new_references, occupancy)


def solution(mesh):
    grp_count, dev_count = mesh.devices.shape
    core_count = 2
    y_count = 4
    split = jax.sharding.Mesh(
        mesh.devices.reshape(
            grp_count // core_count, core_count, dev_count // y_count, y_count
        ),
        GRP + DEV,
    )
    return jax.shard_map(
        local,
        mesh=split,
        in_specs=(P(DEV, None), P(None, GRP + DEV), P(GRP + DEV), P(), P(), P()),
        out_specs=(P(DEV, None), P(DEV)),
        check_vma=False,
    )
```

```python
import functools
import math

import jax
import jax.numpy as jnp
from jax import lax
from jax.experimental import pallas as pl
from jax.experimental.pallas import tpu as pltpu
from jax.sharding import PartitionSpec as P

Q = 32
M = 32
R = 128
CLS_DEV = 6
CLS_STEP = 48
GRP = ("x", "core")
DEV = ("z", "y")


def angle_tables(cycle_freqs, count_turns):
    freq_index = jnp.arange(cycle_freqs, dtype=jnp.int32)
    turn_index = jnp.arange(count_turns, dtype=jnp.int32)
    wrapped = freq_index[:, None] * turn_index[None, :] % count_turns
    phases = 2.0 * math.pi / count_turns * wrapped.astype(jnp.float32)
    factor = jnp.where(freq_index == 0, 1.0, 2.0).astype(jnp.float32)[:, None]
    cosine = jnp.cos(phases)
    sine_part = jnp.sin(phases)
    score_table = jnp.stack([factor * cosine, factor * sine_part], 0).astype(jnp.bfloat16)
    turn_table = jnp.stack([cosine, sine_part], 0).astype(jnp.bfloat16)
    return (score_table, turn_table)


def particle_terms(particles, defocus_bin, contrast_table, noise_power):
    columns = particles.shape[1]
    cycle_count = contrast_table.shape[1]
    freq_count = particles.shape[0] // (2 * cycle_count)
    onehot = (
        defocus_bin[None, :] == jnp.arange(contrast_table.shape[0], dtype=jnp.int32)[:, None]
    ).astype(jnp.float32)
    contrast = jnp.dot(contrast_table.T, onehot, precision=lax.Precision.HIGHEST)
    scaled = contrast / noise_power[:, None]
    power_term = contrast * scaled
    weighted = (
        particles.astype(jnp.float32).reshape(freq_count, 2, cycle_count, columns)
        * scaled[None, None]
    ).astype(jnp.bfloat16)
    return (weighted.reshape(freq_count, 2 * cycle_count, columns), power_term)


def block_scores(table_ref, real_ref, imag_ref, shift_ref):
    crossed = jnp.concatenate([real_ref[...], imag_ref[...]], 0)
    raw = jnp.dot(table_ref[...], crossed, preferred_element_type=jnp.float32)
    return raw + shift_ref[...]


def norm_kernel(cols, table_ref, real_ref, imag_ref, bias_ref, out_ref, top_ref, total_ref):
    step = pl.program_id(0)

    @pl.when(step == 0)
    def _():
        top_ref[...] = jnp.full(top_ref.shape, -1e30, jnp.float32)
        total_ref[...] = jnp.zeros(total_ref.shape, jnp.float32)

    scores = block_scores(table_ref, real_ref, imag_ref, bias_ref)
    parts = [scores[:, j * cols : (j + 1) * cols] for j in range(scores.shape[1] // cols)]
    block_top = functools.reduce(jnp.maximum, [jnp.max(s, axis=0, keepdims=True) for s in parts])
    old_top = top_ref[...]
    new_top = jnp.maximum(old_top, block_top)
    block_total = functools.reduce(
        jnp.add, [jnp.sum(jnp.exp(s - new_top), axis=0, keepdims=True) for s in parts]
    )
    total_ref[...] = total_ref[...] * jnp.exp(old_top - new_top) + block_total
    top_ref[...] = new_top

    @pl.when(step == pl.num_programs(0) - 1)
    def _():
        out_ref[...] = top_ref[...] + jnp.log(total_ref[...])


def spectra_kernel(
    cols, table_ref, real_ref, imag_ref, bias_ref, norm_ref, turn_ref, cos_ref, sin_ref, weight_ref
):
    norm_row = jnp.concatenate([norm_ref[...]] * (bias_ref.shape[1] // cols), 1)
    scores = block_scores(table_ref, real_ref, imag_ref, bias_ref)
    responsibility = jnp.exp(scores - norm_row)
    full = jnp.dot(
        turn_ref[...], responsibility.astype(jnp.bfloat16), preferred_element_type=jnp.float32
    )
    rows = cos_ref.shape[0]
    cos_ref[...] = full[:rows].astype(jnp.bfloat16)
    sin_ref[...] = full[rows : 2 * rows].astype(jnp.bfloat16)
    weight_ref[...] = full[2 * rows : 2 * rows + 1]


def local(references, particles, defocus_bin, contrast_table, noise_power, class_prior):
    weighted, power_term = particle_terms(particles, defocus_bin, contrast_table, noise_power)
    score_table, turn_table = angle_tables(M, R)
    columns = particles.shape[1]
    dev_count = lax.axis_size(DEV)
    classes_total = CLS_DEV * dev_count

    core = lax.axis_index("core")
    own_rows = jnp.transpose(references.reshape(CLS_DEV, M, 2 * Q), (1, 0, 2))
    freq_half = M // 2
    own_half = lax.dynamic_slice_in_dim(own_rows, core * freq_half, freq_half, 0)
    copies = jnp.broadcast_to(own_half[None], (dev_count,) + own_half.shape)
    gathered = lax.all_to_all(copies, DEV, 0, 2, tiled=True)[0]
    grid_rows = lax.all_gather(gathered, "core", axis=0, tiled=True)
    factor = jnp.where(jnp.arange(M) == 0, 1.0, 2.0).astype(jnp.float32)
    squares = jnp.sum(grid_rows.astype(jnp.float32) ** 2 * factor[:, None, None], axis=0)
    cycle_power = squares[:, :Q] + squares[:, Q:]
    swapped = jnp.concatenate([weighted[:, Q:], -weighted[:, :Q]], 1)
    weighted, swapped, power_term = lax.optimization_barrier((weighted, swapped, power_term))
    rows = M
    width = classes_total * columns
    crossed_real = jnp.einsum(
        "mkc,mcb->mkb", grid_rows, weighted, preferred_element_type=jnp.float32
    ).astype(jnp.bfloat16).reshape(rows, width)
    crossed_imag = jnp.einsum(
        "mkc,mcb->mkb", grid_rows, swapped, preferred_element_type=jnp.float32
    ).astype(jnp.bfloat16).reshape(rows, width)
    penalty = jnp.dot(cycle_power, power_term, precision=lax.Precision.HIGHEST)
    bias = (class_prior[:, None] - 0.5 * penalty).reshape(1, width)
    table = jnp.transpose(score_table, (2, 0, 1)).reshape(R, 2 * M)
    turn = jnp.concatenate(
        [turn_table.reshape(2 * M, R), jnp.ones((1, R), jnp.bfloat16), jnp.zeros((15, R), jnp.bfloat16)], 0
    )

    block = CLS_STEP * columns
    steps = width // block
    table_spec = pl.BlockSpec((R, 2 * rows), lambda i: (0, 0))
    crossed_spec = pl.BlockSpec((rows, block), lambda i: (0, i))
    row_spec = pl.BlockSpec((1, block), lambda i: (0, i))
    log_norm = pl.pallas_call(
        functools.partial(norm_kernel, columns),
        grid=(steps,),
        in_specs=[table_spec, crossed_spec, crossed_spec, row_spec],
        out_specs=pl.BlockSpec((1, columns), lambda i: (0, 0)),
        out_shape=jax.ShapeDtypeStruct((1, columns), jnp.float32),
        scratch_shapes=[pltpu.VMEM((1, columns), jnp.float32)] * 2,
        compiler_params=pltpu.CompilerParams(dimension_semantics=("arbitrary",)),
    )(table, crossed_real, crossed_imag, bias)
    spectra_cos, spectra_sin, class_weight = pl.pallas_call(
        functools.partial(spectra_kernel, columns),
        grid=(steps,),
        in_specs=[
            table_spec,
            crossed_spec,
            crossed_spec,
            row_spec,
            pl.BlockSpec((1, columns), lambda i: (0, 0)),
            pl.BlockSpec(turn.shape, lambda i: (0, 0)),
        ],
        out_specs=[crossed_spec, crossed_spec, row_spec],
        out_shape=[
            jax.ShapeDtypeStruct((rows, width), jnp.bfloat16),
            jax.ShapeDtypeStruct((rows, width), jnp.bfloat16),
            jax.ShapeDtypeStruct((1, width), jnp.float32),
        ],
        compiler_params=pltpu.CompilerParams(dimension_semantics=("arbitrary",)),
    )(table, crossed_real, crossed_imag, bias, log_norm, turn)

    spectra_cos = spectra_cos.reshape(M, classes_total, columns)
    spectra_sin = spectra_sin.reshape(M, classes_total, columns)
    numer_all = jnp.einsum(
        "mkb,mcb->kmc", spectra_cos, weighted, preferred_element_type=jnp.float32
    ) + jnp.einsum("mkb,mcb->kmc", spectra_sin, swapped, preferred_element_type=jnp.float32)
    numer_all = numer_all.reshape(classes_total, 2 * M * Q)
    class_weight = class_weight.reshape(classes_total, columns)
    cycles_all = jnp.dot(class_weight, power_term.T, precision=lax.Precision.HIGHEST)
    mass_all = jnp.sum(class_weight, axis=1)

    width = numer_all.shape[1]
    packed = jnp.concatenate(
        [numer_all, cycles_all, mass_all[:, None], jnp.zeros((classes_total, 223), jnp.float32)], 1
    )
    core_count = lax.axis_size("core")
    half = packed.shape[1] // core_count
    paired = lax.all_to_all(packed.reshape(classes_total, core_count, half), "core", 1, 1, tiled=True)
    packed = jnp.sum(paired, 1)
    packed = packed.reshape(lax.axis_size("z"), lax.axis_size("y"), CLS_DEV, half)
    own = jnp.sum(lax.all_to_all(packed, "y", 1, 1, tiled=True), 1)
    own = jnp.sum(lax.all_to_all(own, "z", 0, 0, tiled=True), 0)
    own = lax.all_gather(own, GRP, axis=0, tiled=False)
    own = jnp.sum(own.reshape(lax.axis_size("x"), core_count, CLS_DEV, half), 0)
    own = jnp.concatenate([own[0], own[1]], 1)
    numerator = own[:, :width]
    cycle_sum = own[:, width : width + Q]
    class_mass = own[:, width + Q]
    new_references = (numerator.reshape(CLS_DEV, M, 2, Q) / cycle_sum[:, None, None, :]).reshape(
        CLS_DEV, 2 * M * Q
    )
    particle_total = columns * lax.axis_size(GRP) * lax.axis_size(DEV)
    occupancy = class_mass * (classes_total / particle_total)
    return (new_references, occupancy)


def solution(mesh):
    grp_count, dev_count = mesh.devices.shape
    core_count = 2
    y_count = 4
    split = jax.sharding.Mesh(
        mesh.devices.reshape(
            grp_count // core_count, core_count, dev_count // y_count, y_count
        ),
        GRP + DEV,
    )
    return jax.shard_map(
        local,
        mesh=split,
        in_specs=(P(DEV, None), P(None, GRP + DEV), P(GRP + DEV), P(), P(), P()),
        out_specs=(P(DEV, None), P(DEV)),
        check_vma=False,
    )
```

```python
import functools
import math

import jax
import jax.numpy as jnp
from jax import lax
from jax.experimental import pallas as pl
from jax.experimental.pallas import tpu as pltpu
from jax.sharding import PartitionSpec as P

Q = 32
M = 32
R = 128
CLS_DEV = 6
CLS_STEP = 64
GRP = ("x", "core")
DEV = ("z", "y")


def angle_tables(cycle_freqs, count_turns):
    freq_index = jnp.arange(cycle_freqs, dtype=jnp.int32)
    turn_index = jnp.arange(count_turns, dtype=jnp.int32)
    wrapped = freq_index[:, None] * turn_index[None, :] % count_turns
    phases = 2.0 * math.pi / count_turns * wrapped.astype(jnp.float32)
    factor = jnp.where(freq_index == 0, 1.0, 2.0).astype(jnp.float32)[:, None]
    cosine = jnp.cos(phases)
    sine_part = jnp.sin(phases)
    score_table = jnp.stack([factor * cosine, factor * sine_part], 0).astype(jnp.bfloat16)
    turn_table = jnp.stack([cosine, sine_part], 0).astype(jnp.bfloat16)
    return (score_table, turn_table)


def particle_terms(particles, defocus_bin, contrast_table, noise_power):
    columns = particles.shape[1]
    cycle_count = contrast_table.shape[1]
    freq_count = particles.shape[0] // (2 * cycle_count)
    onehot = (
        defocus_bin[None, :] == jnp.arange(contrast_table.shape[0], dtype=jnp.int32)[:, None]
    ).astype(jnp.float32)
    contrast = jnp.dot(contrast_table.T, onehot, precision=lax.Precision.HIGHEST)
    scaled = contrast / noise_power[:, None]
    power_term = contrast * scaled
    weighted = (
        particles.astype(jnp.float32).reshape(freq_count, 2, cycle_count, columns)
        * scaled[None, None]
    ).astype(jnp.bfloat16)
    return (weighted.reshape(freq_count, 2 * cycle_count, columns), power_term)


def block_scores(table_ref, real_ref, imag_ref, shift_ref):
    crossed = jnp.concatenate([real_ref[...], imag_ref[...]], 0)
    raw = jnp.dot(table_ref[...], crossed, preferred_element_type=jnp.float32)
    return raw + shift_ref[...]


def norm_kernel(cols, table_ref, real_ref, imag_ref, bias_ref, out_ref, top_ref, total_ref):
    step = pl.program_id(0)

    @pl.when(step == 0)
    def _():
        top_ref[...] = jnp.full(top_ref.shape, -1e30, jnp.float32)
        total_ref[...] = jnp.zeros(total_ref.shape, jnp.float32)

    scores = block_scores(table_ref, real_ref, imag_ref, bias_ref)
    parts = [scores[:, j * cols : (j + 1) * cols] for j in range(scores.shape[1] // cols)]
    block_top = functools.reduce(jnp.maximum, [jnp.max(s, axis=0, keepdims=True) for s in parts])
    old_top = top_ref[...]
    new_top = jnp.maximum(old_top, block_top)
    block_total = functools.reduce(
        jnp.add, [jnp.sum(jnp.exp(s - new_top), axis=0, keepdims=True) for s in parts]
    )
    total_ref[...] = total_ref[...] * jnp.exp(old_top - new_top) + block_total
    top_ref[...] = new_top

    @pl.when(step == pl.num_programs(0) - 1)
    def _():
        out_ref[...] = top_ref[...] + jnp.log(total_ref[...])


def spectra_kernel(
    cols, table_ref, real_ref, imag_ref, bias_ref, norm_ref, turn_ref, cos_ref, sin_ref, weight_ref
):
    norm_row = jnp.concatenate([norm_ref[...]] * (bias_ref.shape[1] // cols), 1)
    scores = block_scores(table_ref, real_ref, imag_ref, bias_ref)
    responsibility = jnp.exp(scores - norm_row)
    full = jnp.dot(
        turn_ref[...], responsibility.astype(jnp.bfloat16), preferred_element_type=jnp.float32
    )
    rows = cos_ref.shape[0]
    cos_ref[...] = full[:rows].astype(jnp.bfloat16)
    sin_ref[...] = full[rows : 2 * rows].astype(jnp.bfloat16)
    weight_ref[...] = full[2 * rows : 2 * rows + 1]


def local(references, particles, defocus_bin, contrast_table, noise_power, class_prior):
    weighted, power_term = particle_terms(particles, defocus_bin, contrast_table, noise_power)
    score_table, turn_table = angle_tables(M, R)
    columns = particles.shape[1]
    dev_count = lax.axis_size(DEV)
    classes_total = CLS_DEV * dev_count

    core = lax.axis_index("core")
    own_rows = jnp.transpose(references.reshape(CLS_DEV, M, 2 * Q), (1, 0, 2))
    freq_half = M // 2
    own_half = lax.dynamic_slice_in_dim(own_rows, core * freq_half, freq_half, 0)
    copies = jnp.broadcast_to(own_half[None], (dev_count,) + own_half.shape)
    gathered = lax.all_to_all(copies, DEV, 0, 2, tiled=True)[0]
    grid_rows = lax.all_gather(gathered, "core", axis=0, tiled=True)
    factor = jnp.where(jnp.arange(M) == 0, 1.0, 2.0).astype(jnp.float32)
    squares = jnp.sum(grid_rows.astype(jnp.float32) ** 2 * factor[:, None, None], axis=0)
    cycle_power = squares[:, :Q] + squares[:, Q:]
    swapped = jnp.concatenate([weighted[:, Q:], -weighted[:, :Q]], 1)
    weighted, swapped, power_term = lax.optimization_barrier((weighted, swapped, power_term))
    rows = M
    width = classes_total * columns
    crossed_real = jnp.einsum(
        "mkc,mcb->mkb", grid_rows, weighted, preferred_element_type=jnp.float32
    ).astype(jnp.bfloat16).reshape(rows, width)
    crossed_imag = jnp.einsum(
        "mkc,mcb->mkb", grid_rows, swapped, preferred_element_type=jnp.float32
    ).astype(jnp.bfloat16).reshape(rows, width)
    penalty = jnp.dot(cycle_power, power_term, precision=lax.Precision.HIGHEST)
    bias = (class_prior[:, None] - 0.5 * penalty).reshape(1, width)
    table = jnp.transpose(score_table, (2, 0, 1)).reshape(R, 2 * M)
    turn = jnp.concatenate(
        [turn_table.reshape(2 * M, R), jnp.ones((1, R), jnp.bfloat16), jnp.zeros((15, R), jnp.bfloat16)], 0
    )

    block = CLS_STEP * columns
    steps = width // block
    table_spec = pl.BlockSpec((R, 2 * rows), lambda i: (0, 0))
    crossed_spec = pl.BlockSpec((rows, block), lambda i: (0, i))
    row_spec = pl.BlockSpec((1, block), lambda i: (0, i))
    log_norm = pl.pallas_call(
        functools.partial(norm_kernel, columns),
        grid=(steps,),
        in_specs=[table_spec, crossed_spec, crossed_spec, row_spec],
        out_specs=pl.BlockSpec((1, columns), lambda i: (0, 0)),
        out_shape=jax.ShapeDtypeStruct((1, columns), jnp.float32),
        scratch_shapes=[pltpu.VMEM((1, columns), jnp.float32)] * 2,
        compiler_params=pltpu.CompilerParams(dimension_semantics=("arbitrary",)),
    )(table, crossed_real, crossed_imag, bias)
    spectra_cos, spectra_sin, class_weight = pl.pallas_call(
        functools.partial(spectra_kernel, columns),
        grid=(steps,),
        in_specs=[
            table_spec,
            crossed_spec,
            crossed_spec,
            row_spec,
            pl.BlockSpec((1, columns), lambda i: (0, 0)),
            pl.BlockSpec(turn.shape, lambda i: (0, 0)),
        ],
        out_specs=[crossed_spec, crossed_spec, row_spec],
        out_shape=[
            jax.ShapeDtypeStruct((rows, width), jnp.bfloat16),
            jax.ShapeDtypeStruct((rows, width), jnp.bfloat16),
            jax.ShapeDtypeStruct((1, width), jnp.float32),
        ],
        compiler_params=pltpu.CompilerParams(dimension_semantics=("arbitrary",)),
    )(table, crossed_real, crossed_imag, bias, log_norm, turn)

    spectra_cos = spectra_cos.reshape(M, classes_total, columns)
    spectra_sin = spectra_sin.reshape(M, classes_total, columns)
    numer_all = jnp.einsum(
        "mkb,mcb->kmc", spectra_cos, weighted, preferred_element_type=jnp.float32
    ) + jnp.einsum("mkb,mcb->kmc", spectra_sin, swapped, preferred_element_type=jnp.float32)
    numer_all = numer_all.reshape(classes_total, 2 * M * Q)
    class_weight = class_weight.reshape(classes_total, columns)
    cycles_all = jnp.dot(class_weight, power_term.T, precision=lax.Precision.HIGHEST)
    mass_all = jnp.sum(class_weight, axis=1)

    width = numer_all.shape[1]
    packed = jnp.concatenate(
        [numer_all, cycles_all, mass_all[:, None], jnp.zeros((classes_total, 223), jnp.float32)], 1
    )
    core_count = lax.axis_size("core")
    half = packed.shape[1] // core_count
    mine = lax.dynamic_slice_in_dim(packed, core * half, half, 1)
    other = lax.dynamic_slice_in_dim(packed, (1 - core) * half, half, 1)
    packed = mine + lax.ppermute(other, "core", [(0, 1), (1, 0)])
    packed = packed.reshape(lax.axis_size("z"), lax.axis_size("y"), CLS_DEV, half)
    own = jnp.sum(lax.all_to_all(packed, "y", 1, 1, tiled=True), 1)
    own = jnp.sum(lax.all_to_all(own, "z", 0, 0, tiled=True), 0)
    own = lax.all_gather(own, GRP, axis=0, tiled=False)
    own = jnp.sum(own.reshape(lax.axis_size("x"), core_count, CLS_DEV, half), 0)
    own = jnp.concatenate([own[0], own[1]], 1)
    numerator = own[:, :width]
    cycle_sum = own[:, width : width + Q]
    class_mass = own[:, width + Q]
    new_references = (numerator.reshape(CLS_DEV, M, 2, Q) / cycle_sum[:, None, None, :]).reshape(
        CLS_DEV, 2 * M * Q
    )
    particle_total = columns * lax.axis_size(GRP) * lax.axis_size(DEV)
    occupancy = class_mass * (classes_total / particle_total)
    return (new_references, occupancy)


def solution(mesh):
    grp_count, dev_count = mesh.devices.shape
    core_count = 2
    y_count = 4
    split = jax.sharding.Mesh(
        mesh.devices.reshape(
            grp_count // core_count, core_count, dev_count // y_count, y_count
        ),
        GRP + DEV,
    )
    return jax.shard_map(
        local,
        mesh=split,
        in_specs=(P(DEV, None), P(None, GRP + DEV), P(GRP + DEV), P(), P(), P()),
        out_specs=(P(DEV, None), P(DEV)),
        check_vma=False,
    )
```
